128 devices in a mesh: face: 4 (over y), col: 32 (over z, x, core).
Axes of the slice: x: 4, y: 4, z: 4, core: 2. Of those that a mesh axis runs over, the one named last changes fastest.
Arguments:
- dyn_state: float32 [16, 256, 16, 720], P('face', 'col'), may hold values from -6 to 6
- edge_links: int32 [16, 256, 4], P('face', 'col'), may hold values from 0 to 32767, as said below
- phys_slot: int32 [16, 256, 4], P('face', 'col'), may hold values from 0 to 16383, as said below
- crm_active: int32 [16384], P(('face', 'col')), may hold values 0 or 1
- crm_state: bfloat16 [10, 32, 64, 16384], P(None, None, None, ('face', 'col')), may hold values from -4 to 4
Outputs:
- dyn_new: float32 [16, 256, 16, 720], P('face', 'col')
- column_tend: float32 [16, 256, 4, 320], P('face', 'col')
- crm_new: bfloat16 [10, 32, 64, 16384], P(None, None, None, ('face', 'col'))
The draws below stay inside these ranges and needn't reach their ends.
Inputs may be any that keep to these rules, and one draw needn't show every extreme that they name: `edge_links`: each entry is 8 n + 2 k' + r: element n (id row * 256 + column in a grid of 16 x 256 elements), its edge k' (0 to 3) and a reversal bit r. For edge 0 of element (row, column) n lies in row - 1, for edge 2 in row + 1, for edge 1 in column + 1, for edge 3 in column - 1, rows modulo 16 and columns modulo 256; the other coordinate differs by at most one. `phys_slot`: A permutation of the physics columns. The physics column p lives on device p // 128 of face+col; of the quadrants on one device of the element layout exactly 1 go to each device.
All inputs are finite; a program needn't handle non-finite values. No bound on the sum of `crm_active` on one device may be relied on, other than what follows from the above.
Results may differ from the reference program's by a relative error of at most 0.001.
Values sent between devices are 32-bit elements; how exact they have to be, the bound alone decides.
No kernel may reach another device: no remote copies, remote signals or barrier semaphores. Data moves between devices by JAX's collectives and lax.ppermute only.
A program may use at most 192 MiB of HBM per device.

```python
import jax
import jax.numpy as jnp
import numpy as np
from jax import lax

NP = 4
NFLD = 10
LEV = 72
CLEV = 32
CX = 64
DSTEPS = 2
CSTEPS = 2
ER = 4
EC = 8
NR = 16
NC = 256
COLS_DEV = 128
COLS = 16384


def draw_edge_links(key, part):
    keys = jax.random.split(jax.random.fold_in(key, 11), 3)
    shape = (NR, NC, 4)
    offset = jax.random.randint(keys[0], shape, -1, 2)
    other = jax.random.randint(keys[1], shape, 0, 4)
    reversal = jax.random.randint(keys[2], shape, 0, 2)
    rows = lax.broadcasted_iota(jnp.int32, shape, 0)
    cols = lax.broadcasted_iota(jnp.int32, shape, 1)
    edge = lax.broadcasted_iota(jnp.int32, shape, 2)
    top_end = (rows == 0) & (cols == NC - 1) & (edge == 0)
    low_end = (rows == 1) & (cols == 0) & (edge == 0)
    offset = jnp.where(top_end | low_end, 0, offset)
    other = jnp.where(top_end, 3, jnp.where(low_end, 0, other))
    reversal = jnp.where(top_end, 1, jnp.where(low_end, 0, reversal))
    drow = jnp.where(edge == 0, -1, jnp.where(edge == 2, 1, offset))
    dcol = jnp.where(edge == 1, 1, jnp.where(edge == 3, -1, offset))
    near_row = (rows + drow) % NR
    near_col = (cols + dcol) % NC
    return ((near_row * NC + near_col) * 8 + other * 2 + reversal).astype(jnp.int32)


def draw_phys_slot(key, part):
    nface = NR // ER
    ncol = NC // EC
    ndev = nface * ncol
    per_dev = 4 * ER * EC
    count = per_dev // ndev
    first, second = jax.random.split(jax.random.fold_in(key, 23))
    ranks = jax.vmap(lambda sub: jax.random.permutation(sub, per_dev))(jax.random.split(first, ndev))
    places = jax.vmap(lambda sub: jax.random.permutation(sub, per_dev))(jax.random.split(second, ndev))
    target = ranks // count
    within = ranks % count
    source = jnp.arange(ndev, dtype=jnp.int32)[:, None]
    slot = places[target, source * count + within]
    global_slot = (target * per_dev + slot).astype(jnp.int32)
    laid = global_slot.reshape(nface, ncol, ER, EC, 4).transpose(0, 2, 1, 3, 4)
    return laid.reshape(NR, NC, 4)


def plant(values, own_key, least, top_value):
    longest = values.shape.index(max(values.shape))
    spots = []
    for shift in (0, 1):
        where = [jax.random.randint(jax.random.fold_in(own_key, axis), (), 0, length) for axis, length in enumerate(values.shape)]
        where[longest] = (where[longest] + shift) % values.shape[longest]
        spots.append(tuple(where))
    return values.at[spots[0]].set(least).at[spots[1]].set(top_value)


def levels(own_key, dims, shards, low, high):
    def one(axis_at, shards_of):
        heights = jax.random.uniform(jax.random.fold_in(jax.random.fold_in(own_key, 6), axis_at), (shards_of,), jnp.float32, low / len(shards), high / len(shards))
        return jnp.repeat(jnp.exp(heights), dims[axis_at] // shards_of).reshape((-1,) + (1,) * (len(dims) - axis_at - 1))

    level = one(*shards[0])
    for cut in shards[1:]:
        level = level * one(*cut)
    return level


def scatter_about(rng, dims, scale, bound, cuts=(), held_as=jnp.bfloat16):
    drawn = jax.random.normal(rng, dims, jnp.float32) * scale
    if len(cuts) > 0:
        drawn = levels(rng, dims, cuts, -0.22, 0.18) * drawn
    return jnp.clip(drawn, min=-bound, max=bound).astype(held_as)


def setup_inputs(seed: int = 0) -> dict:
    seeds = jax.random.split(jax.random.key(seed), 6)
    return {
        "dyn_state": scatter_about(seeds[0], (NR, NC, NP * NP, NFLD * LEV), 1.0, 6.0, ((0, 4), (1, 32)), jnp.float32),
        "edge_links": draw_edge_links(jax.random.fold_in(seeds[5], 71), 0),
        "phys_slot": draw_phys_slot(jax.random.fold_in(seeds[5], 71), 0),
        "crm_active": plant((jax.random.randint(seeds[3], (COLS,), 0, 4) < 3).astype(jnp.int32), jax.random.fold_in(seeds[3], 1), 0, 1),
        "crm_state": scatter_about(seeds[4], (NFLD, CLEV, CX, COLS), 1.0, 4.0, ((3, 128),)),
    }


KAPPA = 0.1
ADVECT = 0.1
DIFF_X = 0.2
DIFF_Z = 0.1
RELAX = 0.2
CONVERT = 0.5


def node_tables():
    laplace = np.zeros((16, 16), np.float32)
    for row_a in range(4):
        for row_b in range(4):
            here = row_a * 4 + row_b
            for step_a, step_b in ((1, 0), (-1, 0), (0, 1), (0, -1)):
                near_a, near_b = row_a + step_a, row_b + step_b
                if 0 <= near_a < 4 and 0 <= near_b < 4:
                    laplace[here, near_a * 4 + near_b] += 1.0
                    laplace[here, here] -= 1.0
    edge_nodes = np.array([[0, 1, 2, 3], [3, 7, 11, 15], [12, 13, 14, 15], [0, 4, 8, 12]])
    spread = np.zeros((16, 16), np.float32)
    for edge in range(4):
        for point in range(4):
            spread[edge_nodes[edge, point], edge * 4 + point] = 1.0
    denom = 1.0 + spread.sum(axis=1)
    quarter = np.zeros((4, 16), np.float32)
    for row_a in range(4):
        for row_b in range(4):
            quarter[(row_a // 2) * 2 + row_b // 2, row_a * 4 + row_b] = 0.25
    return laplace, spread, denom, quarter


def matched_points(links):
    other_edge = (links // 2) % 4
    reversal = links % 2
    points = jnp.arange(4, dtype=jnp.int32)
    along = jnp.where(reversal[..., None] == 1, 3 - points, points)
    base = jnp.where(other_edge == 1, 3, jnp.where(other_edge == 2, 12, 0))
    stride = jnp.where((other_edge == 1) | (other_edge == 3), 4, 1)
    return (base[..., None] + stride[..., None] * along).astype(jnp.int32)


def crm_run(state, forcing, active):
    start_mean = jnp.mean(state, axis=2)
    live = (active == 1)[None, None, None, :]
    for step in range(CSTEPS):
        east = jnp.roll(state, -1, axis=2)
        west = jnp.roll(state, 1, axis=2)
        upper = jnp.concatenate([state[:, 1:], state[:, -1:]], axis=1)
        lower = jnp.concatenate([state[:, :1], state[:, :-1]], axis=1)
        mean_x = jnp.mean(state, axis=2, keepdims=True)
        fresh = (state - ADVECT * state[0:1] * (east - west) + DIFF_X * (east + west - 2.0 * state)
                 + DIFF_Z * (upper + lower - 2.0 * state) + RELAX * (forcing[:, :, None, :] - mean_x))
        cond = CONVERT * jnp.maximum(fresh[3:4] - fresh[2:3], 0.0)
        fresh = jnp.concatenate([fresh[:3], fresh[3:4] - cond, fresh[4:5] + cond, fresh[5:]], axis=0)
        state = jnp.where(live, fresh, state)
    tend = (jnp.mean(state, axis=2) - start_mean) / CSTEPS
    return state, tend


def reference(dyn_state, edge_links, phys_slot, crm_active, crm_state):
    laplace, spread, denom, quarter = [jnp.asarray(table) for table in node_tables()]
    width = NFLD * LEV
    elems = NR * NC
    state = dyn_state.reshape(elems, 16, width)
    links = edge_links.reshape(elems, 4)
    neighbour = links // 8
    pick = matched_points(links)
    index_flat = (neighbour[..., None] * 16 + pick).reshape(-1)
    for step in range(DSTEPS):
        state = state + KAPPA * jnp.einsum("nm,emw->enw", laplace, state, precision=lax.Precision.HIGHEST)
        matched = state.reshape(elems * 16, width)[index_flat].reshape(elems, 16, width)
        summed = jnp.einsum("nm,emw->enw", spread, matched, precision=lax.Precision.HIGHEST)
        state = (state + summed) / denom[None, :, None]
    dyn_new = state.reshape(NR, NC, 16, width)
    columns = jnp.einsum("qn,enw->eqw", quarter, state, precision=lax.Precision.HIGHEST).reshape(COLS, width)
    slots = phys_slot.reshape(-1)
    physics = jnp.zeros((COLS, width), jnp.float32).at[slots].set(columns)
    forcing = physics.reshape(COLS, NFLD, LEV)[:, :, :CLEV].transpose(1, 2, 0)
    blocks = COLS // COLS_DEV
    blocked_state = crm_state.astype(jnp.float32).reshape(NFLD, CLEV, CX, blocks, COLS_DEV).transpose(3, 0, 1, 2, 4)
    blocked_force = forcing.reshape(NFLD, CLEV, blocks, COLS_DEV).transpose(2, 0, 1, 3)
    blocked_live = crm_active.reshape(blocks, COLS_DEV)

    def one_block(items):
        final, tend = crm_run(items[0], items[1], items[2])
        return final.astype(jnp.bfloat16), tend

    finals, tends = lax.map(one_block, (blocked_state, blocked_force, blocked_live))
    crm_new = finals.transpose(1, 2, 3, 0, 4).reshape(NFLD, CLEV, CX, COLS)
    tend_all = tends.transpose(1, 2, 0, 3).reshape(NFLD * CLEV, COLS)
    column_tend = tend_all.T[slots].reshape(NR, NC, 4, NFLD * CLEV)
    return dyn_new, column_tend, crm_new
```

```python
import jax
import jax.numpy as jnp
import numpy as np
from jax import lax
from jax.experimental import pallas as pl
from jax.experimental.pallas import tpu as pltpu
from jax.sharding import PartitionSpec as P

NFLD = 10
LEV = 72
CLEV = 32
DSTEPS = 2
CSTEPS = 2


KAPPA = 0.1
ADVECT = 0.1
DIFF_X = 0.2
DIFF_Z = 0.1
RELAX = 0.2
CONVERT = 0.5


def extended_2(cells, sides, width):
    for axis, dim in sides:
        count = lax.axis_size(axis)
        head = lax.slice_in_dim(cells, 0, width, axis=dim)
        tail = lax.slice_in_dim(cells, cells.shape[dim] - width, cells.shape[dim], axis=dim)
        cells = jnp.concatenate(
            [
                lax.ppermute(tail, axis, [(i, (i + 1) % count) for i in range(count)]),
                cells,
                lax.ppermute(head, axis, [((i + 1) % count, i) for i in range(count)]),
            ],
            axis=dim,
        )
    return cells


def node_tables():
    laplace = np.zeros((16, 16), np.float32)
    for row_a in range(4):
        for row_b in range(4):
            here = row_a * 4 + row_b
            for step_a, step_b in ((1, 0), (-1, 0), (0, 1), (0, -1)):
                near_a, near_b = (row_a + step_a, row_b + step_b)
                if 0 <= near_a < 4 and 0 <= near_b < 4:
                    laplace[here, near_a * 4 + near_b] += 1.0
                    laplace[here, here] -= 1.0
    edge_nodes = np.array([[0, 1, 2, 3], [3, 7, 11, 15], [12, 13, 14, 15], [0, 4, 8, 12]])
    spread = np.zeros((16, 16), np.float32)
    for edge in range(4):
        for point in range(4):
            spread[edge_nodes[edge, point], edge * 4 + point] = 1.0
    denom = 1.0 + spread.sum(axis=1)
    quarter = np.zeros((4, 16), np.float32)
    for row_a in range(4):
        for row_b in range(4):
            quarter[row_a // 2 * 2 + row_b // 2, row_a * 4 + row_b] = 0.25
    return (laplace, spread, denom, quarter)


def matched_points(links):
    other_edge = links // 2 % 4
    reversal = links % 2
    points = jnp.arange(4, dtype=jnp.int32)
    along = jnp.where(reversal[..., None] == 1, 3 - points, points)
    base = jnp.where(other_edge == 1, 3, jnp.where(other_edge == 2, 12, 0))
    stride = jnp.where((other_edge == 1) | (other_edge == 3), 4, 1)
    return base[..., None] + stride[..., None] * along


ZCHUNK = 4


def crm_kernel(force_ref, live_ref, state_hbm, new_hbm, tend_ref, held, mid, out, in_sem, out_sem):
    nfld, nlev, nx, _ = held.shape
    chunks = nlev // ZCHUNK

    def in_copy(c):
        part = pl.ds(c * ZCHUNK, ZCHUNK)
        return pltpu.make_async_copy(state_hbm.at[:, part], held.at[:, part], in_sem.at[c])

    def out_copy(c):
        part = pl.ds(c * ZCHUNK, ZCHUNK)
        return pltpu.make_async_copy(out.at[:, part], new_hbm.at[:, part], out_sem.at[c])

    for c in range(chunks):
        in_copy(c).start()
    live = live_ref[...] == 1

    def sweep(src, z, last):
        upper_z = jnp.minimum(z + 1, nlev - 1)
        lower_z = jnp.maximum(z - 1, 0)
        lead = src[0, z].astype(jnp.float32)
        kept = {}

        def finish(f, fresh, state):
            new = jnp.where(live, fresh, state)
            if last:
                out[f, z] = new.astype(out.dtype)
                tend_ref[f, pl.ds(z, 1)] = (jnp.mean(new, axis=0, keepdims=True) - tend_ref[f, pl.ds(z, 1)]) / CSTEPS
            else:
                mid[f, z] = new

        for f in range(nfld):
            state = src[f, z].astype(jnp.float32)
            upper = src[f, upper_z].astype(jnp.float32)
            lower = src[f, lower_z].astype(jnp.float32)
            east = pltpu.roll(state, nx - 1, 0)
            west = pltpu.roll(state, 1, 0)
            mean_x = jnp.mean(state, axis=0, keepdims=True)
            if not last:
                tend_ref[f, pl.ds(z, 1)] = mean_x
            fresh = (
                state
                - ADVECT * lead * (east - west)
                + DIFF_X * (east + west - 2.0 * state)
                + DIFF_Z * (upper + lower - 2.0 * state)
                + RELAX * (force_ref[f, pl.ds(z, 1)] - mean_x)
            )
            if f in (2, 3):
                kept[f] = (fresh, state)
                if f == 3:
                    cond = CONVERT * jnp.maximum(kept[3][0] - kept[2][0], 0.0)
                    finish(2, *kept[2])
                    finish(3, kept[3][0] - cond, kept[3][1])
                continue
            if f == 4:
                fresh = fresh + cond
            finish(f, fresh, state)

    for c in range(chunks):
        if c == 0:
            in_copy(0).wait()
        if c + 1 < chunks:
            in_copy(c + 1).wait()

        def first(z, carry):
            sweep(held, z, False)
            return carry

        lax.fori_loop(c * ZCHUNK, (c + 1) * ZCHUNK, first, 0)
    for c in range(chunks):

        def second(z, carry):
            sweep(mid, z, True)
            return carry

        lax.fori_loop(c * ZCHUNK, (c + 1) * ZCHUNK, second, 0)
        out_copy(c).start()
    for c in range(chunks):
        out_copy(c).wait()


def crm_run(state, forcing, active):
    nfld, nlev, nx, ncol = state.shape
    return pl.pallas_call(
        crm_kernel,
        out_shape=(
            jax.ShapeDtypeStruct(state.shape, jnp.bfloat16),
            jax.ShapeDtypeStruct((nfld, nlev, ncol), jnp.float32),
        ),
        in_specs=[
            pl.BlockSpec(memory_space=pltpu.VMEM),
            pl.BlockSpec(memory_space=pltpu.VMEM),
            pl.BlockSpec(memory_space=pl.ANY),
        ],
        out_specs=(
            pl.BlockSpec(memory_space=pl.ANY),
            pl.BlockSpec(memory_space=pltpu.VMEM),
        ),
        scratch_shapes=[
            pltpu.VMEM(state.shape, jnp.bfloat16),
            pltpu.VMEM(state.shape, jnp.float32),
            pltpu.VMEM(state.shape, jnp.bfloat16),
            pltpu.SemaphoreType.DMA((nlev // ZCHUNK,)),
            pltpu.SemaphoreType.DMA((nlev // ZCHUNK,)),
        ],
        compiler_params=pltpu.CompilerParams(vmem_limit_bytes=48 * 1024 * 1024),
    )(forcing, active.reshape(1, ncol), state)


def per_device(dyn_state, edge_links, phys_slot, crm_active, crm_state):
    laplace, spread, denom, quarter = [jnp.asarray(table) for table in node_tables()]
    rows_dev, cols_dev, nodes, width = dyn_state.shape
    nface = lax.axis_size("face")
    ncol = lax.axis_size("col")
    ndev = nface * ncol
    total_rows = rows_dev * nface
    total_cols = cols_dev * ncol
    neighbour = edge_links // 8
    pick = matched_points(edge_links)
    near_row = neighbour // total_cols
    near_col = neighbour % total_cols
    local_row = lax.broadcasted_iota(jnp.int32, (rows_dev, cols_dev, 4), 0)
    local_col = lax.broadcasted_iota(jnp.int32, (rows_dev, cols_dev, 4), 1)
    drow = (near_row - (lax.axis_index("face") * rows_dev + local_row) + 1) % total_rows - 1
    dcol = (near_col - (lax.axis_index("col") * cols_dev + local_col) + 1) % total_cols - 1
    place = (local_row + drow + 1) * (cols_dev + 2) + (local_col + dcol + 1)
    index_flat = place[..., None] * 16 + pick
    index_flat = index_flat.reshape(-1)
    state = dyn_state
    for step in range(DSTEPS):
        state = state + KAPPA * jnp.einsum(
            "nm,rcmw->rcnw", laplace, state, precision=lax.Precision.HIGHEST
        )
        extended = extended_2(state, (("face", 0), ("col", 1)), 1)
        matched = jnp.take(extended.reshape(-1, width), index_flat, axis=0).reshape(
            rows_dev, cols_dev, 16, width
        )
        summed = jnp.einsum("nm,rcmw->rcnw", spread, matched, precision=lax.Precision.HIGHEST)
        state = (state + summed) / denom[None, None, :, None]
    columns = jnp.einsum("qn,rcnw->rcqw", quarter, state, precision=lax.Precision.HIGHEST).reshape(
        -1, width
    )
    per_dev = columns.shape[0]
    count = per_dev // ndev
    keys_local = phys_slot.reshape(-1)
    order = jnp.argsort(keys_local, stable=True)
    outgoing = columns[order]
    out_keys = keys_local[order]
    arrived, arrived_keys = (
        lax.all_to_all(
            outgoing.reshape(ndev, count, width),
            ("face", "col"),
            split_axis=0,
            concat_axis=0,
            tiled=True,
        ),
        lax.all_to_all(
            out_keys.reshape(ndev, count), ("face", "col"), split_axis=0, concat_axis=0, tiled=True
        ),
    )
    slots = arrived_keys.reshape(-1) % per_dev
    physics = jnp.zeros((per_dev, width), jnp.float32).at[slots].set(arrived.reshape(-1, width))
    forcing = physics.reshape(per_dev, NFLD, LEV)[:, :, :CLEV].transpose(1, 2, 0)
    crm_new, tend = crm_run(crm_state, forcing, crm_active)
    tend_rows = tend.reshape(NFLD * CLEV, per_dev).T[slots]
    returned = lax.all_to_all(
        tend_rows.reshape(ndev, count, NFLD * CLEV),
        ("face", "col"),
        split_axis=0,
        concat_axis=0,
        tiled=True,
    )
    placed = (
        jnp.zeros((per_dev, NFLD * CLEV), jnp.float32)
        .at[order]
        .set(returned.reshape(per_dev, NFLD * CLEV))
    )
    column_tend = placed.reshape(rows_dev, cols_dev, 4, NFLD * CLEV)
    return (state, column_tend, crm_new)


def solution(mesh):
    return jax.shard_map(
        per_device,
        mesh=mesh,
        in_specs=(
            P("face", "col", None, None),
            P("face", "col", None),
            P("face", "col", None),
            P(("face", "col")),
            P(None, None, None, ("face", "col")),
        ),
        out_specs=(
            P("face", "col", None, None),
            P("face", "col", None, None),
            P(None, None, None, ("face", "col")),
        ),
        check_vma=False,
    )
```

```python
import jax
import jax.numpy as jnp
import numpy as np
from jax import lax
from jax.experimental import pallas as pl
from jax.experimental.pallas import tpu as pltpu
from jax.sharding import PartitionSpec as P

NFLD = 10
LEV = 72
CLEV = 32
DSTEPS = 2
CSTEPS = 2


KAPPA = 0.1
ADVECT = 0.1
DIFF_X = 0.2
DIFF_Z = 0.1
RELAX = 0.2
CONVERT = 0.5


def extended_2(cells, sides, width):
    for axis, dim in sides:
        count = lax.axis_size(axis)
        head = lax.slice_in_dim(cells, 0, width, axis=dim)
        tail = lax.slice_in_dim(cells, cells.shape[dim] - width, cells.shape[dim], axis=dim)
        cells = jnp.concatenate(
            [
                lax.ppermute(tail, axis, [(i, (i + 1) % count) for i in range(count)]),
                cells,
                lax.ppermute(head, axis, [((i + 1) % count, i) for i in range(count)]),
            ],
            axis=dim,
        )
    return cells


def node_tables():
    laplace = np.zeros((16, 16), np.float32)
    for row_a in range(4):
        for row_b in range(4):
            here = row_a * 4 + row_b
            for step_a, step_b in ((1, 0), (-1, 0), (0, 1), (0, -1)):
                near_a, near_b = (row_a + step_a, row_b + step_b)
                if 0 <= near_a < 4 and 0 <= near_b < 4:
                    laplace[here, near_a * 4 + near_b] += 1.0
                    laplace[here, here] -= 1.0
    edge_nodes = np.array([[0, 1, 2, 3], [3, 7, 11, 15], [12, 13, 14, 15], [0, 4, 8, 12]])
    spread = np.zeros((16, 16), np.float32)
    for edge in range(4):
        for point in range(4):
            spread[edge_nodes[edge, point], edge * 4 + point] = 1.0
    denom = 1.0 + spread.sum(axis=1)
    quarter = np.zeros((4, 16), np.float32)
    for row_a in range(4):
        for row_b in range(4):
            quarter[row_a // 2 * 2 + row_b // 2, row_a * 4 + row_b] = 0.25
    return (laplace, spread, denom, quarter)


def matched_points(links):
    other_edge = links // 2 % 4
    reversal = links % 2
    points = jnp.arange(4, dtype=jnp.int32)
    along = jnp.where(reversal[..., None] == 1, 3 - points, points)
    base = jnp.where(other_edge == 1, 3, jnp.where(other_edge == 2, 12, 0))
    stride = jnp.where((other_edge == 1) | (other_edge == 3), 4, 1)
    return base[..., None] + stride[..., None] * along


ZCHUNK = 4


def crm_kernel(force_ref, live_ref, state_hbm, new_hbm, tend_ref, held, mid, out, in_sem, out_sem):
    nfld, nlev, nx, _ = held.shape
    chunks = nlev // ZCHUNK

    def in_copy(c):
        part = pl.ds(c * ZCHUNK, ZCHUNK)
        return pltpu.make_async_copy(state_hbm.at[:, part], held.at[:, part], in_sem.at[c])

    def out_copy(c):
        part = pl.ds(c * ZCHUNK, ZCHUNK)
        return pltpu.make_async_copy(out.at[:, part], new_hbm.at[:, part], out_sem.at[c])

    for c in range(chunks):
        in_copy(c).start()
    live = live_ref[...] == 1

    def sweep(src, z, last):
        upper_z = jnp.minimum(z + 1, nlev - 1)
        lower_z = jnp.maximum(z - 1, 0)
        lead = src[0, z].astype(jnp.float32)
        kept = {}

        def finish(f, fresh, state):
            new = jnp.where(live, fresh, state)
            if last:
                out[f, z] = new.astype(out.dtype)
                tend_ref[f, pl.ds(z, 1)] = (jnp.mean(new, axis=0, keepdims=True) - tend_ref[f, pl.ds(z, 1)]) / CSTEPS
            else:
                mid[f, z] = new

        for f in range(nfld):
            state = src[f, z].astype(jnp.float32)
            upper = src[f, upper_z].astype(jnp.float32)
            lower = src[f, lower_z].astype(jnp.float32)
            east = pltpu.roll(state, nx - 1, 0)
            west = pltpu.roll(state, 1, 0)
            mean_x = jnp.mean(state, axis=0, keepdims=True)
            if not last:
                tend_ref[f, pl.ds(z, 1)] = mean_x
            fresh = (
                state
                - ADVECT * lead * (east - west)
                + DIFF_X * (east + west - 2.0 * state)
                + DIFF_Z * (upper + lower - 2.0 * state)
                + RELAX * (force_ref[f, pl.ds(z, 1)] - mean_x)
            )
            if f in (2, 3):
                kept[f] = (fresh, state)
                if f == 3:
                    cond = CONVERT * jnp.maximum(kept[3][0] - kept[2][0], 0.0)
                    finish(2, *kept[2])
                    finish(3, kept[3][0] - cond, kept[3][1])
                continue
            if f == 4:
                fresh = fresh + cond
            finish(f, fresh, state)

    for c in range(chunks):
        if c == 0:
            in_copy(0).wait()
        if c + 1 < chunks:
            in_copy(c + 1).wait()

        def first(z, carry):
            sweep(held, z, False)
            return carry

        lax.fori_loop(c * ZCHUNK, (c + 1) * ZCHUNK, first, 0)
    for c in range(chunks):

        def second(z, carry):
            sweep(mid, z, True)
            return carry

        lax.fori_loop(c * ZCHUNK, (c + 1) * ZCHUNK, second, 0)
        out_copy(c).start()
    for c in range(chunks):
        out_copy(c).wait()


def crm_run(state, forcing, active):
    nfld, nlev, nx, ncol = state.shape
    return pl.pallas_call(
        crm_kernel,
        out_shape=(
            jax.ShapeDtypeStruct(state.shape, jnp.bfloat16),
            jax.ShapeDtypeStruct((nfld, nlev, ncol), jnp.float32),
        ),
        in_specs=[
            pl.BlockSpec(memory_space=pltpu.VMEM),
            pl.BlockSpec(memory_space=pltpu.VMEM),
            pl.BlockSpec(memory_space=pl.ANY),
        ],
        out_specs=(
            pl.BlockSpec(memory_space=pl.ANY),
            pl.BlockSpec(memory_space=pltpu.VMEM),
        ),
        scratch_shapes=[
            pltpu.VMEM(state.shape, jnp.bfloat16),
            pltpu.VMEM(state.shape, jnp.float32),
            pltpu.VMEM(state.shape, jnp.bfloat16),
            pltpu.SemaphoreType.DMA((nlev // ZCHUNK,)),
            pltpu.SemaphoreType.DMA((nlev // ZCHUNK,)),
        ],
        compiler_params=pltpu.CompilerParams(vmem_limit_bytes=48 * 1024 * 1024),
    )(forcing, active.reshape(1, ncol), state)


TWO_STAGE = False


def exchange(chunks):
    if not TWO_STAGE:
        return lax.all_to_all(chunks, ("face", "col"), split_axis=0, concat_axis=0, tiled=True)
    nface = lax.axis_size("face")
    ncol = lax.axis_size("col")
    grid = chunks.reshape((nface, ncol) + chunks.shape[1:])
    grid = lax.all_to_all(grid, "col", split_axis=1, concat_axis=1, tiled=True)
    grid = lax.all_to_all(grid, "face", split_axis=0, concat_axis=0, tiled=True)
    return grid.reshape(chunks.shape)


def per_device(dyn_state, edge_links, phys_slot, crm_active, crm_state):
    laplace, spread, denom, quarter = [jnp.asarray(table) for table in node_tables()]
    rows_dev, cols_dev, nodes, width = dyn_state.shape
    nface = lax.axis_size("face")
    ncol = lax.axis_size("col")
    ndev = nface * ncol
    total_rows = rows_dev * nface
    total_cols = cols_dev * ncol
    neighbour = edge_links // 8
    pick = matched_points(edge_links)
    near_row = neighbour // total_cols
    near_col = neighbour % total_cols
    local_row = lax.broadcasted_iota(jnp.int32, (rows_dev, cols_dev, 4), 0)
    local_col = lax.broadcasted_iota(jnp.int32, (rows_dev, cols_dev, 4), 1)
    drow = (near_row - (lax.axis_index("face") * rows_dev + local_row) + 1) % total_rows - 1
    dcol = (near_col - (lax.axis_index("col") * cols_dev + local_col) + 1) % total_cols - 1
    place = (local_row + drow + 1) * (cols_dev + 2) + (local_col + dcol + 1)
    index_flat = place[..., None] * 16 + pick
    index_flat = index_flat.reshape(-1)
    state = dyn_state
    for step in range(DSTEPS):
        state = state + KAPPA * jnp.einsum(
            "nm,rcmw->rcnw", laplace, state, precision=lax.Precision.HIGHEST
        )
        extended = extended_2(state, (("face", 0), ("col", 1)), 1)
        matched = jnp.take(extended.reshape(-1, width), index_flat, axis=0).reshape(
            rows_dev, cols_dev, 16, width
        )
        summed = jnp.einsum("nm,rcmw->rcnw", spread, matched, precision=lax.Precision.HIGHEST)
        state = (state + summed) / denom[None, None, :, None]
    cut = state.reshape(rows_dev, cols_dev, nodes, NFLD, LEV)[..., :CLEV].reshape(
        rows_dev, cols_dev, nodes, NFLD * CLEV
    )
    columns = jnp.einsum("qn,rcnw->rcqw", quarter, cut, precision=lax.Precision.HIGHEST).reshape(
        -1, NFLD * CLEV
    )
    per_dev = columns.shape[0]
    count = per_dev // ndev
    keys_local = phys_slot.reshape(-1)
    order = jnp.argsort(keys_local, stable=True)
    out_keys = keys_local[order]
    outgoing = jnp.concatenate(
        [columns[order], out_keys.astype(jnp.float32)[:, None]], axis=1
    )
    arrived = exchange(outgoing.reshape(ndev, count, NFLD * CLEV + 1)).reshape(per_dev, -1)
    slots = arrived[:, NFLD * CLEV].astype(jnp.int32) % per_dev
    physics = jnp.zeros((per_dev, NFLD * CLEV), jnp.float32).at[slots].set(arrived[:, : NFLD * CLEV])
    forcing = physics.reshape(per_dev, NFLD, CLEV).transpose(1, 2, 0)
    crm_new, tend = crm_run(crm_state, forcing, crm_active)
    tend_rows = tend.reshape(NFLD * CLEV, per_dev).T[slots]
    returned = exchange(tend_rows.reshape(ndev, count, NFLD * CLEV))
    placed = (
        jnp.zeros((per_dev, NFLD * CLEV), jnp.float32)
        .at[order]
        .set(returned.reshape(per_dev, NFLD * CLEV))
    )
    column_tend = placed.reshape(rows_dev, cols_dev, 4, NFLD * CLEV)
    return (state, column_tend, crm_new)


def solution(mesh):
    return jax.shard_map(
        per_device,
        mesh=mesh,
        in_specs=(
            P("face", "col", None, None),
            P("face", "col", None),
            P("face", "col", None),
            P(("face", "col")),
            P(None, None, None, ("face", "col")),
        ),
        out_specs=(
            P("face", "col", None, None),
            P("face", "col", None, None),
            P(None, None, None, ("face", "col")),
        ),
        check_vma=False,
    )
```

```python
import jax
import jax.numpy as jnp
import numpy as np
from jax import lax
from jax.experimental import pallas as pl
from jax.experimental.pallas import tpu as pltpu
from jax.sharding import PartitionSpec as P

NFLD = 10
LEV = 72
CLEV = 32
DSTEPS = 2
CSTEPS = 2


KAPPA = 0.1
ADVECT = 0.1
DIFF_X = 0.2
DIFF_Z = 0.1
RELAX = 0.2
CONVERT = 0.5


def extended_2(cells, sides, width):
    for axis, dim in sides:
        count = lax.axis_size(axis)
        head = lax.slice_in_dim(cells, 0, width, axis=dim)
        tail = lax.slice_in_dim(cells, cells.shape[dim] - width, cells.shape[dim], axis=dim)
        cells = jnp.concatenate(
            [
                lax.ppermute(tail, axis, [(i, (i + 1) % count) for i in range(count)]),
                cells,
                lax.ppermute(head, axis, [((i + 1) % count, i) for i in range(count)]),
            ],
            axis=dim,
        )
    return cells


def node_tables():
    laplace = np.zeros((16, 16), np.float32)
    for row_a in range(4):
        for row_b in range(4):
            here = row_a * 4 + row_b
            for step_a, step_b in ((1, 0), (-1, 0), (0, 1), (0, -1)):
                near_a, near_b = (row_a + step_a, row_b + step_b)
                if 0 <= near_a < 4 and 0 <= near_b < 4:
                    laplace[here, near_a * 4 + near_b] += 1.0
                    laplace[here, here] -= 1.0
    edge_nodes = np.array([[0, 1, 2, 3], [3, 7, 11, 15], [12, 13, 14, 15], [0, 4, 8, 12]])
    spread = np.zeros((16, 16), np.float32)
    for edge in range(4):
        for point in range(4):
            spread[edge_nodes[edge, point], edge * 4 + point] = 1.0
    denom = 1.0 + spread.sum(axis=1)
    quarter = np.zeros((4, 16), np.float32)
    for row_a in range(4):
        for row_b in range(4):
            quarter[row_a // 2 * 2 + row_b // 2, row_a * 4 + row_b] = 0.25
    return (laplace, spread, denom, quarter)


def matched_points(links):
    other_edge = links // 2 % 4
    reversal = links % 2
    points = jnp.arange(4, dtype=jnp.int32)
    along = jnp.where(reversal[..., None] == 1, 3 - points, points)
    base = jnp.where(other_edge == 1, 3, jnp.where(other_edge == 2, 12, 0))
    stride = jnp.where((other_edge == 1) | (other_edge == 3), 4, 1)
    return base[..., None] + stride[..., None] * along


ZCHUNK = 4


def crm_kernel(force_ref, live_ref, state_hbm, new_hbm, tend_ref, held, mid, out, in_sem, out_sem):
    nfld, nlev, nx, _ = held.shape
    chunks = nlev // ZCHUNK

    def in_copy(c):
        part = pl.ds(c * ZCHUNK, ZCHUNK)
        return pltpu.make_async_copy(state_hbm.at[:, part], held.at[:, part], in_sem.at[c])

    def out_copy(c):
        part = pl.ds(c * ZCHUNK, ZCHUNK)
        return pltpu.make_async_copy(out.at[:, part], new_hbm.at[:, part], out_sem.at[c])

    for c in range(chunks):
        in_copy(c).start()
    live = live_ref[...] == 1

    def sweep(src, z, last):
        upper_z = jnp.minimum(z + 1, nlev - 1)
        lower_z = jnp.maximum(z - 1, 0)
        lead = src[0, z].astype(jnp.float32)
        kept = {}

        def finish(f, fresh, state):
            new = jnp.where(live, fresh, state)
            if last:
                out[f, z] = new.astype(out.dtype)
                tend_ref[f, pl.ds(z, 1)] = (jnp.mean(new, axis=0, keepdims=True) - tend_ref[f, pl.ds(z, 1)]) / CSTEPS
            else:
                mid[f, z] = new

        for f in range(nfld):
            state = src[f, z].astype(jnp.float32)
            upper = src[f, upper_z].astype(jnp.float32)
            lower = src[f, lower_z].astype(jnp.float32)
            east = pltpu.roll(state, nx - 1, 0)
            west = pltpu.roll(state, 1, 0)
            mean_x = jnp.mean(state, axis=0, keepdims=True)
            if not last:
                tend_ref[f, pl.ds(z, 1)] = mean_x
            fresh = (
                state
                - ADVECT * lead * (east - west)
                + DIFF_X * (east + west - 2.0 * state)
                + DIFF_Z * (upper + lower - 2.0 * state)
                + RELAX * (force_ref[f, pl.ds(z, 1)] - mean_x)
            )
            if f in (2, 3):
                kept[f] = (fresh, state)
                if f == 3:
                    cond = CONVERT * jnp.maximum(kept[3][0] - kept[2][0], 0.0)
                    finish(2, *kept[2])
                    finish(3, kept[3][0] - cond, kept[3][1])
                continue
            if f == 4:
                fresh = fresh + cond
            finish(f, fresh, state)

    for c in range(chunks):
        if c == 0:
            in_copy(0).wait()
        if c + 1 < chunks:
            in_copy(c + 1).wait()

        def first(z, carry):
            sweep(held, z, False)
            return carry

        lax.fori_loop(c * ZCHUNK, (c + 1) * ZCHUNK, first, 0)
    for c in range(chunks):

        def second(z, carry):
            sweep(mid, z, True)
            return carry

        lax.fori_loop(c * ZCHUNK, (c + 1) * ZCHUNK, second, 0)
        out_copy(c).start()
    for c in range(chunks):
        out_copy(c).wait()


def crm_run(state, forcing, active):
    nfld, nlev, nx, ncol = state.shape
    return pl.pallas_call(
        crm_kernel,
        out_shape=(
            jax.ShapeDtypeStruct(state.shape, jnp.bfloat16),
            jax.ShapeDtypeStruct((nfld, nlev, ncol), jnp.float32),
        ),
        in_specs=[
            pl.BlockSpec(memory_space=pltpu.VMEM),
            pl.BlockSpec(memory_space=pltpu.VMEM),
            pl.BlockSpec(memory_space=pl.ANY),
        ],
        out_specs=(
            pl.BlockSpec(memory_space=pl.ANY),
            pl.BlockSpec(memory_space=pltpu.VMEM),
        ),
        scratch_shapes=[
            pltpu.VMEM(state.shape, jnp.bfloat16),
            pltpu.VMEM(state.shape, jnp.float32),
            pltpu.VMEM(state.shape, jnp.bfloat16),
            pltpu.SemaphoreType.DMA((nlev // ZCHUNK,)),
            pltpu.SemaphoreType.DMA((nlev // ZCHUNK,)),
        ],
        compiler_params=pltpu.CompilerParams(vmem_limit_bytes=48 * 1024 * 1024),
    )(forcing, active.reshape(1, ncol), state)


TWO_STAGE = True


def exchange(chunks):
    if not TWO_STAGE:
        return lax.all_to_all(chunks, ("face", "col"), split_axis=0, concat_axis=0, tiled=True)
    nface = lax.axis_size("face")
    ncol = lax.axis_size("col")
    grid = chunks.reshape((nface, ncol) + chunks.shape[1:])
    grid = lax.all_to_all(grid, "col", split_axis=1, concat_axis=1, tiled=True)
    grid = lax.all_to_all(grid, "face", split_axis=0, concat_axis=0, tiled=True)
    return grid.reshape(chunks.shape)


def per_device(dyn_state, edge_links, phys_slot, crm_active, crm_state):
    laplace, spread, denom, quarter = [jnp.asarray(table) for table in node_tables()]
    rows_dev, cols_dev, nodes, width = dyn_state.shape
    nface = lax.axis_size("face")
    ncol = lax.axis_size("col")
    ndev = nface * ncol
    total_rows = rows_dev * nface
    total_cols = cols_dev * ncol
    neighbour = edge_links // 8
    pick = matched_points(edge_links)
    near_row = neighbour // total_cols
    near_col = neighbour % total_cols
    local_row = lax.broadcasted_iota(jnp.int32, (rows_dev, cols_dev, 4), 0)
    local_col = lax.broadcasted_iota(jnp.int32, (rows_dev, cols_dev, 4), 1)
    drow = (near_row - (lax.axis_index("face") * rows_dev + local_row) + 1) % total_rows - 1
    dcol = (near_col - (lax.axis_index("col") * cols_dev + local_col) + 1) % total_cols - 1
    place = (local_row + drow + 1) * (cols_dev + 2) + (local_col + dcol + 1)
    index_flat = place[..., None] * 16 + pick
    index_flat = index_flat.reshape(-1)
    state = dyn_state
    for step in range(DSTEPS):
        state = state + KAPPA * jnp.einsum(
            "nm,rcmw->rcnw", laplace, state, precision=lax.Precision.HIGHEST
        )
        extended = extended_2(state, (("face", 0), ("col", 1)), 1)
        matched = jnp.take(extended.reshape(-1, width), index_flat, axis=0).reshape(
            rows_dev, cols_dev, 16, width
        )
        summed = jnp.einsum("nm,rcmw->rcnw", spread, matched, precision=lax.Precision.HIGHEST)
        state = (state + summed) / denom[None, None, :, None]
    columns = jnp.einsum("qn,rcnw->rcqw", quarter, state, precision=lax.Precision.HIGHEST).reshape(
        -1, NFLD, LEV
    )[:, :, :CLEV].reshape(-1, NFLD * CLEV)
    per_dev = columns.shape[0]
    count = per_dev // ndev
    keys_local = phys_slot.reshape(-1)
    order = jnp.argsort(keys_local, stable=True)
    out_keys = keys_local[order]
    outgoing = jnp.concatenate(
        [columns[order], out_keys.astype(jnp.float32)[:, None]], axis=1
    )
    arrived = exchange(outgoing.reshape(ndev, count, NFLD * CLEV + 1)).reshape(per_dev, -1)
    slots = arrived[:, NFLD * CLEV].astype(jnp.int32) % per_dev
    physics = jnp.zeros((per_dev, NFLD * CLEV), jnp.float32).at[slots].set(arrived[:, : NFLD * CLEV])
    forcing = physics.reshape(per_dev, NFLD, CLEV).transpose(1, 2, 0)
    crm_new, tend = crm_run(crm_state, forcing, crm_active)
    tend_rows = tend.reshape(NFLD * CLEV, per_dev).T[slots]
    returned = exchange(tend_rows.reshape(ndev, count, NFLD * CLEV))
    placed = (
        jnp.zeros((per_dev, NFLD * CLEV), jnp.float32)
        .at[order]
        .set(returned.reshape(per_dev, NFLD * CLEV))
    )
    column_tend = placed.reshape(rows_dev, cols_dev, 4, NFLD * CLEV)
    return (state, column_tend, crm_new)


def solution(mesh):
    return jax.shard_map(
        per_device,
        mesh=mesh,
        in_specs=(
            P("face", "col", None, None),
            P("face", "col", None),
            P("face", "col", None),
            P(("face", "col")),
            P(None, None, None, ("face", "col")),
        ),
        out_specs=(
            P("face", "col", None, None),
            P("face", "col", None, None),
            P(None, None, None, ("face", "col")),
        ),
        check_vma=False,
    )
```

```python
import jax
import jax.numpy as jnp
import numpy as np
from jax import lax
from jax.experimental import pallas as pl
from jax.experimental.pallas import tpu as pltpu
from jax.sharding import PartitionSpec as P

NFLD = 10
LEV = 72
CLEV = 32
DSTEPS = 2
CSTEPS = 2


KAPPA = 0.1
ADVECT = 0.1
DIFF_X = 0.2
DIFF_Z = 0.1
RELAX = 0.2
CONVERT = 0.5


def rim_points(cells):
    return jnp.concatenate([cells[:, :, 0:5], cells[:, :, 7:9], cells[:, :, 11:16]], axis=2)


def halo_table(rim):
    nface = lax.axis_size("face")
    ncol = lax.axis_size("col")
    rows, cols = rim.shape[:2]

    def along(piece, axis, count, step):
        return lax.ppermute(piece, axis, [(i, (i + step) % count) for i in range(count)])

    def corner(piece, df, dc):
        pairs = [
            (f * ncol + c, ((f + df) % nface) * ncol + (c + dc) % ncol)
            for f in range(nface)
            for c in range(ncol)
        ]
        return lax.ppermute(piece, ("face", "col"), pairs)

    up = along(rim[rows - 1 : rows], "face", nface, 1)
    down = along(rim[0:1], "face", nface, -1)
    left = along(rim[:, cols - 1 : cols], "col", ncol, 1)
    right = along(rim[:, 0:1], "col", ncol, -1)
    up_left = corner(rim[rows - 1 : rows, cols - 1 : cols], 1, 1)
    up_right = corner(rim[rows - 1 : rows, 0:1], 1, -1)
    down_left = corner(rim[0:1, cols - 1 : cols], -1, 1)
    down_right = corner(rim[0:1, 0:1], -1, -1)
    top = jnp.concatenate([up_left, up, up_right], axis=1)
    middle = jnp.concatenate([left, rim, right], axis=1)
    bottom = jnp.concatenate([down_left, down, down_right], axis=1)
    return jnp.concatenate([top, middle, bottom], axis=0)


def node_tables():
    laplace = np.zeros((16, 16), np.float32)
    for row_a in range(4):
        for row_b in range(4):
            here = row_a * 4 + row_b
            for step_a, step_b in ((1, 0), (-1, 0), (0, 1), (0, -1)):
                near_a, near_b = (row_a + step_a, row_b + step_b)
                if 0 <= near_a < 4 and 0 <= near_b < 4:
                    laplace[here, near_a * 4 + near_b] += 1.0
                    laplace[here, here] -= 1.0
    edge_nodes = np.array([[0, 1, 2, 3], [3, 7, 11, 15], [12, 13, 14, 15], [0, 4, 8, 12]])
    spread = np.zeros((16, 16), np.float32)
    for edge in range(4):
        for point in range(4):
            spread[edge_nodes[edge, point], edge * 4 + point] = 1.0
    denom = 1.0 + spread.sum(axis=1)
    quarter = np.zeros((4, 16), np.float32)
    for row_a in range(4):
        for row_b in range(4):
            quarter[row_a // 2 * 2 + row_b // 2, row_a * 4 + row_b] = 0.25
    return (laplace, spread, denom, quarter)


def matched_points(links):
    other_edge = links // 2 % 4
    reversal = links % 2
    points = jnp.arange(4, dtype=jnp.int32)
    along = jnp.where(reversal[..., None] == 1, 3 - points, points)
    base = jnp.where(other_edge == 1, 3, jnp.where(other_edge == 2, 12, 0))
    stride = jnp.where((other_edge == 1) | (other_edge == 3), 4, 1)
    return base[..., None] + stride[..., None] * along


ZCHUNK = 4


def crm_kernel(force_ref, live_ref, state_hbm, new_hbm, tend_ref, held, mid, out, in_sem, out_sem):
    nfld, nlev, nx, _ = held.shape
    chunks = nlev // ZCHUNK

    def in_copy(c):
        part = pl.ds(c * ZCHUNK, ZCHUNK)
        return pltpu.make_async_copy(state_hbm.at[:, part], held.at[:, part], in_sem.at[c])

    def out_copy(c):
        part = pl.ds(c * ZCHUNK, ZCHUNK)
        return pltpu.make_async_copy(out.at[:, part], new_hbm.at[:, part], out_sem.at[c])

    for c in range(chunks):
        in_copy(c).start()
    live = live_ref[...] == 1

    def sweep(src, z, last):
        upper_z = jnp.minimum(z + 1, nlev - 1)
        lower_z = jnp.maximum(z - 1, 0)
        lead = src[0, z].astype(jnp.float32)
        kept = {}

        def finish(f, fresh, state):
            new = jnp.where(live, fresh, state)
            if last:
                out[f, z] = new.astype(out.dtype)
                tend_ref[f, pl.ds(z, 1)] = (jnp.mean(new, axis=0, keepdims=True) - tend_ref[f, pl.ds(z, 1)]) / CSTEPS
            else:
                mid[f, z] = new

        for f in range(nfld):
            state = src[f, z].astype(jnp.float32)
            upper = src[f, upper_z].astype(jnp.float32)
            lower = src[f, lower_z].astype(jnp.float32)
            east = pltpu.roll(state, nx - 1, 0)
            west = pltpu.roll(state, 1, 0)
            mean_x = jnp.mean(state, axis=0, keepdims=True)
            if not last:
                tend_ref[f, pl.ds(z, 1)] = mean_x
            fresh = (
                state
                - ADVECT * lead * (east - west)
                + DIFF_X * (east + west - 2.0 * state)
                + DIFF_Z * (upper + lower - 2.0 * state)
                + RELAX * (force_ref[f, pl.ds(z, 1)] - mean_x)
            )
            if f in (2, 3):
                kept[f] = (fresh, state)
                if f == 3:
                    cond = CONVERT * jnp.maximum(kept[3][0] - kept[2][0], 0.0)
                    finish(2, *kept[2])
                    finish(3, kept[3][0] - cond, kept[3][1])
                continue
            if f == 4:
                fresh = fresh + cond
            finish(f, fresh, state)

    for c in range(chunks):
        if c == 0:
            in_copy(0).wait()
        if c + 1 < chunks:
            in_copy(c + 1).wait()

        def first(z, carry):
            sweep(held, z, False)
            return carry

        lax.fori_loop(c * ZCHUNK, (c + 1) * ZCHUNK, first, 0)
    for c in range(chunks):

        def second(z, carry):
            sweep(mid, z, True)
            return carry

        lax.fori_loop(c * ZCHUNK, (c + 1) * ZCHUNK, second, 0)
        out_copy(c).start()
    for c in range(chunks):
        out_copy(c).wait()


def crm_run(state, forcing, active):
    nfld, nlev, nx, ncol = state.shape
    return pl.pallas_call(
        crm_kernel,
        out_shape=(
            jax.ShapeDtypeStruct(state.shape, jnp.bfloat16),
            jax.ShapeDtypeStruct((nfld, nlev, ncol), jnp.float32),
        ),
        in_specs=[
            pl.BlockSpec(memory_space=pltpu.VMEM),
            pl.BlockSpec(memory_space=pltpu.VMEM),
            pl.BlockSpec(memory_space=pltpu.HBM),
        ],
        out_specs=(
            pl.BlockSpec(memory_space=pltpu.HBM),
            pl.BlockSpec(memory_space=pltpu.VMEM),
        ),
        scratch_shapes=[
            pltpu.VMEM(state.shape, jnp.bfloat16),
            pltpu.VMEM(state.shape, jnp.float32),
            pltpu.VMEM(state.shape, jnp.bfloat16),
            pltpu.SemaphoreType.DMA((nlev // ZCHUNK,)),
            pltpu.SemaphoreType.DMA((nlev // ZCHUNK,)),
        ],
        compiler_params=pltpu.CompilerParams(vmem_limit_bytes=48 * 1024 * 1024),
    )(forcing, active.reshape(1, ncol), state)


TWO_STAGE = False


def exchange(chunks):
    if not TWO_STAGE:
        return lax.all_to_all(chunks, ("face", "col"), split_axis=0, concat_axis=0, tiled=True)
    nface = lax.axis_size("face")
    ncol = lax.axis_size("col")
    grid = chunks.reshape((nface, ncol) + chunks.shape[1:])
    grid = lax.all_to_all(grid, "col", split_axis=1, concat_axis=1, tiled=True)
    grid = lax.all_to_all(grid, "face", split_axis=0, concat_axis=0, tiled=True)
    return grid.reshape(chunks.shape)


def per_device(dyn_state, edge_links, phys_slot, crm_active, crm_state):
    laplace, spread, denom, quarter = [jnp.asarray(table) for table in node_tables()]
    rows_dev, cols_dev, nodes, width = dyn_state.shape
    nface = lax.axis_size("face")
    ncol = lax.axis_size("col")
    ndev = nface * ncol
    total_rows = rows_dev * nface
    total_cols = cols_dev * ncol
    neighbour = edge_links // 8
    pick = matched_points(edge_links)
    near_row = neighbour // total_cols
    near_col = neighbour % total_cols
    local_row = lax.broadcasted_iota(jnp.int32, (rows_dev, cols_dev, 4), 0)
    local_col = lax.broadcasted_iota(jnp.int32, (rows_dev, cols_dev, 4), 1)
    drow = (near_row - (lax.axis_index("face") * rows_dev + local_row) + 1) % total_rows - 1
    dcol = (near_col - (lax.axis_index("col") * cols_dev + local_col) + 1) % total_cols - 1
    place = (local_row + drow + 1) * (cols_dev + 2) + (local_col + dcol + 1)
    rim_slot = np.full(16, 0, np.int32)
    rim_slot[[0, 1, 2, 3, 4, 7, 8, 11, 12, 13, 14, 15]] = np.arange(12, dtype=np.int32)
    index_flat = place[..., None] * 12 + jnp.asarray(rim_slot)[pick]
    index_flat = index_flat.reshape(-1)
    state = dyn_state
    for step in range(DSTEPS):
        state = state + KAPPA * jnp.einsum(
            "nm,rcmw->rcnw", laplace, state, precision=lax.Precision.HIGHEST
        )
        extended = halo_table(rim_points(state))
        matched = jnp.take(extended.reshape(-1, width), index_flat, axis=0).reshape(
            rows_dev, cols_dev, 16, width
        )
        summed = jnp.einsum("nm,rcmw->rcnw", spread, matched, precision=lax.Precision.HIGHEST)
        state = (state + summed) / denom[None, None, :, None]
    columns = jnp.einsum("qn,rcnw->rcqw", quarter, state, precision=lax.Precision.HIGHEST).reshape(
        -1, NFLD, LEV
    )[:, :, :CLEV].reshape(-1, NFLD * CLEV)
    per_dev = columns.shape[0]
    count = per_dev // ndev
    keys_local = phys_slot.reshape(-1)
    order = jnp.argsort(keys_local, stable=True)
    out_keys = keys_local[order]
    outgoing = jnp.concatenate(
        [columns[order], out_keys.astype(jnp.float32)[:, None]], axis=1
    )
    arrived = exchange(outgoing.reshape(ndev, count, NFLD * CLEV + 1)).reshape(per_dev, -1)
    slots = arrived[:, NFLD * CLEV].astype(jnp.int32) % per_dev
    physics = jnp.zeros((per_dev, NFLD * CLEV), jnp.float32).at[slots].set(arrived[:, : NFLD * CLEV])
    forcing = physics.reshape(per_dev, NFLD, CLEV).transpose(1, 2, 0)
    crm_new, tend = crm_run(crm_state, forcing, crm_active)
    tend_rows = tend.reshape(NFLD * CLEV, per_dev).T[slots]
    returned = exchange(tend_rows.reshape(ndev, count, NFLD * CLEV))
    placed = (
        jnp.zeros((per_dev, NFLD * CLEV), jnp.float32)
        .at[order]
        .set(returned.reshape(per_dev, NFLD * CLEV))
    )
    column_tend = placed.reshape(rows_dev, cols_dev, 4, NFLD * CLEV)
    return (state, column_tend, crm_new)


def solution(mesh):
    return jax.shard_map(
        per_device,
        mesh=mesh,
        in_specs=(
            P("face", "col", None, None),
            P("face", "col", None),
            P("face", "col", None),
            P(("face", "col")),
            P(None, None, None, ("face", "col")),
        ),
        out_specs=(
            P("face", "col", None, None),
            P("face", "col", None, None),
            P(None, None, None, ("face", "col")),
        ),
        check_vma=False,
    )
```

```python
import jax
import jax.numpy as jnp
import numpy as np
from jax import lax
from jax.experimental import pallas as pl
from jax.experimental.pallas import tpu as pltpu
from jax.sharding import PartitionSpec as P

NFLD = 10
LEV = 72
CLEV = 32
DSTEPS = 2
CSTEPS = 2


KAPPA = 0.1
ADVECT = 0.1
DIFF_X = 0.2
DIFF_Z = 0.1
RELAX = 0.2
CONVERT = 0.5
KEEP = 1.0 - 2.0 * DIFF_X - 2.0 * DIFF_Z


def extended_2(cells, sides, width):
    for axis, dim in sides:
        count = lax.axis_size(axis)
        head = lax.slice_in_dim(cells, 0, width, axis=dim)
        tail = lax.slice_in_dim(cells, cells.shape[dim] - width, cells.shape[dim], axis=dim)
        cells = jnp.concatenate(
            [
                lax.ppermute(tail, axis, [(i, (i + 1) % count) for i in range(count)]),
                cells,
                lax.ppermute(head, axis, [((i + 1) % count, i) for i in range(count)]),
            ],
            axis=dim,
        )
    return cells


def node_tables():
    laplace = np.zeros((16, 16), np.float32)
    for row_a in range(4):
        for row_b in range(4):
            here = row_a * 4 + row_b
            for step_a, step_b in ((1, 0), (-1, 0), (0, 1), (0, -1)):
                near_a, near_b = (row_a + step_a, row_b + step_b)
                if 0 <= near_a < 4 and 0 <= near_b < 4:
                    laplace[here, near_a * 4 + near_b] += 1.0
                    laplace[here, here] -= 1.0
    edge_nodes = np.array([[0, 1, 2, 3], [3, 7, 11, 15], [12, 13, 14, 15], [0, 4, 8, 12]])
    spread = np.zeros((16, 16), np.float32)
    for edge in range(4):
        for point in range(4):
            spread[edge_nodes[edge, point], edge * 4 + point] = 1.0
    denom = 1.0 + spread.sum(axis=1)
    quarter = np.zeros((4, 16), np.float32)
    for row_a in range(4):
        for row_b in range(4):
            quarter[row_a // 2 * 2 + row_b // 2, row_a * 4 + row_b] = 0.25
    return (laplace, spread, denom, quarter)


def matched_points(links):
    other_edge = links // 2 % 4
    reversal = links % 2
    points = jnp.arange(4, dtype=jnp.int32)
    along = jnp.where(reversal[..., None] == 1, 3 - points, points)
    base = jnp.where(other_edge == 1, 3, jnp.where(other_edge == 2, 12, 0))
    stride = jnp.where((other_edge == 1) | (other_edge == 3), 4, 1)
    return base[..., None] + stride[..., None] * along


ZCHUNK = 4


def crm_kernel(force_ref, live_ref, state_hbm, new_hbm, tend_ref, held, wide, mid, out, in_sem, out_sem):
    nfld, nlev, nx, _ = held.shape
    chunks = nlev // ZCHUNK

    def in_copy(c):
        part = pl.ds(c * ZCHUNK, ZCHUNK)
        return pltpu.make_async_copy(state_hbm.at[:, part], held.at[:, part], in_sem.at[c])

    def out_copy(c):
        part = pl.ds(c * ZCHUNK, ZCHUNK)
        return pltpu.make_async_copy(out.at[:, part], new_hbm.at[:, part], out_sem.at[c])

    for c in range(chunks):
        in_copy(c).start()
    live = live_ref[...] == 1

    def sweep(src, z, last):
        upper_z = jnp.minimum(z + 1, nlev - 1)
        lower_z = jnp.maximum(z - 1, 0)
        if last:
            lead = ADVECT * mid[0, z]
        else:
            lead = ADVECT * wide[0, z]
        kept = {}

        def finish(f, fresh, state):
            new = jnp.where(live, fresh, state)
            if last:
                out[f, z] = new.astype(out.dtype)
                tend_ref[f, pl.ds(z, 1)] = (jnp.mean(new, axis=0, keepdims=True) - tend_ref[f, pl.ds(z, 1)]) / CSTEPS
            else:
                mid[f, z] = new

        for f in range(nfld):
            if last:
                state = mid[f, z]
                upper = mid[f, upper_z]
                lower = mid[f, lower_z]
            else:
                state = wide[f, z]
                lower = wide[f, lower_z]
                upper = held[f, upper_z].astype(jnp.float32)
                wide[f, upper_z] = upper
            east = pltpu.roll(state, nx - 1, 0)
            west = pltpu.roll(state, 1, 0)
            mean_x = jnp.mean(state, axis=0, keepdims=True)
            if not last:
                tend_ref[f, pl.ds(z, 1)] = mean_x
            fresh = (
                KEEP * state
                + DIFF_X * (east + west)
                + DIFF_Z * (upper + lower)
                - lead * (east - west)
                + RELAX * (force_ref[f, pl.ds(z, 1)] - mean_x)
            )
            if f in (2, 3):
                kept[f] = (fresh, state)
                if f == 3:
                    cond = CONVERT * jnp.maximum(kept[3][0] - kept[2][0], 0.0)
                    finish(2, *kept[2])
                    finish(3, kept[3][0] - cond, kept[3][1])
                continue
            if f == 4:
                fresh = fresh + cond
            finish(f, fresh, state)

    for c in range(chunks):
        if c == 0:
            in_copy(0).wait()
            for f in range(nfld):
                wide[f, 0] = held[f, 0].astype(jnp.float32)
        if c + 1 < chunks:
            in_copy(c + 1).wait()

        def first(z, carry):
            sweep(held, z, False)
            return carry

        lax.fori_loop(c * ZCHUNK, (c + 1) * ZCHUNK, first, 0)
    for c in range(chunks):

        def second(z, carry):
            sweep(mid, z, True)
            return carry

        lax.fori_loop(c * ZCHUNK, (c + 1) * ZCHUNK, second, 0)
        out_copy(c).start()
    for c in range(chunks):
        out_copy(c).wait()


def crm_run(state, forcing, active):
    nfld, nlev, nx, ncol = state.shape
    return pl.pallas_call(
        crm_kernel,
        out_shape=(
            jax.ShapeDtypeStruct(state.shape, jnp.bfloat16),
            jax.ShapeDtypeStruct((nfld, nlev, ncol), jnp.float32),
        ),
        in_specs=[
            pl.BlockSpec(memory_space=pltpu.VMEM),
            pl.BlockSpec(memory_space=pltpu.VMEM),
            pl.BlockSpec(memory_space=pltpu.HBM),
        ],
        out_specs=(
            pl.BlockSpec(memory_space=pltpu.HBM),
            pl.BlockSpec(memory_space=pltpu.VMEM),
        ),
        scratch_shapes=[
            pltpu.VMEM(state.shape, jnp.bfloat16),
            pltpu.VMEM(state.shape, jnp.float32),
            pltpu.VMEM(state.shape, jnp.float32),
            pltpu.VMEM(state.shape, jnp.bfloat16),
            pltpu.SemaphoreType.DMA((nlev // ZCHUNK,)),
            pltpu.SemaphoreType.DMA((nlev // ZCHUNK,)),
        ],
        compiler_params=pltpu.CompilerParams(vmem_limit_bytes=48 * 1024 * 1024),
    )(forcing, active.reshape(1, ncol), state)


TWO_STAGE = False


def exchange(chunks):
    if not TWO_STAGE:
        return lax.all_to_all(chunks, ("face", "col"), split_axis=0, concat_axis=0, tiled=True)
    nface = lax.axis_size("face")
    ncol = lax.axis_size("col")
    grid = chunks.reshape((nface, ncol) + chunks.shape[1:])
    grid = lax.all_to_all(grid, "col", split_axis=1, concat_axis=1, tiled=True)
    grid = lax.all_to_all(grid, "face", split_axis=0, concat_axis=0, tiled=True)
    return grid.reshape(chunks.shape)


def per_device(dyn_state, edge_links, phys_slot, crm_active, crm_state):
    laplace, spread, denom, quarter = [jnp.asarray(table) for table in node_tables()]
    rows_dev, cols_dev, nodes, width = dyn_state.shape
    nface = lax.axis_size("face")
    ncol = lax.axis_size("col")
    ndev = nface * ncol
    total_rows = rows_dev * nface
    total_cols = cols_dev * ncol
    neighbour = edge_links // 8
    pick = matched_points(edge_links)
    near_row = neighbour // total_cols
    near_col = neighbour % total_cols
    local_row = lax.broadcasted_iota(jnp.int32, (rows_dev, cols_dev, 4), 0)
    local_col = lax.broadcasted_iota(jnp.int32, (rows_dev, cols_dev, 4), 1)
    drow = (near_row - (lax.axis_index("face") * rows_dev + local_row) + 1) % total_rows - 1
    dcol = (near_col - (lax.axis_index("col") * cols_dev + local_col) + 1) % total_cols - 1
    place = (local_row + drow + 1) * (cols_dev + 2) + (local_col + dcol + 1)
    index_flat = place[..., None] * 16 + pick
    index_flat = index_flat.reshape(-1)
    state = dyn_state
    for step in range(DSTEPS):
        state = state + KAPPA * jnp.einsum(
            "nm,rcmw->rcnw", laplace, state, precision=lax.Precision.HIGHEST
        )
        extended = extended_2(state, (("face", 0), ("col", 1)), 1)
        matched = jnp.take(extended.reshape(-1, width), index_flat, axis=0).reshape(
            rows_dev, cols_dev, 16, width
        )
        summed = jnp.einsum("nm,rcmw->rcnw", spread, matched, precision=lax.Precision.HIGHEST)
        state = (state + summed) / denom[None, None, :, None]
    columns = jnp.einsum("qn,rcnw->rcqw", quarter, state, precision=lax.Precision.HIGHEST).reshape(
        -1, NFLD, LEV
    )[:, :, :CLEV].reshape(-1, NFLD * CLEV)
    per_dev = columns.shape[0]
    count = per_dev // ndev
    keys_local = phys_slot.reshape(-1)
    order = jnp.argsort(keys_local, stable=True)
    out_keys = keys_local[order]
    outgoing = jnp.concatenate(
        [columns[order], out_keys.astype(jnp.float32)[:, None]], axis=1
    )
    arrived = exchange(outgoing.reshape(ndev, count, NFLD * CLEV + 1)).reshape(per_dev, -1)
    slots = arrived[:, NFLD * CLEV].astype(jnp.int32) % per_dev
    physics = jnp.zeros((per_dev, NFLD * CLEV), jnp.float32).at[slots].set(arrived[:, : NFLD * CLEV])
    forcing = physics.reshape(per_dev, NFLD, CLEV).transpose(1, 2, 0)
    crm_new, tend = crm_run(crm_state, forcing, crm_active)
    tend_rows = tend.reshape(NFLD * CLEV, per_dev).T[slots]
    returned = exchange(tend_rows.reshape(ndev, count, NFLD * CLEV))
    placed = (
        jnp.zeros((per_dev, NFLD * CLEV), jnp.float32)
        .at[order]
        .set(returned.reshape(per_dev, NFLD * CLEV))
    )
    column_tend = placed.reshape(rows_dev, cols_dev, 4, NFLD * CLEV)
    return (state, column_tend, crm_new)


def solution(mesh):
    return jax.shard_map(
        per_device,
        mesh=mesh,
        in_specs=(
            P("face", "col", None, None),
            P("face", "col", None),
            P("face", "col", None),
            P(("face", "col")),
            P(None, None, None, ("face", "col")),
        ),
        out_specs=(
            P("face", "col", None, None),
            P("face", "col", None, None),
            P(None, None, None, ("face", "col")),
        ),
        check_vma=False,
    )
```

```python
import jax
import jax.numpy as jnp
import numpy as np
from jax import lax
from jax.experimental import pallas as pl
from jax.experimental.pallas import tpu as pltpu
from jax.sharding import PartitionSpec as P

NFLD = 10
LEV = 72
CLEV = 32
DSTEPS = 2
CSTEPS = 2


KAPPA = 0.1
ADVECT = 0.1
DIFF_X = 0.2
DIFF_Z = 0.1
RELAX = 0.2
CONVERT = 0.5
KEEP = 1.0 - 2.0 * DIFF_X - 2.0 * DIFF_Z


def extended_2(cells, sides, width):
    for axis, dim in sides:
        count = lax.axis_size(axis)
        head = lax.slice_in_dim(cells, 0, width, axis=dim)
        tail = lax.slice_in_dim(cells, cells.shape[dim] - width, cells.shape[dim], axis=dim)
        cells = jnp.concatenate(
            [
                lax.ppermute(tail, axis, [(i, (i + 1) % count) for i in range(count)]),
                cells,
                lax.ppermute(head, axis, [((i + 1) % count, i) for i in range(count)]),
            ],
            axis=dim,
        )
    return cells


def node_tables():
    laplace = np.zeros((16, 16), np.float32)
    for row_a in range(4):
        for row_b in range(4):
            here = row_a * 4 + row_b
            for step_a, step_b in ((1, 0), (-1, 0), (0, 1), (0, -1)):
                near_a, near_b = (row_a + step_a, row_b + step_b)
                if 0 <= near_a < 4 and 0 <= near_b < 4:
                    laplace[here, near_a * 4 + near_b] += 1.0
                    laplace[here, here] -= 1.0
    edge_nodes = np.array([[0, 1, 2, 3], [3, 7, 11, 15], [12, 13, 14, 15], [0, 4, 8, 12]])
    spread = np.zeros((16, 16), np.float32)
    for edge in range(4):
        for point in range(4):
            spread[edge_nodes[edge, point], edge * 4 + point] = 1.0
    denom = 1.0 + spread.sum(axis=1)
    quarter = np.zeros((4, 16), np.float32)
    for row_a in range(4):
        for row_b in range(4):
            quarter[row_a // 2 * 2 + row_b // 2, row_a * 4 + row_b] = 0.25
    return (laplace, spread, denom, quarter)


def matched_points(links):
    other_edge = links // 2 % 4
    reversal = links % 2
    points = jnp.arange(4, dtype=jnp.int32)
    along = jnp.where(reversal[..., None] == 1, 3 - points, points)
    base = jnp.where(other_edge == 1, 3, jnp.where(other_edge == 2, 12, 0))
    stride = jnp.where((other_edge == 1) | (other_edge == 3), 4, 1)
    return base[..., None] + stride[..., None] * along


ZCHUNK = 4


def chunk_copies(src, dst, sems, count):
    def one(c):
        part = pl.ds(c * ZCHUNK, ZCHUNK)
        return pltpu.make_async_copy(src.at[:, part], dst.at[:, part], sems.at[c])

    return [one(c) for c in range(count)]


def neighbours(z, nlev):
    return jnp.minimum(z + 1, nlev - 1), jnp.maximum(z - 1, 0)


def crm_first_kernel(live_ref, state_hbm, part_hbm, mean_ref, held, wide, part, in_sem, out_sem):
    nfld, nlev, nx, _ = held.shape
    chunks = nlev // ZCHUNK
    loads = chunk_copies(state_hbm, held, in_sem, chunks)
    stores = chunk_copies(part, part_hbm, out_sem, chunks)
    for copy in loads:
        copy.start()
    live = live_ref[...] == 1

    def level(z, carry):
        upper_z, lower_z = neighbours(z, nlev)
        lead = ADVECT * wide[0, z]
        for f in range(nfld):
            state = wide[f, z]
            lower = wide[f, lower_z]
            upper = held[f, upper_z].astype(jnp.float32)
            wide[f, upper_z] = upper
            east = pltpu.roll(state, nx - 1, 0)
            west = pltpu.roll(state, 1, 0)
            mean_ref[f, pl.ds(z, 1)] = jnp.mean(state, axis=0, keepdims=True)
            fresh = KEEP * state + DIFF_X * (east + west) + DIFF_Z * (upper + lower) - lead * (east - west)
            part[f, z] = jnp.where(live, fresh, state)
        return carry

    for c in range(chunks):
        if c == 0:
            loads[0].wait()
            for f in range(nfld):
                wide[f, 0] = held[f, 0].astype(jnp.float32)
        if c + 1 < chunks:
            loads[c + 1].wait()
        lax.fori_loop(c * ZCHUNK, (c + 1) * ZCHUNK, level, 0)
        stores[c].start()
    for copy in stores:
        copy.wait()


def crm_second_kernel(force_ref, live_ref, mean_ref, part_hbm, new_hbm, tend_ref, mid, out, in_sem, out_sem):
    nfld, nlev, nx, _ = mid.shape
    chunks = nlev // ZCHUNK
    loads = chunk_copies(part_hbm, mid, in_sem, chunks)
    stores = chunk_copies(out, new_hbm, out_sem, chunks)
    for copy in loads:
        copy.start()
    live = live_ref[...] == 1

    def finish_first(z, carry):
        fresh = [
            mid[f, z]
            + jnp.where(live, RELAX * (force_ref[f, pl.ds(z, 1)] - mean_ref[f, pl.ds(z, 1)]), 0.0)
            for f in range(nfld)
        ]
        cond = CONVERT * jnp.maximum(fresh[3] - fresh[2], 0.0)
        fresh[3] = jnp.where(live, fresh[3] - cond, fresh[3])
        fresh[4] = jnp.where(live, fresh[4] + cond, fresh[4])
        for f in range(nfld):
            mid[f, z] = fresh[f]
        return carry

    for c in range(chunks):
        loads[c].wait()
        lax.fori_loop(c * ZCHUNK, (c + 1) * ZCHUNK, finish_first, 0)

    def level(z, carry):
        upper_z, lower_z = neighbours(z, nlev)
        lead = ADVECT * mid[0, z]
        kept = {}

        def finish(f, fresh, state):
            new = jnp.where(live, fresh, state)
            out[f, z] = new.astype(out.dtype)
            tend_ref[f, pl.ds(z, 1)] = (jnp.mean(new, axis=0, keepdims=True) - mean_ref[f, pl.ds(z, 1)]) / CSTEPS

        for f in range(nfld):
            state = mid[f, z]
            upper = mid[f, upper_z]
            lower = mid[f, lower_z]
            east = pltpu.roll(state, nx - 1, 0)
            west = pltpu.roll(state, 1, 0)
            mean_x = jnp.mean(state, axis=0, keepdims=True)
            fresh = (
                KEEP * state
                + DIFF_X * (east + west)
                + DIFF_Z * (upper + lower)
                - lead * (east - west)
                + RELAX * (force_ref[f, pl.ds(z, 1)] - mean_x)
            )
            if f in (2, 3):
                kept[f] = (fresh, state)
                if f == 3:
                    cond = CONVERT * jnp.maximum(kept[3][0] - kept[2][0], 0.0)
                    finish(2, *kept[2])
                    finish(3, kept[3][0] - cond, kept[3][1])
                continue
            if f == 4:
                fresh = fresh + cond
            finish(f, fresh, state)
        return carry

    for c in range(chunks):
        lax.fori_loop(c * ZCHUNK, (c + 1) * ZCHUNK, level, 0)
        stores[c].start()
    for copy in stores:
        copy.wait()


def crm_first(state, active):
    nfld, nlev, nx, ncol = state.shape
    chunks = nlev // ZCHUNK
    return pl.pallas_call(
        crm_first_kernel,
        out_shape=(
            jax.ShapeDtypeStruct(state.shape, jnp.float32),
            jax.ShapeDtypeStruct((nfld, nlev, ncol), jnp.float32),
        ),
        in_specs=[pl.BlockSpec(memory_space=pltpu.VMEM), pl.BlockSpec(memory_space=pl.ANY)],
        out_specs=(pl.BlockSpec(memory_space=pl.ANY), pl.BlockSpec(memory_space=pltpu.VMEM)),
        scratch_shapes=[
            pltpu.VMEM(state.shape, jnp.bfloat16),
            pltpu.VMEM(state.shape, jnp.float32),
            pltpu.VMEM(state.shape, jnp.float32),
            pltpu.SemaphoreType.DMA((chunks,)),
            pltpu.SemaphoreType.DMA((chunks,)),
        ],
        compiler_params=pltpu.CompilerParams(vmem_limit_bytes=48 * 1024 * 1024),
    )(active.reshape(1, ncol), state)


def crm_second(part, start_mean, forcing, active):
    nfld, nlev, nx, ncol = part.shape
    chunks = nlev // ZCHUNK
    return pl.pallas_call(
        crm_second_kernel,
        out_shape=(
            jax.ShapeDtypeStruct(part.shape, jnp.bfloat16),
            jax.ShapeDtypeStruct((nfld, nlev, ncol), jnp.float32),
        ),
        in_specs=[
            pl.BlockSpec(memory_space=pltpu.VMEM),
            pl.BlockSpec(memory_space=pltpu.VMEM),
            pl.BlockSpec(memory_space=pltpu.VMEM),
            pl.BlockSpec(memory_space=pl.ANY),
        ],
        out_specs=(pl.BlockSpec(memory_space=pl.ANY), pl.BlockSpec(memory_space=pltpu.VMEM)),
        scratch_shapes=[
            pltpu.VMEM(part.shape, jnp.float32),
            pltpu.VMEM(part.shape, jnp.bfloat16),
            pltpu.SemaphoreType.DMA((chunks,)),
            pltpu.SemaphoreType.DMA((chunks,)),
        ],
        compiler_params=pltpu.CompilerParams(vmem_limit_bytes=48 * 1024 * 1024),
    )(forcing, active.reshape(1, ncol), start_mean, part)


def crm_run(state, forcing, active):
    part, start_mean = crm_first(state, active)
    return crm_second(part, start_mean, forcing, active)


TWO_STAGE = False


def exchange(chunks):
    if not TWO_STAGE:
        return lax.all_to_all(chunks, ("face", "col"), split_axis=0, concat_axis=0, tiled=True)
    nface = lax.axis_size("face")
    ncol = lax.axis_size("col")
    grid = chunks.reshape((nface, ncol) + chunks.shape[1:])
    grid = lax.all_to_all(grid, "col", split_axis=1, concat_axis=1, tiled=True)
    grid = lax.all_to_all(grid, "face", split_axis=0, concat_axis=0, tiled=True)
    return grid.reshape(chunks.shape)


def per_device(dyn_state, edge_links, phys_slot, crm_active, crm_state):
    laplace, spread, denom, quarter = [jnp.asarray(table) for table in node_tables()]
    rows_dev, cols_dev, nodes, width = dyn_state.shape
    nface = lax.axis_size("face")
    ncol = lax.axis_size("col")
    ndev = nface * ncol
    total_rows = rows_dev * nface
    total_cols = cols_dev * ncol
    neighbour = edge_links // 8
    pick = matched_points(edge_links)
    near_row = neighbour // total_cols
    near_col = neighbour % total_cols
    local_row = lax.broadcasted_iota(jnp.int32, (rows_dev, cols_dev, 4), 0)
    local_col = lax.broadcasted_iota(jnp.int32, (rows_dev, cols_dev, 4), 1)
    drow = (near_row - (lax.axis_index("face") * rows_dev + local_row) + 1) % total_rows - 1
    dcol = (near_col - (lax.axis_index("col") * cols_dev + local_col) + 1) % total_cols - 1
    place = (local_row + drow + 1) * (cols_dev + 2) + (local_col + dcol + 1)
    index_flat = place[..., None] * 16 + pick
    index_flat = index_flat.reshape(-1)
    state = dyn_state
    for step in range(DSTEPS):
        state = state + KAPPA * jnp.einsum(
            "nm,rcmw->rcnw", laplace, state, precision=lax.Precision.HIGHEST
        )
        extended = extended_2(state, (("face", 0), ("col", 1)), 1)
        matched = jnp.take(extended.reshape(-1, width), index_flat, axis=0).reshape(
            rows_dev, cols_dev, 16, width
        )
        summed = jnp.einsum("nm,rcmw->rcnw", spread, matched, precision=lax.Precision.HIGHEST)
        state = (state + summed) / denom[None, None, :, None]
    columns = jnp.einsum("qn,rcnw->rcqw", quarter, state, precision=lax.Precision.HIGHEST).reshape(
        -1, NFLD, LEV
    )[:, :, :CLEV].reshape(-1, NFLD * CLEV)
    per_dev = columns.shape[0]
    count = per_dev // ndev
    keys_local = phys_slot.reshape(-1)
    order = jnp.argsort(keys_local, stable=True)
    out_keys = keys_local[order]
    outgoing = jnp.concatenate(
        [columns[order], out_keys.astype(jnp.float32)[:, None]], axis=1
    )
    arrived = exchange(outgoing.reshape(ndev, count, NFLD * CLEV + 1)).reshape(per_dev, -1)
    slots = arrived[:, NFLD * CLEV].astype(jnp.int32) % per_dev
    physics = jnp.zeros((per_dev, NFLD * CLEV), jnp.float32).at[slots].set(arrived[:, : NFLD * CLEV])
    forcing = physics.reshape(per_dev, NFLD, CLEV).transpose(1, 2, 0)
    crm_new, tend = crm_run(crm_state, forcing, crm_active)
    tend_rows = tend.reshape(NFLD * CLEV, per_dev).T[slots]
    returned = exchange(tend_rows.reshape(ndev, count, NFLD * CLEV))
    placed = (
        jnp.zeros((per_dev, NFLD * CLEV), jnp.float32)
        .at[order]
        .set(returned.reshape(per_dev, NFLD * CLEV))
    )
    column_tend = placed.reshape(rows_dev, cols_dev, 4, NFLD * CLEV)
    return (state, column_tend, crm_new)


def solution(mesh):
    return jax.shard_map(
        per_device,
        mesh=mesh,
        in_specs=(
            P("face", "col", None, None),
            P("face", "col", None),
            P("face", "col", None),
            P(("face", "col")),
            P(None, None, None, ("face", "col")),
        ),
        out_specs=(
            P("face", "col", None, None),
            P("face", "col", None, None),
            P(None, None, None, ("face", "col")),
        ),
        check_vma=False,
    )
```

```python
import jax
import jax.numpy as jnp
import numpy as np
from jax import lax
from jax.experimental import pallas as pl
from jax.experimental.pallas import tpu as pltpu
from jax.sharding import PartitionSpec as P

NFLD = 10
LEV = 72
CLEV = 32
DSTEPS = 2
CSTEPS = 2


KAPPA = 0.1
ADVECT = 0.1
DIFF_X = 0.2
DIFF_Z = 0.1
RELAX = 0.2
CONVERT = 0.5
KEEP = 1.0 - 2.0 * DIFF_X - 2.0 * DIFF_Z


def extended_2(cells, sides, width):
    for axis, dim in sides:
        count = lax.axis_size(axis)
        head = lax.slice_in_dim(cells, 0, width, axis=dim)
        tail = lax.slice_in_dim(cells, cells.shape[dim] - width, cells.shape[dim], axis=dim)
        cells = jnp.concatenate(
            [
                lax.ppermute(tail, axis, [(i, (i + 1) % count) for i in range(count)]),
                cells,
                lax.ppermute(head, axis, [((i + 1) % count, i) for i in range(count)]),
            ],
            axis=dim,
        )
    return cells


def node_tables():
    laplace = np.zeros((16, 16), np.float32)
    for row_a in range(4):
        for row_b in range(4):
            here = row_a * 4 + row_b
            for step_a, step_b in ((1, 0), (-1, 0), (0, 1), (0, -1)):
                near_a, near_b = (row_a + step_a, row_b + step_b)
                if 0 <= near_a < 4 and 0 <= near_b < 4:
                    laplace[here, near_a * 4 + near_b] += 1.0
                    laplace[here, here] -= 1.0
    edge_nodes = np.array([[0, 1, 2, 3], [3, 7, 11, 15], [12, 13, 14, 15], [0, 4, 8, 12]])
    spread = np.zeros((16, 16), np.float32)
    for edge in range(4):
        for point in range(4):
            spread[edge_nodes[edge, point], edge * 4 + point] = 1.0
    denom = 1.0 + spread.sum(axis=1)
    quarter = np.zeros((4, 16), np.float32)
    for row_a in range(4):
        for row_b in range(4):
            quarter[row_a // 2 * 2 + row_b // 2, row_a * 4 + row_b] = 0.25
    return (laplace, spread, denom, quarter)


def matched_points(links):
    other_edge = links // 2 % 4
    reversal = links % 2
    points = jnp.arange(4, dtype=jnp.int32)
    along = jnp.where(reversal[..., None] == 1, 3 - points, points)
    base = jnp.where(other_edge == 1, 3, jnp.where(other_edge == 2, 12, 0))
    stride = jnp.where((other_edge == 1) | (other_edge == 3), 4, 1)
    return base[..., None] + stride[..., None] * along


ZCHUNK = 4


def chunk_copies(src, dst, sems, count):
    def one(c):
        part = pl.ds(c * ZCHUNK, ZCHUNK)
        return pltpu.make_async_copy(src.at[:, part], dst.at[:, part], sems.at[c])

    return [one(c) for c in range(count)]


def neighbours(z, nlev):
    return jnp.minimum(z + 1, nlev - 1), jnp.maximum(z - 1, 0)


def crm_first_kernel(live_ref, state_hbm, part_hbm, mean_ref, held, wide, part, in_sem, out_sem):
    nfld, nlev, nx, _ = held.shape
    chunks = nlev // ZCHUNK
    loads = chunk_copies(state_hbm, held, in_sem, chunks)
    stores = chunk_copies(part, part_hbm, out_sem, chunks)
    for copy in loads:
        copy.start()
    live = live_ref[...] == 1

    def level(z, carry):
        upper_z, lower_z = neighbours(z, nlev)
        lead = ADVECT * wide[0, z]
        for f in range(nfld):
            state = wide[f, z]
            lower = wide[f, lower_z]
            upper = held[f, upper_z].astype(jnp.float32)
            wide[f, upper_z] = upper
            east = pltpu.roll(state, nx - 1, 0)
            west = pltpu.roll(state, 1, 0)
            mean_ref[f, pl.ds(z, 1)] = jnp.mean(state, axis=0, keepdims=True)
            fresh = KEEP * state + DIFF_X * (east + west) + DIFF_Z * (upper + lower) - lead * (east - west)
            part[f, z] = jnp.where(live, fresh, state)
        return carry

    for c in range(chunks):
        if c == 0:
            loads[0].wait()
            for f in range(nfld):
                wide[f, 0] = held[f, 0].astype(jnp.float32)
        if c + 1 < chunks:
            loads[c + 1].wait()
        lax.fori_loop(c * ZCHUNK, (c + 1) * ZCHUNK, level, 0)
        stores[c].start()
    for copy in stores:
        copy.wait()


def crm_second_kernel(force_ref, live_ref, mean_ref, part_hbm, new_hbm, tend_ref, mid, out, in_sem, out_sem):
    nfld, nlev, nx, _ = mid.shape
    chunks = nlev // ZCHUNK
    loads = chunk_copies(part_hbm, mid, in_sem, chunks)
    stores = chunk_copies(out, new_hbm, out_sem, chunks)
    for copy in loads:
        copy.start()
    live = live_ref[...] == 1

    def finish_first(z, carry):
        fresh = [
            mid[f, z]
            + jnp.where(live, RELAX * (force_ref[f, pl.ds(z, 1)] - mean_ref[f, pl.ds(z, 1)]), 0.0)
            for f in range(nfld)
        ]
        cond = CONVERT * jnp.maximum(fresh[3] - fresh[2], 0.0)
        fresh[3] = jnp.where(live, fresh[3] - cond, fresh[3])
        fresh[4] = jnp.where(live, fresh[4] + cond, fresh[4])
        for f in range(nfld):
            mid[f, z] = fresh[f]
        return carry

    for c in range(chunks):
        loads[c].wait()
        lax.fori_loop(c * ZCHUNK, (c + 1) * ZCHUNK, finish_first, 0)

    def level(z, carry):
        upper_z, lower_z = neighbours(z, nlev)
        lead = ADVECT * mid[0, z]
        kept = {}

        def finish(f, fresh, state):
            new = jnp.where(live, fresh, state)
            out[f, z] = new.astype(out.dtype)
            tend_ref[f, pl.ds(z, 1)] = (jnp.mean(new, axis=0, keepdims=True) - mean_ref[f, pl.ds(z, 1)]) / CSTEPS

        for f in range(nfld):
            state = mid[f, z]
            upper = mid[f, upper_z]
            lower = mid[f, lower_z]
            east = pltpu.roll(state, nx - 1, 0)
            west = pltpu.roll(state, 1, 0)
            mean_x = jnp.mean(state, axis=0, keepdims=True)
            fresh = (
                KEEP * state
                + DIFF_X * (east + west)
                + DIFF_Z * (upper + lower)
                - lead * (east - west)
                + RELAX * (force_ref[f, pl.ds(z, 1)] - mean_x)
            )
            if f in (2, 3):
                kept[f] = (fresh, state)
                if f == 3:
                    cond = CONVERT * jnp.maximum(kept[3][0] - kept[2][0], 0.0)
                    finish(2, *kept[2])
                    finish(3, kept[3][0] - cond, kept[3][1])
                continue
            if f == 4:
                fresh = fresh + cond
            finish(f, fresh, state)
        return carry

    for c in range(chunks):
        lax.fori_loop(c * ZCHUNK, (c + 1) * ZCHUNK, level, 0)
        stores[c].start()
    for copy in stores:
        copy.wait()


def crm_first(state, active):
    nfld, nlev, nx, ncol = state.shape
    chunks = nlev // ZCHUNK
    return pl.pallas_call(
        crm_first_kernel,
        out_shape=(
            jax.ShapeDtypeStruct(state.shape, jnp.float32),
            jax.ShapeDtypeStruct((nfld, nlev, ncol), jnp.float32),
        ),
        in_specs=[pl.BlockSpec(memory_space=pltpu.VMEM), pl.BlockSpec(memory_space=pl.ANY)],
        out_specs=(pl.BlockSpec(memory_space=pl.ANY), pl.BlockSpec(memory_space=pltpu.VMEM)),
        scratch_shapes=[
            pltpu.VMEM(state.shape, jnp.bfloat16),
            pltpu.VMEM(state.shape, jnp.float32),
            pltpu.VMEM(state.shape, jnp.float32),
            pltpu.SemaphoreType.DMA((chunks,)),
            pltpu.SemaphoreType.DMA((chunks,)),
        ],
        compiler_params=pltpu.CompilerParams(vmem_limit_bytes=48 * 1024 * 1024),
    )(active.reshape(1, ncol), state)


def crm_second(part, start_mean, forcing, active):
    nfld, nlev, nx, ncol = part.shape
    chunks = nlev // ZCHUNK
    return pl.pallas_call(
        crm_second_kernel,
        out_shape=(
            jax.ShapeDtypeStruct(part.shape, jnp.bfloat16),
            jax.ShapeDtypeStruct((nfld, nlev, ncol), jnp.float32),
        ),
        in_specs=[
            pl.BlockSpec(memory_space=pltpu.VMEM),
            pl.BlockSpec(memory_space=pltpu.VMEM),
            pl.BlockSpec(memory_space=pltpu.VMEM),
            pl.BlockSpec(memory_space=pl.ANY),
        ],
        out_specs=(pl.BlockSpec(memory_space=pl.ANY), pl.BlockSpec(memory_space=pltpu.VMEM)),
        scratch_shapes=[
            pltpu.VMEM(part.shape, jnp.float32),
            pltpu.VMEM(part.shape, jnp.bfloat16),
            pltpu.SemaphoreType.DMA((chunks,)),
            pltpu.SemaphoreType.DMA((chunks,)),
        ],
        compiler_params=pltpu.CompilerParams(vmem_limit_bytes=48 * 1024 * 1024),
    )(forcing, active.reshape(1, ncol), start_mean, part)


def crm_run(state, forcing, active):
    part, start_mean = crm_first(state, active)
    return crm_second(part, start_mean, forcing, active)


TWO_STAGE = False


def exchange(chunks):
    if not TWO_STAGE:
        return lax.all_to_all(chunks, ("face", "col"), split_axis=0, concat_axis=0, tiled=True)
    nface = lax.axis_size("face")
    ncol = lax.axis_size("col")
    grid = chunks.reshape((nface, ncol) + chunks.shape[1:])
    grid = lax.all_to_all(grid, "col", split_axis=1, concat_axis=1, tiled=True)
    grid = lax.all_to_all(grid, "face", split_axis=0, concat_axis=0, tiled=True)
    return grid.reshape(chunks.shape)


def per_device(dyn_state, edge_links, phys_slot, crm_active, crm_state):
    laplace, spread, denom, quarter = [jnp.asarray(table) for table in node_tables()]
    rows_dev, cols_dev, nodes, width = dyn_state.shape
    nface = lax.axis_size("face")
    ncol = lax.axis_size("col")
    ndev = nface * ncol
    total_rows = rows_dev * nface
    total_cols = cols_dev * ncol
    neighbour = edge_links // 8
    pick = matched_points(edge_links)
    near_row = neighbour // total_cols
    near_col = neighbour % total_cols
    local_row = lax.broadcasted_iota(jnp.int32, (rows_dev, cols_dev, 4), 0)
    local_col = lax.broadcasted_iota(jnp.int32, (rows_dev, cols_dev, 4), 1)
    drow = (near_row - (lax.axis_index("face") * rows_dev + local_row) + 1) % total_rows - 1
    dcol = (near_col - (lax.axis_index("col") * cols_dev + local_col) + 1) % total_cols - 1
    place = (local_row + drow + 1) * (cols_dev + 2) + (local_col + dcol + 1)
    index_flat = place[..., None] * 16 + pick
    index_flat = index_flat.reshape(-1)
    part, start_mean = crm_first(crm_state, crm_active)
    state = dyn_state
    for step in range(DSTEPS):
        state = state + KAPPA * jnp.einsum(
            "nm,rcmw->rcnw", laplace, state, precision=lax.Precision.HIGHEST
        )
        extended = extended_2(state, (("face", 0), ("col", 1)), 1)
        if step == 0:
            extended, part, start_mean = lax.optimization_barrier((extended, part, start_mean))
        matched = jnp.take(extended.reshape(-1, width), index_flat, axis=0).reshape(
            rows_dev, cols_dev, 16, width
        )
        summed = jnp.einsum("nm,rcmw->rcnw", spread, matched, precision=lax.Precision.HIGHEST)
        state = (state + summed) / denom[None, None, :, None]
    columns = jnp.einsum("qn,rcnw->rcqw", quarter, state, precision=lax.Precision.HIGHEST).reshape(
        -1, NFLD, LEV
    )[:, :, :CLEV].reshape(-1, NFLD * CLEV)
    per_dev = columns.shape[0]
    count = per_dev // ndev
    keys_local = phys_slot.reshape(-1)
    order = jnp.argsort(keys_local, stable=True)
    out_keys = keys_local[order]
    outgoing = jnp.concatenate(
        [columns[order], out_keys.astype(jnp.float32)[:, None]], axis=1
    )
    arrived = exchange(outgoing.reshape(ndev, count, NFLD * CLEV + 1)).reshape(per_dev, -1)
    slots = arrived[:, NFLD * CLEV].astype(jnp.int32) % per_dev
    physics = jnp.zeros((per_dev, NFLD * CLEV), jnp.float32).at[slots].set(arrived[:, : NFLD * CLEV])
    forcing = physics.reshape(per_dev, NFLD, CLEV).transpose(1, 2, 0)
    crm_new, tend = crm_second(part, start_mean, forcing, crm_active)
    tend_rows = tend.reshape(NFLD * CLEV, per_dev).T[slots]
    returned = exchange(tend_rows.reshape(ndev, count, NFLD * CLEV))
    placed = (
        jnp.zeros((per_dev, NFLD * CLEV), jnp.float32)
        .at[order]
        .set(returned.reshape(per_dev, NFLD * CLEV))
    )
    column_tend = placed.reshape(rows_dev, cols_dev, 4, NFLD * CLEV)
    return (state, column_tend, crm_new)


def solution(mesh):
    return jax.shard_map(
        per_device,
        mesh=mesh,
        in_specs=(
            P("face", "col", None, None),
            P("face", "col", None),
            P("face", "col", None),
            P(("face", "col")),
            P(None, None, None, ("face", "col")),
        ),
        out_specs=(
            P("face", "col", None, None),
            P("face", "col", None, None),
            P(None, None, None, ("face", "col")),
        ),
        check_vma=False,
    )
```

```python
import jax
import jax.numpy as jnp
import numpy as np
from jax import lax
from jax.experimental import pallas as pl
from jax.experimental.pallas import tpu as pltpu
from jax.sharding import PartitionSpec as P

NFLD = 10
LEV = 72
CLEV = 32
DSTEPS = 2
CSTEPS = 2


KAPPA = 0.1
ADVECT = 0.1
DIFF_X = 0.2
DIFF_Z = 0.1
RELAX = 0.2
CONVERT = 0.5
KEEP = 1.0 - 2.0 * DIFF_X - 2.0 * DIFF_Z


def extended_2(cells, sides, width):
    for axis, dim in sides:
        count = lax.axis_size(axis)
        head = lax.slice_in_dim(cells, 0, width, axis=dim)
        tail = lax.slice_in_dim(cells, cells.shape[dim] - width, cells.shape[dim], axis=dim)
        cells = jnp.concatenate(
            [
                lax.ppermute(tail, axis, [(i, (i + 1) % count) for i in range(count)]),
                cells,
                lax.ppermute(head, axis, [((i + 1) % count, i) for i in range(count)]),
            ],
            axis=dim,
        )
    return cells


def node_tables():
    laplace = np.zeros((16, 16), np.float32)
    for row_a in range(4):
        for row_b in range(4):
            here = row_a * 4 + row_b
            for step_a, step_b in ((1, 0), (-1, 0), (0, 1), (0, -1)):
                near_a, near_b = (row_a + step_a, row_b + step_b)
                if 0 <= near_a < 4 and 0 <= near_b < 4:
                    laplace[here, near_a * 4 + near_b] += 1.0
                    laplace[here, here] -= 1.0
    edge_nodes = np.array([[0, 1, 2, 3], [3, 7, 11, 15], [12, 13, 14, 15], [0, 4, 8, 12]])
    spread = np.zeros((16, 16), np.float32)
    for edge in range(4):
        for point in range(4):
            spread[edge_nodes[edge, point], edge * 4 + point] = 1.0
    denom = 1.0 + spread.sum(axis=1)
    quarter = np.zeros((4, 16), np.float32)
    for row_a in range(4):
        for row_b in range(4):
            quarter[row_a // 2 * 2 + row_b // 2, row_a * 4 + row_b] = 0.25
    return (laplace, spread, denom, quarter)


def matched_points(links):
    other_edge = links // 2 % 4
    reversal = links % 2
    points = jnp.arange(4, dtype=jnp.int32)
    along = jnp.where(reversal[..., None] == 1, 3 - points, points)
    base = jnp.where(other_edge == 1, 3, jnp.where(other_edge == 2, 12, 0))
    stride = jnp.where((other_edge == 1) | (other_edge == 3), 4, 1)
    return base[..., None] + stride[..., None] * along


ZCHUNK = 4


def chunk_copies(src, dst, sems, count):
    def one(c):
        part = pl.ds(c * ZCHUNK, ZCHUNK)
        return pltpu.make_async_copy(src.at[:, part], dst.at[:, part], sems.at[c])

    return [one(c) for c in range(count)]


def neighbours(z, nlev):
    return jnp.minimum(z + 1, nlev - 1), jnp.maximum(z - 1, 0)


def crm_first_kernel(live_ref, state_hbm, part_hbm, mean_ref, held, wide, part, in_sem, out_sem):
    nfld, nlev, nx, _ = held.shape
    chunks = nlev // ZCHUNK
    loads = chunk_copies(state_hbm, held, in_sem, chunks)
    stores = chunk_copies(part, part_hbm, out_sem, chunks)
    for copy in loads:
        copy.start()
    live = live_ref[...] == 1

    def level(z, carry):
        upper_z, lower_z = neighbours(z, nlev)
        lead = ADVECT * wide[0, z]
        for f in range(nfld):
            state = wide[f, z]
            lower = wide[f, lower_z]
            upper = held[f, upper_z].astype(jnp.float32)
            wide[f, upper_z] = upper
            east = pltpu.roll(state, nx - 1, 0)
            west = pltpu.roll(state, 1, 0)
            mean_ref[f, pl.ds(z, 1)] = jnp.mean(state, axis=0, keepdims=True)
            fresh = KEEP * state + DIFF_X * (east + west) + DIFF_Z * (upper + lower) - lead * (east - west)
            part[f, z] = jnp.where(live, fresh, state)
        return carry

    for c in range(chunks):
        if c == 0:
            loads[0].wait()
            for f in range(nfld):
                wide[f, 0] = held[f, 0].astype(jnp.float32)
        if c + 1 < chunks:
            loads[c + 1].wait()
        lax.fori_loop(c * ZCHUNK, (c + 1) * ZCHUNK, level, 0)
        stores[c].start()
    for copy in stores:
        copy.wait()


def crm_second_kernel(force_ref, live_ref, mean_ref, part_hbm, new_hbm, tend_ref, mid, out, in_sem, out_sem):
    nfld, nlev, nx, _ = mid.shape
    chunks = nlev // ZCHUNK
    loads = chunk_copies(part_hbm, mid, in_sem, chunks)
    stores = chunk_copies(out, new_hbm, out_sem, chunks)
    for copy in loads:
        copy.start()
    live = live_ref[...] == 1

    def finish_first(z, carry):
        fresh = [
            mid[f, z]
            + jnp.where(live, RELAX * (force_ref[f, pl.ds(z, 1)] - mean_ref[f, pl.ds(z, 1)]), 0.0)
            for f in range(nfld)
        ]
        cond = CONVERT * jnp.maximum(fresh[3] - fresh[2], 0.0)
        fresh[3] = jnp.where(live, fresh[3] - cond, fresh[3])
        fresh[4] = jnp.where(live, fresh[4] + cond, fresh[4])
        for f in range(nfld):
            mid[f, z] = fresh[f]
        return carry

    def level(z, carry):
        upper_z, lower_z = neighbours(z, nlev)
        lead = ADVECT * mid[0, z]
        kept = {}

        def finish(f, fresh, state):
            new = jnp.where(live, fresh, state)
            out[f, z] = new.astype(out.dtype)
            tend_ref[f, pl.ds(z, 1)] = (jnp.mean(new, axis=0, keepdims=True) - mean_ref[f, pl.ds(z, 1)]) / CSTEPS

        for f in range(nfld):
            state = mid[f, z]
            upper = mid[f, upper_z]
            lower = mid[f, lower_z]
            east = pltpu.roll(state, nx - 1, 0)
            west = pltpu.roll(state, 1, 0)
            mean_x = jnp.mean(state, axis=0, keepdims=True)
            fresh = (
                KEEP * state
                + DIFF_X * (east + west)
                + DIFF_Z * (upper + lower)
                - lead * (east - west)
                + RELAX * (force_ref[f, pl.ds(z, 1)] - mean_x)
            )
            if f in (2, 3):
                kept[f] = (fresh, state)
                if f == 3:
                    cond = CONVERT * jnp.maximum(kept[3][0] - kept[2][0], 0.0)
                    finish(2, *kept[2])
                    finish(3, kept[3][0] - cond, kept[3][1])
                continue
            if f == 4:
                fresh = fresh + cond
            finish(f, fresh, state)
        return carry

    def ahead(z, carry):
        @pl.when(z + 1 < nlev)
        def _():
            finish_first(z + 1, 0)

        return level(z, carry)

    loads[0].wait()
    finish_first(0, 0)
    for c in range(chunks):
        if c + 1 < chunks:
            loads[c + 1].wait()
        lax.fori_loop(c * ZCHUNK, (c + 1) * ZCHUNK, ahead, 0)
        stores[c].start()
    for copy in stores:
        copy.wait()


def crm_first(state, active):
    nfld, nlev, nx, ncol = state.shape
    chunks = nlev // ZCHUNK
    return pl.pallas_call(
        crm_first_kernel,
        out_shape=(
            jax.ShapeDtypeStruct(state.shape, jnp.float32),
            jax.ShapeDtypeStruct((nfld, nlev, ncol), jnp.float32),
        ),
        in_specs=[pl.BlockSpec(memory_space=pltpu.VMEM), pl.BlockSpec(memory_space=pl.ANY)],
        out_specs=(pl.BlockSpec(memory_space=pl.ANY), pl.BlockSpec(memory_space=pltpu.VMEM)),
        scratch_shapes=[
            pltpu.VMEM(state.shape, jnp.bfloat16),
            pltpu.VMEM(state.shape, jnp.float32),
            pltpu.VMEM(state.shape, jnp.float32),
            pltpu.SemaphoreType.DMA((chunks,)),
            pltpu.SemaphoreType.DMA((chunks,)),
        ],
        compiler_params=pltpu.CompilerParams(vmem_limit_bytes=48 * 1024 * 1024),
    )(active.reshape(1, ncol), state)


def crm_second(part, start_mean, forcing, active):
    nfld, nlev, nx, ncol = part.shape
    chunks = nlev // ZCHUNK
    return pl.pallas_call(
        crm_second_kernel,
        out_shape=(
            jax.ShapeDtypeStruct(part.shape, jnp.bfloat16),
            jax.ShapeDtypeStruct((nfld, nlev, ncol), jnp.float32),
        ),
        in_specs=[
            pl.BlockSpec(memory_space=pltpu.VMEM),
            pl.BlockSpec(memory_space=pltpu.VMEM),
            pl.BlockSpec(memory_space=pltpu.VMEM),
            pl.BlockSpec(memory_space=pl.ANY),
        ],
        out_specs=(pl.BlockSpec(memory_space=pl.ANY), pl.BlockSpec(memory_space=pltpu.VMEM)),
        scratch_shapes=[
            pltpu.VMEM(part.shape, jnp.float32),
            pltpu.VMEM(part.shape, jnp.bfloat16),
            pltpu.SemaphoreType.DMA((chunks,)),
            pltpu.SemaphoreType.DMA((chunks,)),
        ],
        compiler_params=pltpu.CompilerParams(vmem_limit_bytes=48 * 1024 * 1024),
    )(forcing, active.reshape(1, ncol), start_mean, part)


def crm_run(state, forcing, active):
    part, start_mean = crm_first(state, active)
    return crm_second(part, start_mean, forcing, active)


TWO_STAGE = False


def exchange(chunks):
    if not TWO_STAGE:
        return lax.all_to_all(chunks, ("face", "col"), split_axis=0, concat_axis=0, tiled=True)
    nface = lax.axis_size("face")
    ncol = lax.axis_size("col")
    grid = chunks.reshape((nface, ncol) + chunks.shape[1:])
    grid = lax.all_to_all(grid, "col", split_axis=1, concat_axis=1, tiled=True)
    grid = lax.all_to_all(grid, "face", split_axis=0, concat_axis=0, tiled=True)
    return grid.reshape(chunks.shape)


def per_device(dyn_state, edge_links, phys_slot, crm_active, crm_state):
    laplace, spread, denom, quarter = [jnp.asarray(table) for table in node_tables()]
    rows_dev, cols_dev, nodes, width = dyn_state.shape
    nface = lax.axis_size("face")
    ncol = lax.axis_size("col")
    ndev = nface * ncol
    total_rows = rows_dev * nface
    total_cols = cols_dev * ncol
    neighbour = edge_links // 8
    pick = matched_points(edge_links)
    near_row = neighbour // total_cols
    near_col = neighbour % total_cols
    local_row = lax.broadcasted_iota(jnp.int32, (rows_dev, cols_dev, 4), 0)
    local_col = lax.broadcasted_iota(jnp.int32, (rows_dev, cols_dev, 4), 1)
    drow = (near_row - (lax.axis_index("face") * rows_dev + local_row) + 1) % total_rows - 1
    dcol = (near_col - (lax.axis_index("col") * cols_dev + local_col) + 1) % total_cols - 1
    place = (local_row + drow + 1) * (cols_dev + 2) + (local_col + dcol + 1)
    index_flat = place[..., None] * 16 + pick
    index_flat = index_flat.reshape(-1)
    part, start_mean = crm_first(crm_state, crm_active)
    state = dyn_state
    for step in range(DSTEPS):
        state = state + KAPPA * jnp.einsum(
            "nm,rcmw->rcnw", laplace, state, precision=lax.Precision.HIGHEST
        )
        if step == 0:
            faced = extended_2(state, (("face", 0),), 1)
            faced, part, start_mean = lax.optimization_barrier((faced, part, start_mean))
            extended = extended_2(faced, (("col", 1),), 1)
        else:
            extended = extended_2(state, (("face", 0), ("col", 1)), 1)
        matched = jnp.take(extended.reshape(-1, width), index_flat, axis=0).reshape(
            rows_dev, cols_dev, 16, width
        )
        summed = jnp.einsum("nm,rcmw->rcnw", spread, matched, precision=lax.Precision.HIGHEST)
        state = (state + summed) / denom[None, None, :, None]
    columns = jnp.einsum("qn,rcnw->rcqw", quarter, state, precision=lax.Precision.HIGHEST).reshape(
        -1, NFLD, LEV
    )[:, :, :CLEV].reshape(-1, NFLD * CLEV)
    per_dev = columns.shape[0]
    count = per_dev // ndev
    keys_local = phys_slot.reshape(-1)
    order = jnp.argsort(keys_local, stable=True)
    out_keys = keys_local[order]
    outgoing = jnp.concatenate(
        [columns[order], out_keys.astype(jnp.float32)[:, None]], axis=1
    )
    arrived = exchange(outgoing.reshape(ndev, count, NFLD * CLEV + 1)).reshape(per_dev, -1)
    slots = arrived[:, NFLD * CLEV].astype(jnp.int32) % per_dev
    physics = jnp.zeros((per_dev, NFLD * CLEV), jnp.float32).at[slots].set(arrived[:, : NFLD * CLEV])
    forcing = physics.reshape(per_dev, NFLD, CLEV).transpose(1, 2, 0)
    crm_new, tend = crm_second(part, start_mean, forcing, crm_active)
    tend_rows = tend.reshape(NFLD * CLEV, per_dev).T[slots]
    returned = exchange(tend_rows.reshape(ndev, count, NFLD * CLEV))
    placed = (
        jnp.zeros((per_dev, NFLD * CLEV), jnp.float32)
        .at[order]
        .set(returned.reshape(per_dev, NFLD * CLEV))
    )
    column_tend = placed.reshape(rows_dev, cols_dev, 4, NFLD * CLEV)
    return (state, column_tend, crm_new)


def solution(mesh):
    return jax.shard_map(
        per_device,
        mesh=mesh,
        in_specs=(
            P("face", "col", None, None),
            P("face", "col", None),
            P("face", "col", None),
            P(("face", "col")),
            P(None, None, None, ("face", "col")),
        ),
        out_specs=(
            P("face", "col", None, None),
            P("face", "col", None, None),
            P(None, None, None, ("face", "col")),
        ),
        check_vma=False,
    )
```

```python
import jax
import jax.numpy as jnp
import numpy as np
from jax import lax
from jax.experimental import pallas as pl
from jax.experimental.pallas import tpu as pltpu
from jax.sharding import PartitionSpec as P

NFLD = 10
LEV = 72
CLEV = 32
DSTEPS = 2
CSTEPS = 2


KAPPA = 0.1
ADVECT = 0.1
DIFF_X = 0.2
DIFF_Z = 0.1
RELAX = 0.2
CONVERT = 0.5
KEEP = 1.0 - 2.0 * DIFF_X - 2.0 * DIFF_Z


def extended_2(cells, sides, width):
    for axis, dim in sides:
        count = lax.axis_size(axis)
        head = lax.slice_in_dim(cells, 0, width, axis=dim)
        tail = lax.slice_in_dim(cells, cells.shape[dim] - width, cells.shape[dim], axis=dim)
        cells = jnp.concatenate(
            [
                lax.ppermute(tail, axis, [(i, (i + 1) % count) for i in range(count)]),
                cells,
                lax.ppermute(head, axis, [((i + 1) % count, i) for i in range(count)]),
            ],
            axis=dim,
        )
    return cells


def in_element_laplace(cells):
    point = np.arange(16)
    b_of = point % 4
    a_of = point // 4

    def shifted(step, valid):
        if step > 0:
            moved = jnp.concatenate([cells[:, :, step:], jnp.zeros_like(cells[:, :, :step])], axis=2)
        else:
            moved = jnp.concatenate([jnp.zeros_like(cells[:, :, step:]), cells[:, :, :step]], axis=2)
        mask = jnp.asarray(valid.astype(np.float32))[None, None, :, None]
        return moved * mask

    total = (
        shifted(1, b_of < 3)
        + shifted(-1, b_of > 0)
        + shifted(4, a_of < 3)
        + shifted(-4, a_of > 0)
    )
    degree = (b_of < 3).astype(np.float32) + (b_of > 0) + (a_of < 3) + (a_of > 0)
    return total - jnp.asarray(degree.astype(np.float32))[None, None, :, None] * cells


def node_tables():
    laplace = np.zeros((16, 16), np.float32)
    for row_a in range(4):
        for row_b in range(4):
            here = row_a * 4 + row_b
            for step_a, step_b in ((1, 0), (-1, 0), (0, 1), (0, -1)):
                near_a, near_b = (row_a + step_a, row_b + step_b)
                if 0 <= near_a < 4 and 0 <= near_b < 4:
                    laplace[here, near_a * 4 + near_b] += 1.0
                    laplace[here, here] -= 1.0
    edge_nodes = np.array([[0, 1, 2, 3], [3, 7, 11, 15], [12, 13, 14, 15], [0, 4, 8, 12]])
    spread = np.zeros((16, 16), np.float32)
    for edge in range(4):
        for point in range(4):
            spread[edge_nodes[edge, point], edge * 4 + point] = 1.0
    denom = 1.0 + spread.sum(axis=1)
    quarter = np.zeros((4, 16), np.float32)
    for row_a in range(4):
        for row_b in range(4):
            quarter[row_a // 2 * 2 + row_b // 2, row_a * 4 + row_b] = 0.25
    return (laplace, spread, denom, quarter)


def matched_points(links):
    other_edge = links // 2 % 4
    reversal = links % 2
    points = jnp.arange(4, dtype=jnp.int32)
    along = jnp.where(reversal[..., None] == 1, 3 - points, points)
    base = jnp.where(other_edge == 1, 3, jnp.where(other_edge == 2, 12, 0))
    stride = jnp.where((other_edge == 1) | (other_edge == 3), 4, 1)
    return base[..., None] + stride[..., None] * along


ZCHUNK = 4


def chunk_copies(src, dst, sems, count):
    def one(c):
        part = pl.ds(c * ZCHUNK, ZCHUNK)
        return pltpu.make_async_copy(src.at[:, part], dst.at[:, part], sems.at[c])

    return [one(c) for c in range(count)]


def neighbours(z, nlev):
    return jnp.minimum(z + 1, nlev - 1), jnp.maximum(z - 1, 0)


def crm_first_kernel(live_ref, state_hbm, part_hbm, mean_ref, held, wide, part, in_sem, out_sem):
    nfld, nlev, nx, _ = held.shape
    chunks = nlev // ZCHUNK
    loads = chunk_copies(state_hbm, held, in_sem, chunks)
    stores = chunk_copies(part, part_hbm, out_sem, chunks)
    for copy in loads:
        copy.start()
    live = live_ref[...] == 1

    def level(z, carry):
        upper_z, lower_z = neighbours(z, nlev)
        lead = ADVECT * wide[0, z]
        for f in range(nfld):
            state = wide[f, z]
            lower = wide[f, lower_z]
            upper = held[f, upper_z].astype(jnp.float32)
            wide[f, upper_z] = upper
            east = pltpu.roll(state, nx - 1, 0)
            west = pltpu.roll(state, 1, 0)
            mean_ref[f, pl.ds(z, 1)] = jnp.mean(state, axis=0, keepdims=True)
            fresh = KEEP * state + DIFF_X * (east + west) + DIFF_Z * (upper + lower) - lead * (east - west)
            part[f, z] = jnp.where(live, fresh, state)
        return carry

    for c in range(chunks):
        if c == 0:
            loads[0].wait()
            for f in range(nfld):
                wide[f, 0] = held[f, 0].astype(jnp.float32)
        if c + 1 < chunks:
            loads[c + 1].wait()
        lax.fori_loop(c * ZCHUNK, (c + 1) * ZCHUNK, level, 0)
        stores[c].start()
    for copy in stores:
        copy.wait()


def crm_second_kernel(force_ref, live_ref, mean_ref, part_hbm, new_hbm, tend_ref, mid, out, in_sem, out_sem):
    nfld, nlev, nx, _ = mid.shape
    chunks = nlev // ZCHUNK
    loads = chunk_copies(part_hbm, mid, in_sem, chunks)
    stores = chunk_copies(out, new_hbm, out_sem, chunks)
    for copy in loads:
        copy.start()
    live = live_ref[...] == 1

    def finish_first(z, carry):
        fresh = [
            mid[f, z]
            + jnp.where(live, RELAX * (force_ref[f, pl.ds(z, 1)] - mean_ref[f, pl.ds(z, 1)]), 0.0)
            for f in range(nfld)
        ]
        cond = CONVERT * jnp.maximum(fresh[3] - fresh[2], 0.0)
        fresh[3] = jnp.where(live, fresh[3] - cond, fresh[3])
        fresh[4] = jnp.where(live, fresh[4] + cond, fresh[4])
        for f in range(nfld):
            mid[f, z] = fresh[f]
        return carry

    def level(z, carry):
        upper_z, lower_z = neighbours(z, nlev)
        lead = ADVECT * mid[0, z]
        kept = {}

        def finish(f, fresh, state):
            new = jnp.where(live, fresh, state)
            out[f, z] = new.astype(out.dtype)
            tend_ref[f, pl.ds(z, 1)] = (jnp.mean(new, axis=0, keepdims=True) - mean_ref[f, pl.ds(z, 1)]) / CSTEPS

        for f in range(nfld):
            state = mid[f, z]
            upper = mid[f, upper_z]
            lower = mid[f, lower_z]
            east = pltpu.roll(state, nx - 1, 0)
            west = pltpu.roll(state, 1, 0)
            mean_x = jnp.mean(state, axis=0, keepdims=True)
            fresh = (
                KEEP * state
                + DIFF_X * (east + west)
                + DIFF_Z * (upper + lower)
                - lead * (east - west)
                + RELAX * (force_ref[f, pl.ds(z, 1)] - mean_x)
            )
            if f in (2, 3):
                kept[f] = (fresh, state)
                if f == 3:
                    cond = CONVERT * jnp.maximum(kept[3][0] - kept[2][0], 0.0)
                    finish(2, *kept[2])
                    finish(3, kept[3][0] - cond, kept[3][1])
                continue
            if f == 4:
                fresh = fresh + cond
            finish(f, fresh, state)
        return carry

    def ahead(z, carry):
        @pl.when(z + 1 < nlev)
        def _():
            finish_first(z + 1, 0)

        return level(z, carry)

    loads[0].wait()
    finish_first(0, 0)
    for c in range(chunks):
        if c + 1 < chunks:
            loads[c + 1].wait()
        lax.fori_loop(c * ZCHUNK, (c + 1) * ZCHUNK, ahead, 0)
        stores[c].start()
    for copy in stores:
        copy.wait()


def crm_first(state, active):
    nfld, nlev, nx, ncol = state.shape
    chunks = nlev // ZCHUNK
    return pl.pallas_call(
        crm_first_kernel,
        out_shape=(
            jax.ShapeDtypeStruct(state.shape, jnp.float32),
            jax.ShapeDtypeStruct((nfld, nlev, ncol), jnp.float32),
        ),
        in_specs=[pl.BlockSpec(memory_space=pltpu.VMEM), pl.BlockSpec(memory_space=pl.ANY)],
        out_specs=(pl.BlockSpec(memory_space=pl.ANY), pl.BlockSpec(memory_space=pltpu.VMEM)),
        scratch_shapes=[
            pltpu.VMEM(state.shape, jnp.bfloat16),
            pltpu.VMEM(state.shape, jnp.float32),
            pltpu.VMEM(state.shape, jnp.float32),
            pltpu.SemaphoreType.DMA((chunks,)),
            pltpu.SemaphoreType.DMA((chunks,)),
        ],
        compiler_params=pltpu.CompilerParams(vmem_limit_bytes=48 * 1024 * 1024),
    )(active.reshape(1, ncol), state)


def crm_second(part, start_mean, forcing, active):
    nfld, nlev, nx, ncol = part.shape
    chunks = nlev // ZCHUNK
    return pl.pallas_call(
        crm_second_kernel,
        out_shape=(
            jax.ShapeDtypeStruct(part.shape, jnp.bfloat16),
            jax.ShapeDtypeStruct((nfld, nlev, ncol), jnp.float32),
        ),
        in_specs=[
            pl.BlockSpec(memory_space=pltpu.VMEM),
            pl.BlockSpec(memory_space=pltpu.VMEM),
            pl.BlockSpec(memory_space=pltpu.VMEM),
            pl.BlockSpec(memory_space=pl.ANY),
        ],
        out_specs=(pl.BlockSpec(memory_space=pl.ANY), pl.BlockSpec(memory_space=pltpu.VMEM)),
        scratch_shapes=[
            pltpu.VMEM(part.shape, jnp.float32),
            pltpu.VMEM(part.shape, jnp.bfloat16),
            pltpu.SemaphoreType.DMA((chunks,)),
            pltpu.SemaphoreType.DMA((chunks,)),
        ],
        compiler_params=pltpu.CompilerParams(vmem_limit_bytes=48 * 1024 * 1024),
    )(forcing, active.reshape(1, ncol), start_mean, part)


def crm_run(state, forcing, active):
    part, start_mean = crm_first(state, active)
    return crm_second(part, start_mean, forcing, active)


TWO_STAGE = False


def exchange(chunks):
    if not TWO_STAGE:
        return lax.all_to_all(chunks, ("face", "col"), split_axis=0, concat_axis=0, tiled=True)
    nface = lax.axis_size("face")
    ncol = lax.axis_size("col")
    grid = chunks.reshape((nface, ncol) + chunks.shape[1:])
    grid = lax.all_to_all(grid, "col", split_axis=1, concat_axis=1, tiled=True)
    grid = lax.all_to_all(grid, "face", split_axis=0, concat_axis=0, tiled=True)
    return grid.reshape(chunks.shape)


def per_device(dyn_state, edge_links, phys_slot, crm_active, crm_state):
    laplace, spread, denom, quarter = [jnp.asarray(table) for table in node_tables()]
    rows_dev, cols_dev, nodes, width = dyn_state.shape
    nface = lax.axis_size("face")
    ncol = lax.axis_size("col")
    ndev = nface * ncol
    total_rows = rows_dev * nface
    total_cols = cols_dev * ncol
    neighbour = edge_links // 8
    pick = matched_points(edge_links)
    near_row = neighbour // total_cols
    near_col = neighbour % total_cols
    local_row = lax.broadcasted_iota(jnp.int32, (rows_dev, cols_dev, 4), 0)
    local_col = lax.broadcasted_iota(jnp.int32, (rows_dev, cols_dev, 4), 1)
    drow = (near_row - (lax.axis_index("face") * rows_dev + local_row) + 1) % total_rows - 1
    dcol = (near_col - (lax.axis_index("col") * cols_dev + local_col) + 1) % total_cols - 1
    place = (local_row + drow + 1) * (cols_dev + 2) + (local_col + dcol + 1)
    index_flat = place[..., None] * 16 + pick
    index_flat = index_flat.reshape(-1)
    part, start_mean = crm_first(crm_state, crm_active)
    state = dyn_state
    for step in range(DSTEPS):
        state = state + KAPPA * in_element_laplace(state)
        if step == 0:
            faced = extended_2(state, (("face", 0),), 1)
            faced, part, start_mean = lax.optimization_barrier((faced, part, start_mean))
            extended = extended_2(faced, (("col", 1),), 1)
        else:
            extended = extended_2(state, (("face", 0), ("col", 1)), 1)
        matched = jnp.take(extended.reshape(-1, width), index_flat, axis=0, mode="clip").reshape(
            rows_dev, cols_dev, 16, width
        )
        summed = jnp.einsum("nm,rcmw->rcnw", spread, matched, precision=lax.Precision.HIGHEST)
        state = (state + summed) / denom[None, None, :, None]
    columns = jnp.einsum("qn,rcnw->rcqw", quarter, state, precision=lax.Precision.HIGHEST).reshape(
        -1, NFLD, LEV
    )[:, :, :CLEV].reshape(-1, NFLD * CLEV)
    per_dev = columns.shape[0]
    count = per_dev // ndev
    keys_local = phys_slot.reshape(-1)
    order = jnp.argsort(keys_local, stable=True)
    out_keys = keys_local[order]
    outgoing = jnp.concatenate(
        [columns[order], out_keys.astype(jnp.float32)[:, None]], axis=1
    )
    arrived = exchange(outgoing.reshape(ndev, count, NFLD * CLEV + 1)).reshape(per_dev, -1)
    slots = arrived[:, NFLD * CLEV].astype(jnp.int32) % per_dev
    physics = jnp.zeros((per_dev, NFLD * CLEV), jnp.float32).at[slots].set(arrived[:, : NFLD * CLEV])
    forcing = physics.reshape(per_dev, NFLD, CLEV).transpose(1, 2, 0)
    crm_new, tend = crm_second(part, start_mean, forcing, crm_active)
    tend_rows = tend.reshape(NFLD * CLEV, per_dev).T[slots]
    returned = exchange(tend_rows.reshape(ndev, count, NFLD * CLEV))
    placed = (
        jnp.zeros((per_dev, NFLD * CLEV), jnp.float32)
        .at[order]
        .set(returned.reshape(per_dev, NFLD * CLEV))
    )
    column_tend = placed.reshape(rows_dev, cols_dev, 4, NFLD * CLEV)
    return (state, column_tend, crm_new)


def solution(mesh):
    return jax.shard_map(
        per_device,
        mesh=mesh,
        in_specs=(
            P("face", "col", None, None),
            P("face", "col", None),
            P("face", "col", None),
            P(("face", "col")),
            P(None, None, None, ("face", "col")),
        ),
        out_specs=(
            P("face", "col", None, None),
            P("face", "col", None, None),
            P(None, None, None, ("face", "col")),
        ),
        check_vma=False,
    )
```

```python
import jax
import jax.numpy as jnp
import numpy as np
from jax import lax
from jax.experimental import pallas as pl
from jax.experimental.pallas import tpu as pltpu
from jax.sharding import PartitionSpec as P

NFLD = 10
LEV = 72
CLEV = 32
DSTEPS = 2
CSTEPS = 2


KAPPA = 0.1
ADVECT = 0.1
DIFF_X = 0.2
DIFF_Z = 0.1
RELAX = 0.2
CONVERT = 0.5
KEEP = 1.0 - 2.0 * DIFF_X - 2.0 * DIFF_Z


def extended_2(cells, sides, width):
    for axis, dim in sides:
        count = lax.axis_size(axis)
        head = lax.slice_in_dim(cells, 0, width, axis=dim)
        tail = lax.slice_in_dim(cells, cells.shape[dim] - width, cells.shape[dim], axis=dim)
        cells = jnp.concatenate(
            [
                lax.ppermute(tail, axis, [(i, (i + 1) % count) for i in range(count)]),
                cells,
                lax.ppermute(head, axis, [((i + 1) % count, i) for i in range(count)]),
            ],
            axis=dim,
        )
    return cells


def node_tables():
    laplace = np.zeros((16, 16), np.float32)
    for row_a in range(4):
        for row_b in range(4):
            here = row_a * 4 + row_b
            for step_a, step_b in ((1, 0), (-1, 0), (0, 1), (0, -1)):
                near_a, near_b = (row_a + step_a, row_b + step_b)
                if 0 <= near_a < 4 and 0 <= near_b < 4:
                    laplace[here, near_a * 4 + near_b] += 1.0
                    laplace[here, here] -= 1.0
    edge_nodes = np.array([[0, 1, 2, 3], [3, 7, 11, 15], [12, 13, 14, 15], [0, 4, 8, 12]])
    spread = np.zeros((16, 16), np.float32)
    for edge in range(4):
        for point in range(4):
            spread[edge_nodes[edge, point], edge * 4 + point] = 1.0
    denom = 1.0 + spread.sum(axis=1)
    quarter = np.zeros((4, 16), np.float32)
    for row_a in range(4):
        for row_b in range(4):
            quarter[row_a // 2 * 2 + row_b // 2, row_a * 4 + row_b] = 0.25
    return (laplace, spread, denom, quarter)


def matched_points(links):
    other_edge = links // 2 % 4
    reversal = links % 2
    points = jnp.arange(4, dtype=jnp.int32)
    along = jnp.where(reversal[..., None] == 1, 3 - points, points)
    base = jnp.where(other_edge == 1, 3, jnp.where(other_edge == 2, 12, 0))
    stride = jnp.where((other_edge == 1) | (other_edge == 3), 4, 1)
    return base[..., None] + stride[..., None] * along


ZCHUNK = 4


def chunk_copies(src, dst, sems, count):
    def one(c):
        part = pl.ds(c * ZCHUNK, ZCHUNK)
        return pltpu.make_async_copy(src.at[:, part], dst.at[:, part], sems.at[c])

    return [one(c) for c in range(count)]


def neighbours(z, nlev):
    return jnp.minimum(z + 1, nlev - 1), jnp.maximum(z - 1, 0)


def crm_first_kernel(live_ref, state_hbm, part_hbm, mean_ref, held, wide, part, in_sem, out_sem):
    nfld, nlev, nx, _ = held.shape
    chunks = nlev // ZCHUNK
    loads = chunk_copies(state_hbm, held, in_sem, chunks)
    stores = chunk_copies(part, part_hbm, out_sem, chunks)
    for copy in loads:
        copy.start()
    live = live_ref[...] == 1

    def level(z, carry):
        upper_z, lower_z = neighbours(z, nlev)
        lead = ADVECT * wide[0, z]
        for f in range(nfld):
            state = wide[f, z]
            lower = wide[f, lower_z]
            upper = held[f, upper_z].astype(jnp.float32)
            wide[f, upper_z] = upper
            east = pltpu.roll(state, nx - 1, 0)
            west = pltpu.roll(state, 1, 0)
            mean_ref[f, pl.ds(z, 1)] = jnp.mean(state, axis=0, keepdims=True)
            fresh = KEEP * state + DIFF_X * (east + west) + DIFF_Z * (upper + lower) - lead * (east - west)
            part[f, z] = jnp.where(live, fresh, state)
        return carry

    for c in range(chunks):
        if c == 0:
            loads[0].wait()
            for f in range(nfld):
                wide[f, 0] = held[f, 0].astype(jnp.float32)
        if c + 1 < chunks:
            loads[c + 1].wait()
        lax.fori_loop(c * ZCHUNK, (c + 1) * ZCHUNK, level, 0)
        stores[c].start()
    for copy in stores:
        copy.wait()


def crm_second_kernel(force_ref, live_ref, mean_ref, part_hbm, new_hbm, tend_ref, mid, out, in_sem, out_sem):
    nfld, nlev, nx, _ = mid.shape
    chunks = nlev // ZCHUNK
    loads = chunk_copies(part_hbm, mid, in_sem, chunks)
    stores = chunk_copies(out, new_hbm, out_sem, chunks)
    for copy in loads:
        copy.start()
    live = live_ref[...] == 1

    def finish_first(z, carry):
        fresh = [
            mid[f, z]
            + jnp.where(live, RELAX * (force_ref[f, pl.ds(z, 1)] - mean_ref[f, pl.ds(z, 1)]), 0.0)
            for f in range(nfld)
        ]
        cond = CONVERT * jnp.maximum(fresh[3] - fresh[2], 0.0)
        fresh[3] = jnp.where(live, fresh[3] - cond, fresh[3])
        fresh[4] = jnp.where(live, fresh[4] + cond, fresh[4])
        for f in range(nfld):
            mid[f, z] = fresh[f]
        return carry

    def level(z, carry):
        upper_z, lower_z = neighbours(z, nlev)
        lead = ADVECT * mid[0, z]
        kept = {}

        def finish(f, fresh, state):
            new = jnp.where(live, fresh, state)
            out[f, z] = new.astype(out.dtype)
            tend_ref[f, pl.ds(z, 1)] = (jnp.mean(new, axis=0, keepdims=True) - mean_ref[f, pl.ds(z, 1)]) / CSTEPS

        for f in range(nfld):
            state = mid[f, z]
            upper = mid[f, upper_z]
            lower = mid[f, lower_z]
            east = pltpu.roll(state, nx - 1, 0)
            west = pltpu.roll(state, 1, 0)
            mean_x = jnp.mean(state, axis=0, keepdims=True)
            fresh = (
                KEEP * state
                + DIFF_X * (east + west)
                + DIFF_Z * (upper + lower)
                - lead * (east - west)
                + RELAX * (force_ref[f, pl.ds(z, 1)] - mean_x)
            )
            if f in (2, 3):
                kept[f] = (fresh, state)
                if f == 3:
                    cond = CONVERT * jnp.maximum(kept[3][0] - kept[2][0], 0.0)
                    finish(2, *kept[2])
                    finish(3, kept[3][0] - cond, kept[3][1])
                continue
            if f == 4:
                fresh = fresh + cond
            finish(f, fresh, state)
        return carry

    def ahead(z, carry):
        @pl.when(z + 1 < nlev)
        def _():
            finish_first(z + 1, 0)

        return level(z, carry)

    loads[0].wait()
    finish_first(0, 0)
    for c in range(chunks):
        if c + 1 < chunks:
            loads[c + 1].wait()
        lax.fori_loop(c * ZCHUNK, (c + 1) * ZCHUNK, ahead, 0)
        stores[c].start()
    for copy in stores:
        copy.wait()


def crm_first(state, active):
    nfld, nlev, nx, ncol = state.shape
    chunks = nlev // ZCHUNK
    return pl.pallas_call(
        crm_first_kernel,
        out_shape=(
            jax.ShapeDtypeStruct(state.shape, jnp.float32),
            jax.ShapeDtypeStruct((nfld, nlev, ncol), jnp.float32),
        ),
        in_specs=[pl.BlockSpec(memory_space=pltpu.VMEM), pl.BlockSpec(memory_space=pl.ANY)],
        out_specs=(pl.BlockSpec(memory_space=pl.ANY), pl.BlockSpec(memory_space=pltpu.VMEM)),
        scratch_shapes=[
            pltpu.VMEM(state.shape, jnp.bfloat16),
            pltpu.VMEM(state.shape, jnp.float32),
            pltpu.VMEM(state.shape, jnp.float32),
            pltpu.SemaphoreType.DMA((chunks,)),
            pltpu.SemaphoreType.DMA((chunks,)),
        ],
        compiler_params=pltpu.CompilerParams(vmem_limit_bytes=48 * 1024 * 1024),
    )(active.reshape(1, ncol), state)


def crm_second(part, start_mean, forcing, active):
    nfld, nlev, nx, ncol = part.shape
    chunks = nlev // ZCHUNK
    return pl.pallas_call(
        crm_second_kernel,
        out_shape=(
            jax.ShapeDtypeStruct(part.shape, jnp.bfloat16),
            jax.ShapeDtypeStruct((nfld, nlev, ncol), jnp.float32),
        ),
        in_specs=[
            pl.BlockSpec(memory_space=pltpu.VMEM),
            pl.BlockSpec(memory_space=pltpu.VMEM),
            pl.BlockSpec(memory_space=pltpu.VMEM),
            pl.BlockSpec(memory_space=pl.ANY),
        ],
        out_specs=(pl.BlockSpec(memory_space=pl.ANY), pl.BlockSpec(memory_space=pltpu.VMEM)),
        scratch_shapes=[
            pltpu.VMEM(part.shape, jnp.float32),
            pltpu.VMEM(part.shape, jnp.bfloat16),
            pltpu.SemaphoreType.DMA((chunks,)),
            pltpu.SemaphoreType.DMA((chunks,)),
        ],
        compiler_params=pltpu.CompilerParams(vmem_limit_bytes=48 * 1024 * 1024),
    )(forcing, active.reshape(1, ncol), start_mean, part)


def crm_run(state, forcing, active):
    part, start_mean = crm_first(state, active)
    return crm_second(part, start_mean, forcing, active)


TWO_STAGE = False


def exchange(chunks):
    if not TWO_STAGE:
        return lax.all_to_all(chunks, ("face", "col"), split_axis=0, concat_axis=0, tiled=True)
    nface = lax.axis_size("face")
    ncol = lax.axis_size("col")
    grid = chunks.reshape((nface, ncol) + chunks.shape[1:])
    grid = lax.all_to_all(grid, "col", split_axis=1, concat_axis=1, tiled=True)
    grid = lax.all_to_all(grid, "face", split_axis=0, concat_axis=0, tiled=True)
    return grid.reshape(chunks.shape)


def per_device(dyn_state, edge_links, phys_slot, crm_active, crm_state):
    laplace, spread, denom, quarter = [jnp.asarray(table) for table in node_tables()]
    rows_dev, cols_dev, nodes, width = dyn_state.shape
    nface = lax.axis_size("face")
    ncol = lax.axis_size("col")
    ndev = nface * ncol
    total_rows = rows_dev * nface
    total_cols = cols_dev * ncol
    neighbour = edge_links // 8
    pick = matched_points(edge_links)
    near_row = neighbour // total_cols
    near_col = neighbour % total_cols
    local_row = lax.broadcasted_iota(jnp.int32, (rows_dev, cols_dev, 4), 0)
    local_col = lax.broadcasted_iota(jnp.int32, (rows_dev, cols_dev, 4), 1)
    drow = (near_row - (lax.axis_index("face") * rows_dev + local_row) + 1) % total_rows - 1
    dcol = (near_col - (lax.axis_index("col") * cols_dev + local_col) + 1) % total_cols - 1
    place = (local_row + drow + 1) * (cols_dev + 2) + (local_col + dcol + 1)
    index_flat = place[..., None] * 16 + pick
    index_flat = index_flat.reshape(-1)
    part, start_mean = crm_first(crm_state, crm_active)
    state = dyn_state
    for step in range(DSTEPS):
        state = state + KAPPA * jnp.einsum(
            "nm,rcmw->rcnw", laplace, state, precision=lax.Precision.HIGHEST
        )
        if step == 0:
            faced = extended_2(state, (("face", 0),), 1)
            faced, part, start_mean = lax.optimization_barrier((faced, part, start_mean))
            extended = extended_2(faced, (("col", 1),), 1)
        else:
            extended = extended_2(state, (("face", 0), ("col", 1)), 1)
        matched = jnp.take(extended.reshape(-1, width), index_flat, axis=0).reshape(
            rows_dev, cols_dev, 16, width
        )
        summed = jnp.einsum("nm,rcmw->rcnw", spread, matched, precision=lax.Precision.HIGHEST)
        state = (state + summed) / denom[None, None, :, None]
    columns = jnp.einsum("qn,rcnw->rcqw", quarter, state, precision=lax.Precision.HIGHEST).reshape(
        -1, NFLD, LEV
    )[:, :, :CLEV].reshape(-1, NFLD * CLEV)
    per_dev = columns.shape[0]
    count = per_dev // ndev
    keys_local = phys_slot.reshape(-1)
    order = jnp.argsort(keys_local, stable=True)
    out_keys = keys_local[order]
    outgoing = jnp.concatenate(
        [columns[order], out_keys.astype(jnp.float32)[:, None]], axis=1
    )
    arrived = exchange(outgoing.reshape(ndev, count, NFLD * CLEV + 1)).reshape(per_dev, -1)
    slots = arrived[:, NFLD * CLEV].astype(jnp.int32) % per_dev
    physics = jnp.zeros((per_dev, NFLD * CLEV), jnp.float32).at[slots].set(arrived[:, : NFLD * CLEV])
    forcing = physics.reshape(per_dev, NFLD, CLEV).transpose(1, 2, 0)
    crm_new, tend = crm_second(part, start_mean, forcing, crm_active)
    tend_rows = tend.reshape(NFLD * CLEV, per_dev).T[slots]
    returned = exchange(tend_rows.reshape(ndev, count, NFLD * CLEV))
    rank = jnp.zeros((per_dev,), jnp.int32).at[order].set(jnp.arange(per_dev, dtype=jnp.int32))
    column_tend = returned.reshape(per_dev, NFLD * CLEV)[rank.reshape(rows_dev, cols_dev, 4)]
    return (state, column_tend, crm_new)


def solution(mesh):
    return jax.shard_map(
        per_device,
        mesh=mesh,
        in_specs=(
            P("face", "col", None, None),
            P("face", "col", None),
            P("face", "col", None),
            P(("face", "col")),
            P(None, None, None, ("face", "col")),
        ),
        out_specs=(
            P("face", "col", None, None),
            P("face", "col", None, None),
            P(None, None, None, ("face", "col")),
        ),
        check_vma=False,
    )
```

```python
import functools

import jax
import jax.numpy as jnp
import numpy as np
from jax import lax
from jax.experimental import pallas as pl
from jax.experimental.pallas import tpu as pltpu
from jax.sharding import PartitionSpec as P

NFLD = 10
LEV = 72
CLEV = 32
DSTEPS = 2
CSTEPS = 2


KAPPA = 0.1
ADVECT = 0.1
DIFF_X = 0.2
DIFF_Z = 0.1
RELAX = 0.2
CONVERT = 0.5
KEEP = 1.0 - 2.0 * DIFF_X - 2.0 * DIFF_Z


def extended_2(cells, sides, width):
    for axis, dim in sides:
        count = lax.axis_size(axis)
        head = lax.slice_in_dim(cells, 0, width, axis=dim)
        tail = lax.slice_in_dim(cells, cells.shape[dim] - width, cells.shape[dim], axis=dim)
        cells = jnp.concatenate(
            [
                lax.ppermute(tail, axis, [(i, (i + 1) % count) for i in range(count)]),
                cells,
                lax.ppermute(head, axis, [((i + 1) % count, i) for i in range(count)]),
            ],
            axis=dim,
        )
    return cells


def node_tables():
    laplace = np.zeros((16, 16), np.float32)
    for row_a in range(4):
        for row_b in range(4):
            here = row_a * 4 + row_b
            for step_a, step_b in ((1, 0), (-1, 0), (0, 1), (0, -1)):
                near_a, near_b = (row_a + step_a, row_b + step_b)
                if 0 <= near_a < 4 and 0 <= near_b < 4:
                    laplace[here, near_a * 4 + near_b] += 1.0
                    laplace[here, here] -= 1.0
    edge_nodes = np.array([[0, 1, 2, 3], [3, 7, 11, 15], [12, 13, 14, 15], [0, 4, 8, 12]])
    spread = np.zeros((16, 16), np.float32)
    for edge in range(4):
        for point in range(4):
            spread[edge_nodes[edge, point], edge * 4 + point] = 1.0
    denom = 1.0 + spread.sum(axis=1)
    quarter = np.zeros((4, 16), np.float32)
    for row_a in range(4):
        for row_b in range(4):
            quarter[row_a // 2 * 2 + row_b // 2, row_a * 4 + row_b] = 0.25
    return (laplace, spread, denom, quarter)


def matched_points(links):
    other_edge = links // 2 % 4
    reversal = links % 2
    points = jnp.arange(4, dtype=jnp.int32)
    along = jnp.where(reversal[..., None] == 1, 3 - points, points)
    base = jnp.where(other_edge == 1, 3, jnp.where(other_edge == 2, 12, 0))
    stride = jnp.where((other_edge == 1) | (other_edge == 3), 4, 1)
    return base[..., None] + stride[..., None] * along


ZCHUNK = 4


def chunk_copies(src, dst, sems, count):
    def one(c):
        part = pl.ds(c * ZCHUNK, ZCHUNK)
        return pltpu.make_async_copy(src.at[:, part], dst.at[:, part], sems.at[c])

    return [one(c) for c in range(count)]


def neighbours(z, nlev):
    return jnp.minimum(z + 1, nlev - 1), jnp.maximum(z - 1, 0)


def crm_first_kernel(first, last, live_ref, state_hbm, part_hbm, mean_ref, held, wide, part, in_sem, out_sem):
    nfld, nlev, nx, _ = held.shape
    lo_chunk = max(first - 1, 0) // ZCHUNK
    hi_chunk = (min(last + 1, nlev) + ZCHUNK - 1) // ZCHUNK
    loads = {
        c: pltpu.make_async_copy(
            state_hbm.at[:, pl.ds(c * ZCHUNK, ZCHUNK)], held.at[:, pl.ds(c * ZCHUNK, ZCHUNK)], in_sem.at[c]
        )
        for c in range(lo_chunk, hi_chunk)
    }
    own = (last - first) // ZCHUNK

    def store(c):
        return pltpu.make_async_copy(
            part.at[:, pl.ds(c * ZCHUNK, ZCHUNK)], part_hbm.at[:, pl.ds(c * ZCHUNK, ZCHUNK)], out_sem.at[c]
        )

    stores = [store(c) for c in range(own)]
    for c in range(lo_chunk, hi_chunk):
        loads[c].start()
    live = live_ref[...] == 1

    def level(z, carry):
        upper_z, lower_z = neighbours(z, nlev)
        lead = ADVECT * wide[0, z]
        for f in range(nfld):
            state = wide[f, z]
            lower = wide[f, lower_z]
            upper = held[f, upper_z].astype(jnp.float32)
            wide[f, upper_z] = upper
            east = pltpu.roll(state, nx - 1, 0)
            west = pltpu.roll(state, 1, 0)
            mean_ref[f, pl.ds(z - first, 1)] = jnp.mean(state, axis=0, keepdims=True)
            fresh = KEEP * state + DIFF_X * (east + west) + DIFF_Z * (upper + lower) - lead * (east - west)
            part[f, z - first] = jnp.where(live, fresh, state)
        return carry

    waited = set()

    def need(c):
        if c < hi_chunk and c not in waited:
            loads[c].wait()
            waited.add(c)

    for c in range(own):
        base = first + c * ZCHUNK
        if c == 0:
            need(max(first - 1, 0) // ZCHUNK)
            need(first // ZCHUNK)
            for f in range(nfld):
                for z in sorted({max(first - 1, 0), first}):
                    wide[f, z] = held[f, z].astype(jnp.float32)
        need((base + ZCHUNK) // ZCHUNK)
        lax.fori_loop(base, base + ZCHUNK, level, 0)
        stores[c].start()
    for c in range(lo_chunk, hi_chunk):
        need(c)
    for copy in stores:
        copy.wait()


def crm_second_kernel(force_ref, live_ref, mean_ref, low_hbm, high_hbm, new_hbm, tend_ref, mid, out, in_sem, out_sem):
    nfld, nlev, nx, _ = mid.shape
    chunks = nlev // ZCHUNK
    half = low_hbm.shape[1] // ZCHUNK

    def load(c):
        src_ref, at = (low_hbm, c) if c < half else (high_hbm, c - half)
        return pltpu.make_async_copy(
            src_ref.at[:, pl.ds(at * ZCHUNK, ZCHUNK)], mid.at[:, pl.ds(c * ZCHUNK, ZCHUNK)], in_sem.at[c]
        )

    loads = [load(c) for c in range(chunks)]
    stores = chunk_copies(out, new_hbm, out_sem, chunks)
    for copy in loads:
        copy.start()
    live = live_ref[...] == 1

    def finish_first(z, carry):
        fresh = [
            mid[f, z]
            + jnp.where(live, RELAX * (force_ref[f, pl.ds(z, 1)] - mean_ref[f, pl.ds(z, 1)]), 0.0)
            for f in range(nfld)
        ]
        cond = CONVERT * jnp.maximum(fresh[3] - fresh[2], 0.0)
        fresh[3] = jnp.where(live, fresh[3] - cond, fresh[3])
        fresh[4] = jnp.where(live, fresh[4] + cond, fresh[4])
        for f in range(nfld):
            mid[f, z] = fresh[f]
        return carry

    def level(z, carry):
        upper_z, lower_z = neighbours(z, nlev)
        lead = ADVECT * mid[0, z]
        kept = {}

        def finish(f, fresh, state):
            new = jnp.where(live, fresh, state)
            out[f, z] = new.astype(out.dtype)
            tend_ref[f, pl.ds(z, 1)] = (jnp.mean(new, axis=0, keepdims=True) - mean_ref[f, pl.ds(z, 1)]) / CSTEPS

        for f in range(nfld):
            state = mid[f, z]
            upper = mid[f, upper_z]
            lower = mid[f, lower_z]
            east = pltpu.roll(state, nx - 1, 0)
            west = pltpu.roll(state, 1, 0)
            mean_x = jnp.mean(state, axis=0, keepdims=True)
            fresh = (
                KEEP * state
                + DIFF_X * (east + west)
                + DIFF_Z * (upper + lower)
                - lead * (east - west)
                + RELAX * (force_ref[f, pl.ds(z, 1)] - mean_x)
            )
            if f in (2, 3):
                kept[f] = (fresh, state)
                if f == 3:
                    cond = CONVERT * jnp.maximum(kept[3][0] - kept[2][0], 0.0)
                    finish(2, *kept[2])
                    finish(3, kept[3][0] - cond, kept[3][1])
                continue
            if f == 4:
                fresh = fresh + cond
            finish(f, fresh, state)
        return carry

    def ahead(z, carry):
        @pl.when(z + 1 < nlev)
        def _():
            finish_first(z + 1, 0)

        return level(z, carry)

    loads[0].wait()
    finish_first(0, 0)
    for c in range(chunks):
        if c + 1 < chunks:
            loads[c + 1].wait()
        lax.fori_loop(c * ZCHUNK, (c + 1) * ZCHUNK, ahead, 0)
        stores[c].start()
    for copy in stores:
        copy.wait()


def crm_first(state, active, first, last):
    nfld, nlev, nx, ncol = state.shape
    chunks = nlev // ZCHUNK
    span = (nfld, last - first, nx, ncol)
    return pl.pallas_call(
        functools.partial(crm_first_kernel, first, last),
        out_shape=(
            jax.ShapeDtypeStruct(span, jnp.float32),
            jax.ShapeDtypeStruct((nfld, last - first, ncol), jnp.float32),
        ),
        in_specs=[pl.BlockSpec(memory_space=pltpu.VMEM), pl.BlockSpec(memory_space=pl.ANY)],
        out_specs=(pl.BlockSpec(memory_space=pl.ANY), pl.BlockSpec(memory_space=pltpu.VMEM)),
        scratch_shapes=[
            pltpu.VMEM(state.shape, jnp.bfloat16),
            pltpu.VMEM(state.shape, jnp.float32),
            pltpu.VMEM(span, jnp.float32),
            pltpu.SemaphoreType.DMA((chunks,)),
            pltpu.SemaphoreType.DMA((chunks,)),
        ],
        compiler_params=pltpu.CompilerParams(vmem_limit_bytes=48 * 1024 * 1024),
    )(active.reshape(1, ncol), state)


def crm_second(low, high, start_mean, forcing, active):
    nfld, nlev, ncol = start_mean.shape
    nx = low.shape[2]
    chunks = nlev // ZCHUNK
    shape = (nfld, nlev, nx, ncol)
    return pl.pallas_call(
        crm_second_kernel,
        out_shape=(
            jax.ShapeDtypeStruct(shape, jnp.bfloat16),
            jax.ShapeDtypeStruct((nfld, nlev, ncol), jnp.float32),
        ),
        in_specs=[
            pl.BlockSpec(memory_space=pltpu.VMEM),
            pl.BlockSpec(memory_space=pltpu.VMEM),
            pl.BlockSpec(memory_space=pltpu.VMEM),
            pl.BlockSpec(memory_space=pl.ANY),
            pl.BlockSpec(memory_space=pl.ANY),
        ],
        out_specs=(pl.BlockSpec(memory_space=pl.ANY), pl.BlockSpec(memory_space=pltpu.VMEM)),
        scratch_shapes=[
            pltpu.VMEM(shape, jnp.float32),
            pltpu.VMEM(shape, jnp.bfloat16),
            pltpu.SemaphoreType.DMA((chunks,)),
            pltpu.SemaphoreType.DMA((chunks,)),
        ],
        compiler_params=pltpu.CompilerParams(vmem_limit_bytes=48 * 1024 * 1024),
    )(forcing, active.reshape(1, ncol), start_mean, low, high)


TWO_STAGE = False


def exchange(chunks):
    if not TWO_STAGE:
        return lax.all_to_all(chunks, ("face", "col"), split_axis=0, concat_axis=0, tiled=True)
    nface = lax.axis_size("face")
    ncol = lax.axis_size("col")
    grid = chunks.reshape((nface, ncol) + chunks.shape[1:])
    grid = lax.all_to_all(grid, "col", split_axis=1, concat_axis=1, tiled=True)
    grid = lax.all_to_all(grid, "face", split_axis=0, concat_axis=0, tiled=True)
    return grid.reshape(chunks.shape)


def per_device(dyn_state, edge_links, phys_slot, crm_active, crm_state):
    laplace, spread, denom, quarter = [jnp.asarray(table) for table in node_tables()]
    rows_dev, cols_dev, nodes, width = dyn_state.shape
    nface = lax.axis_size("face")
    ncol = lax.axis_size("col")
    ndev = nface * ncol
    total_rows = rows_dev * nface
    total_cols = cols_dev * ncol
    neighbour = edge_links // 8
    pick = matched_points(edge_links)
    near_row = neighbour // total_cols
    near_col = neighbour % total_cols
    local_row = lax.broadcasted_iota(jnp.int32, (rows_dev, cols_dev, 4), 0)
    local_col = lax.broadcasted_iota(jnp.int32, (rows_dev, cols_dev, 4), 1)
    drow = (near_row - (lax.axis_index("face") * rows_dev + local_row) + 1) % total_rows - 1
    dcol = (near_col - (lax.axis_index("col") * cols_dev + local_col) + 1) % total_cols - 1
    place = (local_row + drow + 1) * (cols_dev + 2) + (local_col + dcol + 1)
    index_flat = place[..., None] * 16 + pick
    index_flat = index_flat.reshape(-1)
    split = crm_state.shape[1] // 2
    low, low_mean = crm_first(crm_state, crm_active, 0, split)
    high, high_mean = crm_first(crm_state, crm_active, split, crm_state.shape[1])
    state = dyn_state
    for step in range(DSTEPS):
        state = state + KAPPA * jnp.einsum(
            "nm,rcmw->rcnw", laplace, state, precision=lax.Precision.HIGHEST
        )
        faced = extended_2(state, (("face", 0),), 1)
        if step == 0:
            faced, low, low_mean = lax.optimization_barrier((faced, low, low_mean))
        else:
            faced, high, high_mean = lax.optimization_barrier((faced, high, high_mean))
        extended = extended_2(faced, (("col", 1),), 1)
        matched = jnp.take(extended.reshape(-1, width), index_flat, axis=0).reshape(
            rows_dev, cols_dev, 16, width
        )
        summed = jnp.einsum("nm,rcmw->rcnw", spread, matched, precision=lax.Precision.HIGHEST)
        state = (state + summed) / denom[None, None, :, None]
    columns = jnp.einsum("qn,rcnw->rcqw", quarter, state, precision=lax.Precision.HIGHEST).reshape(
        -1, NFLD, LEV
    )[:, :, :CLEV].reshape(-1, NFLD * CLEV)
    per_dev = columns.shape[0]
    count = per_dev // ndev
    keys_local = phys_slot.reshape(-1)
    order = jnp.argsort(keys_local, stable=True)
    out_keys = keys_local[order]
    outgoing = jnp.concatenate(
        [columns[order], out_keys.astype(jnp.float32)[:, None]], axis=1
    )
    arrived = exchange(outgoing.reshape(ndev, count, NFLD * CLEV + 1)).reshape(per_dev, -1)
    slots = arrived[:, NFLD * CLEV].astype(jnp.int32) % per_dev
    physics = jnp.zeros((per_dev, NFLD * CLEV), jnp.float32).at[slots].set(arrived[:, : NFLD * CLEV])
    forcing = physics.reshape(per_dev, NFLD, CLEV).transpose(1, 2, 0)
    start_mean = jnp.concatenate([low_mean, high_mean], axis=1)
    crm_new, tend = crm_second(low, high, start_mean, forcing, crm_active)
    tend_rows = tend.reshape(NFLD * CLEV, per_dev).T[slots]
    returned = exchange(tend_rows.reshape(ndev, count, NFLD * CLEV))
    placed = (
        jnp.zeros((per_dev, NFLD * CLEV), jnp.float32)
        .at[order]
        .set(returned.reshape(per_dev, NFLD * CLEV))
    )
    column_tend = placed.reshape(rows_dev, cols_dev, 4, NFLD * CLEV)
    return (state, column_tend, crm_new)


def solution(mesh):
    return jax.shard_map(
        per_device,
        mesh=mesh,
        in_specs=(
            P("face", "col", None, None),
            P("face", "col", None),
            P("face", "col", None),
            P(("face", "col")),
            P(None, None, None, ("face", "col")),
        ),
        out_specs=(
            P("face", "col", None, None),
            P("face", "col", None, None),
            P(None, None, None, ("face", "col")),
        ),
        check_vma=False,
    )
```

```python
import jax
import jax.numpy as jnp
import numpy as np
from jax import lax
from jax.experimental import pallas as pl
from jax.experimental.pallas import tpu as pltpu
from jax.sharding import PartitionSpec as P

NFLD = 10
LEV = 72
CLEV = 32
DSTEPS = 2
CSTEPS = 2


KAPPA = 0.1
ADVECT = 0.1
DIFF_X = 0.2
DIFF_Z = 0.1
RELAX = 0.2
CONVERT = 0.5
KEEP = 1.0 - 2.0 * DIFF_X - 2.0 * DIFF_Z


def extended_2(cells, sides, width):
    for axis, dim in sides:
        count = lax.axis_size(axis)
        head = lax.slice_in_dim(cells, 0, width, axis=dim)
        tail = lax.slice_in_dim(cells, cells.shape[dim] - width, cells.shape[dim], axis=dim)
        cells = jnp.concatenate(
            [
                lax.ppermute(tail, axis, [(i, (i + 1) % count) for i in range(count)]),
                cells,
                lax.ppermute(head, axis, [((i + 1) % count, i) for i in range(count)]),
            ],
            axis=dim,
        )
    return cells


def node_tables():
    laplace = np.zeros((16, 16), np.float32)
    for row_a in range(4):
        for row_b in range(4):
            here = row_a * 4 + row_b
            for step_a, step_b in ((1, 0), (-1, 0), (0, 1), (0, -1)):
                near_a, near_b = (row_a + step_a, row_b + step_b)
                if 0 <= near_a < 4 and 0 <= near_b < 4:
                    laplace[here, near_a * 4 + near_b] += 1.0
                    laplace[here, here] -= 1.0
    edge_nodes = np.array([[0, 1, 2, 3], [3, 7, 11, 15], [12, 13, 14, 15], [0, 4, 8, 12]])
    spread = np.zeros((16, 16), np.float32)
    for edge in range(4):
        for point in range(4):
            spread[edge_nodes[edge, point], edge * 4 + point] = 1.0
    denom = 1.0 + spread.sum(axis=1)
    quarter = np.zeros((4, 16), np.float32)
    for row_a in range(4):
        for row_b in range(4):
            quarter[row_a // 2 * 2 + row_b // 2, row_a * 4 + row_b] = 0.25
    return (laplace, spread, denom, quarter)


def matched_points(links):
    other_edge = links // 2 % 4
    reversal = links % 2
    points = jnp.arange(4, dtype=jnp.int32)
    along = jnp.where(reversal[..., None] == 1, 3 - points, points)
    base = jnp.where(other_edge == 1, 3, jnp.where(other_edge == 2, 12, 0))
    stride = jnp.where((other_edge == 1) | (other_edge == 3), 4, 1)
    return base[..., None] + stride[..., None] * along


ZCHUNK = 4


def chunk_copies(src, dst, sems, count):
    def one(c):
        part = pl.ds(c * ZCHUNK, ZCHUNK)
        return pltpu.make_async_copy(src.at[:, part], dst.at[:, part], sems.at[c])

    return [one(c) for c in range(count)]


def neighbours(z, nlev):
    return jnp.minimum(z + 1, nlev - 1), jnp.maximum(z - 1, 0)


def crm_first_kernel(live_ref, state_hbm, part_hbm, mean_ref, held, wide, part, in_sem, out_sem):
    nfld, nlev, nx, _ = held.shape
    chunks = nlev // ZCHUNK
    loads = chunk_copies(state_hbm, held, in_sem, chunks)
    stores = chunk_copies(part, part_hbm, out_sem, chunks)
    for copy in loads:
        copy.start()
    live = live_ref[...] == 1

    def level(z, carry):
        upper_z, lower_z = neighbours(z, nlev)
        lead = ADVECT * wide[0, z]
        for f in range(nfld):
            state = wide[f, z]
            lower = wide[f, lower_z]
            upper = held[f, upper_z].astype(jnp.float32)
            wide[f, upper_z] = upper
            east = pltpu.roll(state, nx - 1, 0)
            west = pltpu.roll(state, 1, 0)
            mean_ref[f, pl.ds(z, 1)] = jnp.mean(state, axis=0, keepdims=True)
            fresh = KEEP * state + DIFF_X * (east + west) + DIFF_Z * (upper + lower) - lead * (east - west)
            part[f, z] = jnp.where(live, fresh, state)
        return carry

    for c in range(chunks):
        if c == 0:
            loads[0].wait()
            for f in range(nfld):
                wide[f, 0] = held[f, 0].astype(jnp.float32)
        if c + 1 < chunks:
            loads[c + 1].wait()
        lax.fori_loop(c * ZCHUNK, (c + 1) * ZCHUNK, level, 0)
        stores[c].start()
    for copy in stores:
        copy.wait()


def crm_second_kernel(force_ref, live_ref, mean_ref, part_hbm, new_hbm, tend_ref, mid, out, in_sem, out_sem):
    nfld, nlev, nx, _ = mid.shape
    chunks = nlev // ZCHUNK
    loads = chunk_copies(part_hbm, mid, in_sem, chunks)
    stores = chunk_copies(out, new_hbm, out_sem, chunks)
    for copy in loads:
        copy.start()
    live = live_ref[...] == 1

    def finish_first(z, carry):
        fresh = [
            mid[f, z]
            + jnp.where(live, RELAX * (force_ref[f, pl.ds(z, 1)] - mean_ref[f, pl.ds(z, 1)]), 0.0)
            for f in range(nfld)
        ]
        cond = CONVERT * jnp.maximum(fresh[3] - fresh[2], 0.0)
        fresh[3] = jnp.where(live, fresh[3] - cond, fresh[3])
        fresh[4] = jnp.where(live, fresh[4] + cond, fresh[4])
        for f in range(nfld):
            mid[f, z] = fresh[f]
        return carry

    def level(z, carry):
        upper_z, lower_z = neighbours(z, nlev)
        lead = ADVECT * mid[0, z]
        kept = {}

        def finish(f, fresh, state):
            new = jnp.where(live, fresh, state)
            out[f, z] = new.astype(out.dtype)
            tend_ref[f, pl.ds(z, 1)] = (jnp.mean(new, axis=0, keepdims=True) - mean_ref[f, pl.ds(z, 1)]) / CSTEPS

        for f in range(nfld):
            state = mid[f, z]
            upper = mid[f, upper_z]
            lower = mid[f, lower_z]
            east = pltpu.roll(state, nx - 1, 0)
            west = pltpu.roll(state, 1, 0)
            mean_x = jnp.mean(state, axis=0, keepdims=True)
            fresh = (
                KEEP * state
                + DIFF_X * (east + west)
                + DIFF_Z * (upper + lower)
                - lead * (east - west)
                + RELAX * (force_ref[f, pl.ds(z, 1)] - mean_x)
            )
            if f in (2, 3):
                kept[f] = (fresh, state)
                if f == 3:
                    cond = CONVERT * jnp.maximum(kept[3][0] - kept[2][0], 0.0)
                    finish(2, *kept[2])
                    finish(3, kept[3][0] - cond, kept[3][1])
                continue
            if f == 4:
                fresh = fresh + cond
            finish(f, fresh, state)
        return carry

    def ahead(z, carry):
        @pl.when(z + 1 < nlev)
        def _():
            finish_first(z + 1, 0)

        return level(z, carry)

    loads[0].wait()
    finish_first(0, 0)
    for c in range(chunks):
        if c + 1 < chunks:
            loads[c + 1].wait()
        lax.fori_loop(c * ZCHUNK, (c + 1) * ZCHUNK, ahead, 0, unroll=2)
        stores[c].start()
    for copy in stores:
        copy.wait()


def crm_first(state, active):
    nfld, nlev, nx, ncol = state.shape
    chunks = nlev // ZCHUNK
    return pl.pallas_call(
        crm_first_kernel,
        out_shape=(
            jax.ShapeDtypeStruct(state.shape, jnp.float32),
            jax.ShapeDtypeStruct((nfld, nlev, ncol), jnp.float32),
        ),
        in_specs=[pl.BlockSpec(memory_space=pltpu.VMEM), pl.BlockSpec(memory_space=pl.ANY)],
        out_specs=(pl.BlockSpec(memory_space=pl.ANY), pl.BlockSpec(memory_space=pltpu.VMEM)),
        scratch_shapes=[
            pltpu.VMEM(state.shape, jnp.bfloat16),
            pltpu.VMEM(state.shape, jnp.float32),
            pltpu.VMEM(state.shape, jnp.float32),
            pltpu.SemaphoreType.DMA((chunks,)),
            pltpu.SemaphoreType.DMA((chunks,)),
        ],
        compiler_params=pltpu.CompilerParams(vmem_limit_bytes=48 * 1024 * 1024),
    )(active.reshape(1, ncol), state)


def crm_second(part, start_mean, forcing, active):
    nfld, nlev, nx, ncol = part.shape
    chunks = nlev // ZCHUNK
    return pl.pallas_call(
        crm_second_kernel,
        out_shape=(
            jax.ShapeDtypeStruct(part.shape, jnp.bfloat16),
            jax.ShapeDtypeStruct((nfld, nlev, ncol), jnp.float32),
        ),
        in_specs=[
            pl.BlockSpec(memory_space=pltpu.VMEM),
            pl.BlockSpec(memory_space=pltpu.VMEM),
            pl.BlockSpec(memory_space=pltpu.VMEM),
            pl.BlockSpec(memory_space=pl.ANY),
        ],
        out_specs=(pl.BlockSpec(memory_space=pl.ANY), pl.BlockSpec(memory_space=pltpu.VMEM)),
        scratch_shapes=[
            pltpu.VMEM(part.shape, jnp.float32),
            pltpu.VMEM(part.shape, jnp.bfloat16),
            pltpu.SemaphoreType.DMA((chunks,)),
            pltpu.SemaphoreType.DMA((chunks,)),
        ],
        compiler_params=pltpu.CompilerParams(vmem_limit_bytes=48 * 1024 * 1024),
    )(forcing, active.reshape(1, ncol), start_mean, part)


def crm_run(state, forcing, active):
    part, start_mean = crm_first(state, active)
    return crm_second(part, start_mean, forcing, active)


TWO_STAGE = False


def exchange(chunks):
    if not TWO_STAGE:
        return lax.all_to_all(chunks, ("face", "col"), split_axis=0, concat_axis=0, tiled=True)
    nface = lax.axis_size("face")
    ncol = lax.axis_size("col")
    grid = chunks.reshape((nface, ncol) + chunks.shape[1:])
    grid = lax.all_to_all(grid, "col", split_axis=1, concat_axis=1, tiled=True)
    grid = lax.all_to_all(grid, "face", split_axis=0, concat_axis=0, tiled=True)
    return grid.reshape(chunks.shape)


def per_device(dyn_state, edge_links, phys_slot, crm_active, crm_state):
    laplace, spread, denom, quarter = [jnp.asarray(table) for table in node_tables()]
    rows_dev, cols_dev, nodes, width = dyn_state.shape
    nface = lax.axis_size("face")
    ncol = lax.axis_size("col")
    ndev = nface * ncol
    total_rows = rows_dev * nface
    total_cols = cols_dev * ncol
    neighbour = edge_links // 8
    pick = matched_points(edge_links)
    near_row = neighbour // total_cols
    near_col = neighbour % total_cols
    local_row = lax.broadcasted_iota(jnp.int32, (rows_dev, cols_dev, 4), 0)
    local_col = lax.broadcasted_iota(jnp.int32, (rows_dev, cols_dev, 4), 1)
    drow = (near_row - (lax.axis_index("face") * rows_dev + local_row) + 1) % total_rows - 1
    dcol = (near_col - (lax.axis_index("col") * cols_dev + local_col) + 1) % total_cols - 1
    place = (local_row + drow + 1) * (cols_dev + 2) + (local_col + dcol + 1)
    index_flat = place[..., None] * 16 + pick
    index_flat = index_flat.reshape(-1)
    part, start_mean = crm_first(crm_state, crm_active)
    state = dyn_state
    for step in range(DSTEPS):
        state = state + KAPPA * jnp.einsum(
            "nm,rcmw->rcnw", laplace, state, precision=lax.Precision.HIGHEST
        )
        if step == 0:
            faced = extended_2(state, (("face", 0),), 1)
            faced, part, start_mean = lax.optimization_barrier((faced, part, start_mean))
            extended = extended_2(faced, (("col", 1),), 1)
        else:
            extended = extended_2(state, (("face", 0), ("col", 1)), 1)
        matched = jnp.take(extended.reshape(-1, width), index_flat, axis=0).reshape(
            rows_dev, cols_dev, 16, width
        )
        summed = jnp.einsum("nm,rcmw->rcnw", spread, matched, precision=lax.Precision.HIGHEST)
        state = (state + summed) / denom[None, None, :, None]
    columns = jnp.einsum("qn,rcnw->rcqw", quarter, state, precision=lax.Precision.HIGHEST).reshape(
        -1, NFLD, LEV
    )[:, :, :CLEV].reshape(-1, NFLD * CLEV)
    per_dev = columns.shape[0]
    count = per_dev // ndev
    keys_local = phys_slot.reshape(-1)
    order = jnp.argsort(keys_local, stable=True)
    out_keys = keys_local[order]
    outgoing = jnp.concatenate(
        [columns[order], out_keys.astype(jnp.float32)[:, None]], axis=1
    )
    arrived = exchange(outgoing.reshape(ndev, count, NFLD * CLEV + 1)).reshape(per_dev, -1)
    slots = arrived[:, NFLD * CLEV].astype(jnp.int32) % per_dev
    physics = jnp.zeros((per_dev, NFLD * CLEV), jnp.float32).at[slots].set(arrived[:, : NFLD * CLEV])
    forcing = physics.reshape(per_dev, NFLD, CLEV).transpose(1, 2, 0)
    crm_new, tend = crm_second(part, start_mean, forcing, crm_active)
    tend_rows = tend.reshape(NFLD * CLEV, per_dev).T[slots]
    returned = exchange(tend_rows.reshape(ndev, count, NFLD * CLEV))
    placed = (
        jnp.zeros((per_dev, NFLD * CLEV), jnp.float32)
        .at[order]
        .set(returned.reshape(per_dev, NFLD * CLEV))
    )
    column_tend = placed.reshape(rows_dev, cols_dev, 4, NFLD * CLEV)
    return (state, column_tend, crm_new)


def solution(mesh):
    return jax.shard_map(
        per_device,
        mesh=mesh,
        in_specs=(
            P("face", "col", None, None),
            P("face", "col", None),
            P("face", "col", None),
            P(("face", "col")),
            P(None, None, None, ("face", "col")),
        ),
        out_specs=(
            P("face", "col", None, None),
            P("face", "col", None, None),
            P(None, None, None, ("face", "col")),
        ),
        check_vma=False,
    )
```

```python
import jax
import jax.numpy as jnp
import numpy as np
from jax import lax
from jax.experimental import pallas as pl
from jax.experimental.pallas import tpu as pltpu
from jax.sharding import PartitionSpec as P

NFLD = 10
LEV = 72
CLEV = 32
DSTEPS = 2
CSTEPS = 2


KAPPA = 0.1
ADVECT = 0.1
DIFF_X = 0.2
DIFF_Z = 0.1
RELAX = 0.2
CONVERT = 0.5
KEEP = 1.0 - 2.0 * DIFF_X - 2.0 * DIFF_Z


def extended_2(cells, sides, width):
    for axis, dim in sides:
        count = lax.axis_size(axis)
        head = lax.slice_in_dim(cells, 0, width, axis=dim)
        tail = lax.slice_in_dim(cells, cells.shape[dim] - width, cells.shape[dim], axis=dim)
        cells = jnp.concatenate(
            [
                lax.ppermute(tail, axis, [(i, (i + 1) % count) for i in range(count)]),
                cells,
                lax.ppermute(head, axis, [((i + 1) % count, i) for i in range(count)]),
            ],
            axis=dim,
        )
    return cells


def node_tables():
    laplace = np.zeros((16, 16), np.float32)
    for row_a in range(4):
        for row_b in range(4):
            here = row_a * 4 + row_b
            for step_a, step_b in ((1, 0), (-1, 0), (0, 1), (0, -1)):
                near_a, near_b = (row_a + step_a, row_b + step_b)
                if 0 <= near_a < 4 and 0 <= near_b < 4:
                    laplace[here, near_a * 4 + near_b] += 1.0
                    laplace[here, here] -= 1.0
    edge_nodes = np.array([[0, 1, 2, 3], [3, 7, 11, 15], [12, 13, 14, 15], [0, 4, 8, 12]])
    spread = np.zeros((16, 16), np.float32)
    for edge in range(4):
        for point in range(4):
            spread[edge_nodes[edge, point], edge * 4 + point] = 1.0
    denom = 1.0 + spread.sum(axis=1)
    quarter = np.zeros((4, 16), np.float32)
    for row_a in range(4):
        for row_b in range(4):
            quarter[row_a // 2 * 2 + row_b // 2, row_a * 4 + row_b] = 0.25
    return (laplace, spread, denom, quarter)


def matched_points(links):
    other_edge = links // 2 % 4
    reversal = links % 2
    points = jnp.arange(4, dtype=jnp.int32)
    along = jnp.where(reversal[..., None] == 1, 3 - points, points)
    base = jnp.where(other_edge == 1, 3, jnp.where(other_edge == 2, 12, 0))
    stride = jnp.where((other_edge == 1) | (other_edge == 3), 4, 1)
    return base[..., None] + stride[..., None] * along


ZCHUNK = 4


def chunk_copies(src, dst, sems, count):
    def one(c):
        part = pl.ds(c * ZCHUNK, ZCHUNK)
        return pltpu.make_async_copy(src.at[:, part], dst.at[:, part], sems.at[c])

    return [one(c) for c in range(count)]


def neighbours(z, nlev):
    return jnp.minimum(z + 1, nlev - 1), jnp.maximum(z - 1, 0)


def crm_first_kernel(live_ref, state_hbm, part_hbm, mean_ref, held, wide, part, in_sem, out_sem):
    nfld, nlev, nx, _ = held.shape
    chunks = nlev // ZCHUNK
    loads = chunk_copies(state_hbm, held, in_sem, chunks)
    stores = chunk_copies(part, part_hbm, out_sem, chunks)
    for copy in loads:
        copy.start()
    live = live_ref[...] == 1

    def level(z, carry):
        upper_z, lower_z = neighbours(z, nlev)
        lead = ADVECT * wide[0, z]
        for f in range(nfld):
            state = wide[f, z]
            lower = wide[f, lower_z]
            upper = held[f, upper_z].astype(jnp.float32)
            wide[f, upper_z] = upper
            east = pltpu.roll(state, nx - 1, 0)
            west = pltpu.roll(state, 1, 0)
            mean_ref[f, pl.ds(z, 1)] = jnp.mean(state, axis=0, keepdims=True)
            fresh = KEEP * state + DIFF_X * (east + west) + DIFF_Z * (upper + lower) - lead * (east - west)
            part[f, z] = jnp.where(live, fresh, state)
        return carry

    for c in range(chunks):
        if c == 0:
            loads[0].wait()
            for f in range(nfld):
                wide[f, 0] = held[f, 0].astype(jnp.float32)
        if c + 1 < chunks:
            loads[c + 1].wait()
        lax.fori_loop(c * ZCHUNK, (c + 1) * ZCHUNK, level, 0)
        stores[c].start()
    for copy in stores:
        copy.wait()


def crm_second_kernel(force_ref, live_ref, mean_ref, part_hbm, new_hbm, tend_ref, mid, out, in_sem, out_sem):
    nfld, nlev, nx, _ = mid.shape
    chunks = nlev // ZCHUNK
    loads = chunk_copies(part_hbm, mid, in_sem, chunks)
    stores = chunk_copies(out, new_hbm, out_sem, chunks)
    for copy in loads:
        copy.start()
    live = live_ref[...] == 1

    def finish_first(z, carry):
        fresh = [
            mid[f, z]
            + jnp.where(live, RELAX * (force_ref[f, pl.ds(z, 1)] - mean_ref[f, pl.ds(z, 1)]), 0.0)
            for f in range(nfld)
        ]
        cond = CONVERT * jnp.maximum(fresh[3] - fresh[2], 0.0)
        fresh[3] = jnp.where(live, fresh[3] - cond, fresh[3])
        fresh[4] = jnp.where(live, fresh[4] + cond, fresh[4])
        for f in range(nfld):
            mid[f, z] = fresh[f]
        return carry

    def level(z, carry):
        upper_z, lower_z = neighbours(z, nlev)
        lead = ADVECT * mid[0, z]
        kept = {}

        def finish(f, fresh, state):
            new = jnp.where(live, fresh, state)
            out[f, z] = new.astype(out.dtype)
            tend_ref[f, pl.ds(z, 1)] = (jnp.mean(new, axis=0, keepdims=True) - mean_ref[f, pl.ds(z, 1)]) / CSTEPS

        for f in range(nfld):
            state = mid[f, z]
            upper = mid[f, upper_z]
            lower = mid[f, lower_z]
            east = pltpu.roll(state, nx - 1, 0)
            west = pltpu.roll(state, 1, 0)
            mean_x = jnp.mean(state, axis=0, keepdims=True)
            fresh = (
                KEEP * state
                + DIFF_X * (east + west)
                + DIFF_Z * (upper + lower)
                - lead * (east - west)
                + RELAX * (force_ref[f, pl.ds(z, 1)] - mean_x)
            )
            if f in (2, 3):
                kept[f] = (fresh, state)
                if f == 3:
                    cond = CONVERT * jnp.maximum(kept[3][0] - kept[2][0], 0.0)
                    finish(2, *kept[2])
                    finish(3, kept[3][0] - cond, kept[3][1])
                continue
            if f == 4:
                fresh = fresh + cond
            finish(f, fresh, state)
        return carry

    def ahead(z, carry):
        @pl.when(z + 1 < nlev)
        def _():
            finish_first(z + 1, 0)

        return level(z, carry)

    loads[0].wait()
    finish_first(0, 0)
    for c in range(chunks):
        if c + 1 < chunks:
            loads[c + 1].wait()
        lax.fori_loop(c * ZCHUNK, (c + 1) * ZCHUNK, ahead, 0, unroll=2)
        stores[c].start()
    for copy in stores:
        copy.wait()


def crm_first(state, active):
    nfld, nlev, nx, ncol = state.shape
    chunks = nlev // ZCHUNK
    return pl.pallas_call(
        crm_first_kernel,
        out_shape=(
            jax.ShapeDtypeStruct(state.shape, jnp.float32),
            jax.ShapeDtypeStruct((nfld, nlev, ncol), jnp.float32),
        ),
        in_specs=[pl.BlockSpec(memory_space=pltpu.VMEM), pl.BlockSpec(memory_space=pl.ANY)],
        out_specs=(pl.BlockSpec(memory_space=pl.ANY), pl.BlockSpec(memory_space=pltpu.VMEM)),
        scratch_shapes=[
            pltpu.VMEM(state.shape, jnp.bfloat16),
            pltpu.VMEM(state.shape, jnp.float32),
            pltpu.VMEM(state.shape, jnp.float32),
            pltpu.SemaphoreType.DMA((chunks,)),
            pltpu.SemaphoreType.DMA((chunks,)),
        ],
        compiler_params=pltpu.CompilerParams(vmem_limit_bytes=48 * 1024 * 1024),
    )(active.reshape(1, ncol), state)


def crm_second(part, start_mean, forcing, active):
    nfld, nlev, nx, ncol = part.shape
    chunks = nlev // ZCHUNK
    return pl.pallas_call(
        crm_second_kernel,
        out_shape=(
            jax.ShapeDtypeStruct(part.shape, jnp.bfloat16),
            jax.ShapeDtypeStruct((nfld, nlev, ncol), jnp.float32),
        ),
        in_specs=[
            pl.BlockSpec(memory_space=pltpu.VMEM),
            pl.BlockSpec(memory_space=pltpu.VMEM),
            pl.BlockSpec(memory_space=pltpu.VMEM),
            pl.BlockSpec(memory_space=pl.ANY),
        ],
        out_specs=(pl.BlockSpec(memory_space=pl.ANY), pl.BlockSpec(memory_space=pltpu.VMEM)),
        scratch_shapes=[
            pltpu.VMEM(part.shape, jnp.float32),
            pltpu.VMEM(part.shape, jnp.bfloat16),
            pltpu.SemaphoreType.DMA((chunks,)),
            pltpu.SemaphoreType.DMA((chunks,)),
        ],
        compiler_params=pltpu.CompilerParams(vmem_limit_bytes=48 * 1024 * 1024),
    )(forcing, active.reshape(1, ncol), start_mean, part)


def crm_run(state, forcing, active):
    part, start_mean = crm_first(state, active)
    return crm_second(part, start_mean, forcing, active)


TWO_STAGE = False


def exchange(chunks):
    if not TWO_STAGE:
        return lax.all_to_all(chunks, ("face", "col"), split_axis=0, concat_axis=0, tiled=True)
    nface = lax.axis_size("face")
    ncol = lax.axis_size("col")
    grid = chunks.reshape((nface, ncol) + chunks.shape[1:])
    grid = lax.all_to_all(grid, "col", split_axis=1, concat_axis=1, tiled=True)
    grid = lax.all_to_all(grid, "face", split_axis=0, concat_axis=0, tiled=True)
    return grid.reshape(chunks.shape)


def per_device(dyn_state, edge_links, phys_slot, crm_active, crm_state):
    laplace, spread, denom, quarter = [jnp.asarray(table) for table in node_tables()]
    rows_dev, cols_dev, nodes, width = dyn_state.shape
    nface = lax.axis_size("face")
    ncol = lax.axis_size("col")
    ndev = nface * ncol
    total_rows = rows_dev * nface
    total_cols = cols_dev * ncol
    neighbour = edge_links // 8
    pick = matched_points(edge_links)
    near_row = neighbour // total_cols
    near_col = neighbour % total_cols
    local_row = lax.broadcasted_iota(jnp.int32, (rows_dev, cols_dev, 4), 0)
    local_col = lax.broadcasted_iota(jnp.int32, (rows_dev, cols_dev, 4), 1)
    drow = (near_row - (lax.axis_index("face") * rows_dev + local_row) + 1) % total_rows - 1
    dcol = (near_col - (lax.axis_index("col") * cols_dev + local_col) + 1) % total_cols - 1
    place = (local_row + drow + 1) * (cols_dev + 2) + (local_col + dcol + 1)
    index_flat = place[..., None] * 16 + pick
    index_flat = index_flat.reshape(-1)
    part, start_mean = crm_first(crm_state, crm_active)
    state = dyn_state
    for step in range(DSTEPS):
        state = state + KAPPA * jnp.einsum(
            "nm,rcmw->rcnw", laplace, state, precision=lax.Precision.HIGHEST
        )
        if step == 0:
            faced = extended_2(state, (("face", 0),), 1)
            faced, part, start_mean = lax.optimization_barrier((faced, part, start_mean))
            extended = extended_2(faced, (("col", 1),), 1)
        else:
            extended = extended_2(state, (("col", 1), ("face", 0)), 1)
        matched = jnp.take(extended.reshape(-1, width), index_flat, axis=0).reshape(
            rows_dev, cols_dev, 16, width
        )
        summed = jnp.einsum("nm,rcmw->rcnw", spread, matched, precision=lax.Precision.HIGHEST)
        state = (state + summed) / denom[None, None, :, None]
    columns = jnp.einsum("qn,rcnw->rcqw", quarter, state, precision=lax.Precision.HIGHEST).reshape(
        -1, NFLD, LEV
    )[:, :, :CLEV].reshape(-1, NFLD * CLEV)
    per_dev = columns.shape[0]
    count = per_dev // ndev
    keys_local = phys_slot.reshape(-1)
    order = jnp.argsort(keys_local, stable=True)
    out_keys = keys_local[order]
    outgoing = jnp.concatenate(
        [columns[order], out_keys.astype(jnp.float32)[:, None]], axis=1
    )
    arrived = exchange(outgoing.reshape(ndev, count, NFLD * CLEV + 1)).reshape(per_dev, -1)
    slots = arrived[:, NFLD * CLEV].astype(jnp.int32) % per_dev
    physics = jnp.zeros((per_dev, NFLD * CLEV), jnp.float32).at[slots].set(arrived[:, : NFLD * CLEV])
    forcing = physics.reshape(per_dev, NFLD, CLEV).transpose(1, 2, 0)
    crm_new, tend = crm_second(part, start_mean, forcing, crm_active)
    tend_rows = tend.reshape(NFLD * CLEV, per_dev).T[slots]
    returned = exchange(tend_rows.reshape(ndev, count, NFLD * CLEV))
    placed = (
        jnp.zeros((per_dev, NFLD * CLEV), jnp.float32)
        .at[order]
        .set(returned.reshape(per_dev, NFLD * CLEV))
    )
    column_tend = placed.reshape(rows_dev, cols_dev, 4, NFLD * CLEV)
    return (state, column_tend, crm_new)


def solution(mesh):
    return jax.shard_map(
        per_device,
        mesh=mesh,
        in_specs=(
            P("face", "col", None, None),
            P("face", "col", None),
            P("face", "col", None),
            P(("face", "col")),
            P(None, None, None, ("face", "col")),
        ),
        out_specs=(
            P("face", "col", None, None),
            P("face", "col", None, None),
            P(None, None, None, ("face", "col")),
        ),
        check_vma=False,
    )
```

```python
import jax
import jax.numpy as jnp
import numpy as np
from jax import lax
from jax.experimental import pallas as pl
from jax.experimental.pallas import tpu as pltpu
from jax.sharding import PartitionSpec as P

NFLD = 10
LEV = 72
CLEV = 32
DSTEPS = 2
CSTEPS = 2


KAPPA = 0.1
ADVECT = 0.1
DIFF_X = 0.2
DIFF_Z = 0.1
RELAX = 0.2
CONVERT = 0.5
KEEP = 1.0 - 2.0 * DIFF_X - 2.0 * DIFF_Z


def extended_2(cells, sides, width):
    for axis, dim in sides:
        count = lax.axis_size(axis)
        head = lax.slice_in_dim(cells, 0, width, axis=dim)
        tail = lax.slice_in_dim(cells, cells.shape[dim] - width, cells.shape[dim], axis=dim)
        cells = jnp.concatenate(
            [
                lax.ppermute(tail, axis, [(i, (i + 1) % count) for i in range(count)]),
                cells,
                lax.ppermute(head, axis, [((i + 1) % count, i) for i in range(count)]),
            ],
            axis=dim,
        )
    return cells


def node_tables():
    laplace = np.zeros((16, 16), np.float32)
    for row_a in range(4):
        for row_b in range(4):
            here = row_a * 4 + row_b
            for step_a, step_b in ((1, 0), (-1, 0), (0, 1), (0, -1)):
                near_a, near_b = (row_a + step_a, row_b + step_b)
                if 0 <= near_a < 4 and 0 <= near_b < 4:
                    laplace[here, near_a * 4 + near_b] += 1.0
                    laplace[here, here] -= 1.0
    edge_nodes = np.array([[0, 1, 2, 3], [3, 7, 11, 15], [12, 13, 14, 15], [0, 4, 8, 12]])
    spread = np.zeros((16, 16), np.float32)
    for edge in range(4):
        for point in range(4):
            spread[edge_nodes[edge, point], edge * 4 + point] = 1.0
    denom = 1.0 + spread.sum(axis=1)
    quarter = np.zeros((4, 16), np.float32)
    for row_a in range(4):
        for row_b in range(4):
            quarter[row_a // 2 * 2 + row_b // 2, row_a * 4 + row_b] = 0.25
    return (laplace, spread, denom, quarter)


def matched_points(links):
    other_edge = links // 2 % 4
    reversal = links % 2
    points = jnp.arange(4, dtype=jnp.int32)
    along = jnp.where(reversal[..., None] == 1, 3 - points, points)
    base = jnp.where(other_edge == 1, 3, jnp.where(other_edge == 2, 12, 0))
    stride = jnp.where((other_edge == 1) | (other_edge == 3), 4, 1)
    return base[..., None] + stride[..., None] * along


ZCHUNK = 4


def chunk_copies(src, dst, sems, count):
    def one(c):
        part = pl.ds(c * ZCHUNK, ZCHUNK)
        return pltpu.make_async_copy(src.at[:, part], dst.at[:, part], sems.at[c])

    return [one(c) for c in range(count)]


def neighbours(z, nlev):
    return jnp.minimum(z + 1, nlev - 1), jnp.maximum(z - 1, 0)


def crm_first_kernel(live_ref, state_hbm, part_hbm, mean_ref, held, wide, part, in_sem, out_sem):
    nfld, nlev, nx, _ = held.shape
    chunks = nlev // ZCHUNK
    loads = chunk_copies(state_hbm, held, in_sem, chunks)
    stores = chunk_copies(part, part_hbm, out_sem, chunks)
    for copy in loads:
        copy.start()
    live = live_ref[...] == 1

    def level(z, carry):
        upper_z, lower_z = neighbours(z, nlev)
        lead = ADVECT * wide[0, z]
        for f in range(nfld):
            state = wide[f, z]
            lower = wide[f, lower_z]
            upper = held[f, upper_z].astype(jnp.float32)
            wide[f, upper_z] = upper
            east = pltpu.roll(state, nx - 1, 0)
            west = pltpu.roll(state, 1, 0)
            mean_ref[f, pl.ds(z, 1)] = jnp.mean(state, axis=0, keepdims=True)
            fresh = KEEP * state + DIFF_X * (east + west) + DIFF_Z * (upper + lower) - lead * (east - west)
            part[f, z] = jnp.where(live, fresh, state)
        return carry

    for c in range(chunks):
        if c == 0:
            loads[0].wait()
            for f in range(nfld):
                wide[f, 0] = held[f, 0].astype(jnp.float32)
        if c + 1 < chunks:
            loads[c + 1].wait()
        lax.fori_loop(c * ZCHUNK, (c + 1) * ZCHUNK, level, 0)
        stores[c].start()
    for copy in stores:
        copy.wait()


def crm_second_kernel(force_ref, live_ref, mean_ref, part_hbm, new_hbm, tend_ref, mid, out, in_sem, out_sem):
    nfld, nlev, nx, _ = mid.shape
    chunks = nlev // ZCHUNK
    loads = chunk_copies(part_hbm, mid, in_sem, chunks)
    stores = chunk_copies(out, new_hbm, out_sem, chunks)
    for copy in loads:
        copy.start()
    live = live_ref[...] == 1

    def finish_first(z, carry):
        fresh = [
            mid[f, z]
            + jnp.where(live, RELAX * (force_ref[f, pl.ds(z, 1)] - mean_ref[f, pl.ds(z, 1)]), 0.0)
            for f in range(nfld)
        ]
        cond = CONVERT * jnp.maximum(fresh[3] - fresh[2], 0.0)
        fresh[3] = jnp.where(live, fresh[3] - cond, fresh[3])
        fresh[4] = jnp.where(live, fresh[4] + cond, fresh[4])
        for f in range(nfld):
            mid[f, z] = fresh[f]
        return carry

    def level(z, carry):
        upper_z, lower_z = neighbours(z, nlev)
        lead = ADVECT * mid[0, z]
        kept = {}

        def finish(f, fresh, state):
            new = jnp.where(live, fresh, state)
            out[f, z] = new.astype(out.dtype)
            tend_ref[f, pl.ds(z, 1)] = (jnp.mean(new, axis=0, keepdims=True) - mean_ref[f, pl.ds(z, 1)]) / CSTEPS

        for f in range(nfld):
            state = mid[f, z]
            upper = mid[f, upper_z]
            lower = mid[f, lower_z]
            east = pltpu.roll(state, nx - 1, 0)
            west = pltpu.roll(state, 1, 0)
            mean_x = jnp.mean(state, axis=0, keepdims=True)
            fresh = (
                KEEP * state
                + DIFF_X * (east + west)
                + DIFF_Z * (upper + lower)
                - lead * (east - west)
                + RELAX * (force_ref[f, pl.ds(z, 1)] - mean_x)
            )
            if f in (2, 3):
                kept[f] = (fresh, state)
                if f == 3:
                    cond = CONVERT * jnp.maximum(kept[3][0] - kept[2][0], 0.0)
                    finish(2, *kept[2])
                    finish(3, kept[3][0] - cond, kept[3][1])
                continue
            if f == 4:
                fresh = fresh + cond
            finish(f, fresh, state)
        return carry

    def ahead(z, carry):
        @pl.when(z + 1 < nlev)
        def _():
            finish_first(z + 1, 0)

        return level(z, carry)

    loads[0].wait()
    finish_first(0, 0)
    for c in range(chunks):
        if c + 1 < chunks:
            loads[c + 1].wait()
        lax.fori_loop(c * ZCHUNK, (c + 1) * ZCHUNK, ahead, 0, unroll=2)
        stores[c].start()
    for copy in stores:
        copy.wait()


def crm_first(state, active):
    nfld, nlev, nx, ncol = state.shape
    chunks = nlev // ZCHUNK
    return pl.pallas_call(
        crm_first_kernel,
        out_shape=(
            jax.ShapeDtypeStruct(state.shape, jnp.float32),
            jax.ShapeDtypeStruct((nfld, nlev, ncol), jnp.float32),
        ),
        in_specs=[pl.BlockSpec(memory_space=pltpu.VMEM), pl.BlockSpec(memory_space=pl.ANY)],
        out_specs=(pl.BlockSpec(memory_space=pl.ANY), pl.BlockSpec(memory_space=pltpu.VMEM)),
        scratch_shapes=[
            pltpu.VMEM(state.shape, jnp.bfloat16),
            pltpu.VMEM(state.shape, jnp.float32),
            pltpu.VMEM(state.shape, jnp.float32),
            pltpu.SemaphoreType.DMA((chunks,)),
            pltpu.SemaphoreType.DMA((chunks,)),
        ],
        compiler_params=pltpu.CompilerParams(vmem_limit_bytes=48 * 1024 * 1024),
    )(active.reshape(1, ncol), state)


def crm_second(part, start_mean, forcing, active):
    nfld, nlev, nx, ncol = part.shape
    chunks = nlev // ZCHUNK
    return pl.pallas_call(
        crm_second_kernel,
        out_shape=(
            jax.ShapeDtypeStruct(part.shape, jnp.bfloat16),
            jax.ShapeDtypeStruct((nfld, nlev, ncol), jnp.float32),
        ),
        in_specs=[
            pl.BlockSpec(memory_space=pltpu.VMEM),
            pl.BlockSpec(memory_space=pltpu.VMEM),
            pl.BlockSpec(memory_space=pltpu.VMEM),
            pl.BlockSpec(memory_space=pl.ANY),
        ],
        out_specs=(pl.BlockSpec(memory_space=pl.ANY), pl.BlockSpec(memory_space=pltpu.VMEM)),
        scratch_shapes=[
            pltpu.VMEM(part.shape, jnp.float32),
            pltpu.VMEM(part.shape, jnp.bfloat16),
            pltpu.SemaphoreType.DMA((chunks,)),
            pltpu.SemaphoreType.DMA((chunks,)),
        ],
        compiler_params=pltpu.CompilerParams(vmem_limit_bytes=48 * 1024 * 1024),
    )(forcing, active.reshape(1, ncol), start_mean, part)


def crm_run(state, forcing, active):
    part, start_mean = crm_first(state, active)
    return crm_second(part, start_mean, forcing, active)


TWO_STAGE = False


def exchange(chunks):
    if not TWO_STAGE:
        return lax.all_to_all(chunks, ("face", "col"), split_axis=0, concat_axis=0, tiled=True)
    nface = lax.axis_size("face")
    ncol = lax.axis_size("col")
    grid = chunks.reshape((nface, ncol) + chunks.shape[1:])
    grid = lax.all_to_all(grid, "col", split_axis=1, concat_axis=1, tiled=True)
    grid = lax.all_to_all(grid, "face", split_axis=0, concat_axis=0, tiled=True)
    return grid.reshape(chunks.shape)


def per_device(dyn_state, edge_links, phys_slot, crm_active, crm_state):
    laplace, spread, denom, quarter = [jnp.asarray(table) for table in node_tables()]
    rows_dev, cols_dev, nodes, width = dyn_state.shape
    nface = lax.axis_size("face")
    ncol = lax.axis_size("col")
    ndev = nface * ncol
    total_rows = rows_dev * nface
    total_cols = cols_dev * ncol
    neighbour = edge_links // 8
    pick = matched_points(edge_links)
    near_row = neighbour // total_cols
    near_col = neighbour % total_cols
    local_row = lax.broadcasted_iota(jnp.int32, (rows_dev, cols_dev, 4), 0)
    local_col = lax.broadcasted_iota(jnp.int32, (rows_dev, cols_dev, 4), 1)
    drow = (near_row - (lax.axis_index("face") * rows_dev + local_row) + 1) % total_rows - 1
    dcol = (near_col - (lax.axis_index("col") * cols_dev + local_col) + 1) % total_cols - 1
    place = (local_row + drow + 1) * (cols_dev + 2) + (local_col + dcol + 1)
    index_flat = place[..., None] * 16 + pick
    index_flat = index_flat.reshape(-1)
    part, start_mean = crm_first(crm_state, crm_active)
    state = dyn_state
    for step in range(DSTEPS):
        state = state + KAPPA * jnp.einsum(
            "nm,rcmw->rcnw", laplace, state, precision=lax.Precision.HIGHEST
        )
        if step == 0:
            sided = extended_2(state, (("col", 1),), 1)
            sided, part, start_mean = lax.optimization_barrier((sided, part, start_mean))
            extended = extended_2(sided, (("face", 0),), 1)
        else:
            extended = extended_2(state, (("col", 1), ("face", 0)), 1)
        matched = jnp.take(extended.reshape(-1, width), index_flat, axis=0).reshape(
            rows_dev, cols_dev, 16, width
        )
        summed = jnp.einsum("nm,rcmw->rcnw", spread, matched, precision=lax.Precision.HIGHEST)
        state = (state + summed) / denom[None, None, :, None]
    columns = jnp.einsum("qn,rcnw->rcqw", quarter, state, precision=lax.Precision.HIGHEST).reshape(
        -1, NFLD, LEV
    )[:, :, :CLEV].reshape(-1, NFLD * CLEV)
    per_dev = columns.shape[0]
    count = per_dev // ndev
    keys_local = phys_slot.reshape(-1)
    order = jnp.argsort(keys_local, stable=True)
    out_keys = keys_local[order]
    outgoing = jnp.concatenate(
        [columns[order], out_keys.astype(jnp.float32)[:, None]], axis=1
    )
    arrived = exchange(outgoing.reshape(ndev, count, NFLD * CLEV + 1)).reshape(per_dev, -1)
    slots = arrived[:, NFLD * CLEV].astype(jnp.int32) % per_dev
    physics = jnp.zeros((per_dev, NFLD * CLEV), jnp.float32).at[slots].set(arrived[:, : NFLD * CLEV])
    forcing = physics.reshape(per_dev, NFLD, CLEV).transpose(1, 2, 0)
    crm_new, tend = crm_second(part, start_mean, forcing, crm_active)
    tend_rows = tend.reshape(NFLD * CLEV, per_dev).T[slots]
    returned = exchange(tend_rows.reshape(ndev, count, NFLD * CLEV))
    placed = (
        jnp.zeros((per_dev, NFLD * CLEV), jnp.float32)
        .at[order]
        .set(returned.reshape(per_dev, NFLD * CLEV))
    )
    column_tend = placed.reshape(rows_dev, cols_dev, 4, NFLD * CLEV)
    return (state, column_tend, crm_new)


def solution(mesh):
    return jax.shard_map(
        per_device,
        mesh=mesh,
        in_specs=(
            P("face", "col", None, None),
            P("face", "col", None),
            P("face", "col", None),
            P(("face", "col")),
            P(None, None, None, ("face", "col")),
        ),
        out_specs=(
            P("face", "col", None, None),
            P("face", "col", None, None),
            P(None, None, None, ("face", "col")),
        ),
        check_vma=False,
    )
```

```python
import jax
import jax.numpy as jnp
import numpy as np
from jax import lax
from jax.experimental import pallas as pl
from jax.experimental.pallas import tpu as pltpu
from jax.sharding import PartitionSpec as P

NFLD = 10
LEV = 72
CLEV = 32
DSTEPS = 2
CSTEPS = 2


KAPPA = 0.1
ADVECT = 0.1
DIFF_X = 0.2
DIFF_Z = 0.1
RELAX = 0.2
CONVERT = 0.5
KEEP = 1.0 - 2.0 * DIFF_X - 2.0 * DIFF_Z


def extended_2(cells, sides, width):
    for axis, dim in sides:
        count = lax.axis_size(axis)
        head = lax.slice_in_dim(cells, 0, width, axis=dim)
        tail = lax.slice_in_dim(cells, cells.shape[dim] - width, cells.shape[dim], axis=dim)
        cells = jnp.concatenate(
            [
                lax.ppermute(tail, axis, [(i, (i + 1) % count) for i in range(count)]),
                cells,
                lax.ppermute(head, axis, [((i + 1) % count, i) for i in range(count)]),
            ],
            axis=dim,
        )
    return cells


def node_tables():
    laplace = np.zeros((16, 16), np.float32)
    for row_a in range(4):
        for row_b in range(4):
            here = row_a * 4 + row_b
            for step_a, step_b in ((1, 0), (-1, 0), (0, 1), (0, -1)):
                near_a, near_b = (row_a + step_a, row_b + step_b)
                if 0 <= near_a < 4 and 0 <= near_b < 4:
                    laplace[here, near_a * 4 + near_b] += 1.0
                    laplace[here, here] -= 1.0
    edge_nodes = np.array([[0, 1, 2, 3], [3, 7, 11, 15], [12, 13, 14, 15], [0, 4, 8, 12]])
    spread = np.zeros((16, 16), np.float32)
    for edge in range(4):
        for point in range(4):
            spread[edge_nodes[edge, point], edge * 4 + point] = 1.0
    denom = 1.0 + spread.sum(axis=1)
    quarter = np.zeros((4, 16), np.float32)
    for row_a in range(4):
        for row_b in range(4):
            quarter[row_a // 2 * 2 + row_b // 2, row_a * 4 + row_b] = 0.25
    return (laplace, spread, denom, quarter)


def matched_points(links):
    other_edge = links // 2 % 4
    reversal = links % 2
    points = jnp.arange(4, dtype=jnp.int32)
    along = jnp.where(reversal[..., None] == 1, 3 - points, points)
    base = jnp.where(other_edge == 1, 3, jnp.where(other_edge == 2, 12, 0))
    stride = jnp.where((other_edge == 1) | (other_edge == 3), 4, 1)
    return base[..., None] + stride[..., None] * along


ZCHUNK = 4
BCHUNK = 2


def chunk_copies(src, dst, sems, count, size=ZCHUNK):
    def one(c):
        part = pl.ds(c * size, size)
        return pltpu.make_async_copy(src.at[:, part], dst.at[:, part], sems.at[c])

    return [one(c) for c in range(count)]


def neighbours(z, nlev):
    return jnp.minimum(z + 1, nlev - 1), jnp.maximum(z - 1, 0)


def crm_first_kernel(live_ref, state_hbm, part_hbm, mean_ref, held, wide, part, in_sem, out_sem):
    nfld, nlev, nx, _ = held.shape
    chunks = nlev // ZCHUNK
    loads = chunk_copies(state_hbm, held, in_sem, chunks)
    stores = chunk_copies(part, part_hbm, out_sem, chunks)
    for copy in loads:
        copy.start()
    live = live_ref[...] == 1

    def level(z, carry):
        upper_z, lower_z = neighbours(z, nlev)
        lead = ADVECT * wide[0, z]
        for f in range(nfld):
            state = wide[f, z]
            lower = wide[f, lower_z]
            upper = held[f, upper_z].astype(jnp.float32)
            wide[f, upper_z] = upper
            east = pltpu.roll(state, nx - 1, 0)
            west = pltpu.roll(state, 1, 0)
            mean_ref[f, pl.ds(z, 1)] = jnp.mean(state, axis=0, keepdims=True)
            fresh = KEEP * state + DIFF_X * (east + west) + DIFF_Z * (upper + lower) - lead * (east - west)
            part[f, z] = jnp.where(live, fresh, state)
        return carry

    for c in range(chunks):
        if c == 0:
            loads[0].wait()
            for f in range(nfld):
                wide[f, 0] = held[f, 0].astype(jnp.float32)
        if c + 1 < chunks:
            loads[c + 1].wait()
        lax.fori_loop(c * ZCHUNK, (c + 1) * ZCHUNK, level, 0)
        stores[c].start()
    for copy in stores:
        copy.wait()


def crm_second_kernel(force_ref, live_ref, mean_ref, part_hbm, new_hbm, tend_ref, mid, out, in_sem, out_sem):
    nfld, nlev, nx, _ = mid.shape
    chunks = nlev // BCHUNK
    loads = chunk_copies(part_hbm, mid, in_sem, chunks, BCHUNK)
    stores = chunk_copies(out, new_hbm, out_sem, chunks, BCHUNK)
    for copy in loads:
        copy.start()
    live = live_ref[...] == 1

    def finish_first(z, carry):
        fresh = [
            mid[f, z]
            + jnp.where(live, RELAX * (force_ref[f, pl.ds(z, 1)] - mean_ref[f, pl.ds(z, 1)]), 0.0)
            for f in range(nfld)
        ]
        cond = CONVERT * jnp.maximum(fresh[3] - fresh[2], 0.0)
        fresh[3] = jnp.where(live, fresh[3] - cond, fresh[3])
        fresh[4] = jnp.where(live, fresh[4] + cond, fresh[4])
        for f in range(nfld):
            mid[f, z] = fresh[f]
        return carry

    def level(z, carry):
        upper_z, lower_z = neighbours(z, nlev)
        lead = ADVECT * mid[0, z]
        kept = {}

        def finish(f, fresh, state):
            new = jnp.where(live, fresh, state)
            out[f, z] = new.astype(out.dtype)
            tend_ref[f, pl.ds(z, 1)] = (jnp.mean(new, axis=0, keepdims=True) - mean_ref[f, pl.ds(z, 1)]) / CSTEPS

        for f in range(nfld):
            state = mid[f, z]
            upper = mid[f, upper_z]
            lower = mid[f, lower_z]
            east = pltpu.roll(state, nx - 1, 0)
            west = pltpu.roll(state, 1, 0)
            mean_x = jnp.mean(state, axis=0, keepdims=True)
            fresh = (
                KEEP * state
                + DIFF_X * (east + west)
                + DIFF_Z * (upper + lower)
                - lead * (east - west)
                + RELAX * (force_ref[f, pl.ds(z, 1)] - mean_x)
            )
            if f in (2, 3):
                kept[f] = (fresh, state)
                if f == 3:
                    cond = CONVERT * jnp.maximum(kept[3][0] - kept[2][0], 0.0)
                    finish(2, *kept[2])
                    finish(3, kept[3][0] - cond, kept[3][1])
                continue
            if f == 4:
                fresh = fresh + cond
            finish(f, fresh, state)
        return carry

    def ahead(z, carry):
        @pl.when(z + 1 < nlev)
        def _():
            finish_first(z + 1, 0)

        return level(z, carry)

    loads[0].wait()
    finish_first(0, 0)
    for c in range(chunks):
        if c + 1 < chunks:
            loads[c + 1].wait()
        lax.fori_loop(c * BCHUNK, (c + 1) * BCHUNK, ahead, 0, unroll=2)
        stores[c].start()
    for copy in stores:
        copy.wait()


def crm_first(state, active):
    nfld, nlev, nx, ncol = state.shape
    chunks = nlev // ZCHUNK
    return pl.pallas_call(
        crm_first_kernel,
        out_shape=(
            jax.ShapeDtypeStruct(state.shape, jnp.float32),
            jax.ShapeDtypeStruct((nfld, nlev, ncol), jnp.float32),
        ),
        in_specs=[pl.BlockSpec(memory_space=pltpu.VMEM), pl.BlockSpec(memory_space=pl.ANY)],
        out_specs=(pl.BlockSpec(memory_space=pl.ANY), pl.BlockSpec(memory_space=pltpu.VMEM)),
        scratch_shapes=[
            pltpu.VMEM(state.shape, jnp.bfloat16),
            pltpu.VMEM(state.shape, jnp.float32),
            pltpu.VMEM(state.shape, jnp.float32),
            pltpu.SemaphoreType.DMA((chunks,)),
            pltpu.SemaphoreType.DMA((chunks,)),
        ],
        compiler_params=pltpu.CompilerParams(vmem_limit_bytes=48 * 1024 * 1024),
    )(active.reshape(1, ncol), state)


def crm_second(part, start_mean, forcing, active):
    nfld, nlev, nx, ncol = part.shape
    chunks = nlev // BCHUNK
    return pl.pallas_call(
        crm_second_kernel,
        out_shape=(
            jax.ShapeDtypeStruct(part.shape, jnp.bfloat16),
            jax.ShapeDtypeStruct((nfld, nlev, ncol), jnp.float32),
        ),
        in_specs=[
            pl.BlockSpec(memory_space=pltpu.VMEM),
            pl.BlockSpec(memory_space=pltpu.VMEM),
            pl.BlockSpec(memory_space=pltpu.VMEM),
            pl.BlockSpec(memory_space=pl.ANY),
        ],
        out_specs=(pl.BlockSpec(memory_space=pl.ANY), pl.BlockSpec(memory_space=pltpu.VMEM)),
        scratch_shapes=[
            pltpu.VMEM(part.shape, jnp.float32),
            pltpu.VMEM(part.shape, jnp.bfloat16),
            pltpu.SemaphoreType.DMA((chunks,)),
            pltpu.SemaphoreType.DMA((chunks,)),
        ],
        compiler_params=pltpu.CompilerParams(vmem_limit_bytes=48 * 1024 * 1024),
    )(forcing, active.reshape(1, ncol), start_mean, part)


def crm_run(state, forcing, active):
    part, start_mean = crm_first(state, active)
    return crm_second(part, start_mean, forcing, active)


TWO_STAGE = False


def exchange(chunks):
    if not TWO_STAGE:
        return lax.all_to_all(chunks, ("face", "col"), split_axis=0, concat_axis=0, tiled=True)
    nface = lax.axis_size("face")
    ncol = lax.axis_size("col")
    grid = chunks.reshape((nface, ncol) + chunks.shape[1:])
    grid = lax.all_to_all(grid, "col", split_axis=1, concat_axis=1, tiled=True)
    grid = lax.all_to_all(grid, "face", split_axis=0, concat_axis=0, tiled=True)
    return grid.reshape(chunks.shape)


def per_device(dyn_state, edge_links, phys_slot, crm_active, crm_state):
    laplace, spread, denom, quarter = [jnp.asarray(table) for table in node_tables()]
    rows_dev, cols_dev, nodes, width = dyn_state.shape
    nface = lax.axis_size("face")
    ncol = lax.axis_size("col")
    ndev = nface * ncol
    total_rows = rows_dev * nface
    total_cols = cols_dev * ncol
    neighbour = edge_links // 8
    pick = matched_points(edge_links)
    near_row = neighbour // total_cols
    near_col = neighbour % total_cols
    local_row = lax.broadcasted_iota(jnp.int32, (rows_dev, cols_dev, 4), 0)
    local_col = lax.broadcasted_iota(jnp.int32, (rows_dev, cols_dev, 4), 1)
    drow = (near_row - (lax.axis_index("face") * rows_dev + local_row) + 1) % total_rows - 1
    dcol = (near_col - (lax.axis_index("col") * cols_dev + local_col) + 1) % total_cols - 1
    place = (local_row + drow + 1) * (cols_dev + 2) + (local_col + dcol + 1)
    index_flat = place[..., None] * 16 + pick
    index_flat = index_flat.reshape(-1)
    part, start_mean = crm_first(crm_state, crm_active)
    state = dyn_state
    for step in range(DSTEPS):
        state = state + KAPPA * jnp.einsum(
            "nm,rcmw->rcnw", laplace, state, precision=lax.Precision.HIGHEST
        )
        if step == 0:
            faced = extended_2(state, (("face", 0),), 1)
            faced, part, start_mean = lax.optimization_barrier((faced, part, start_mean))
            extended = extended_2(faced, (("col", 1),), 1)
        else:
            extended = extended_2(state, (("col", 1), ("face", 0)), 1)
        matched = jnp.take(extended.reshape(-1, width), index_flat, axis=0).reshape(
            rows_dev, cols_dev, 16, width
        )
        summed = jnp.einsum("nm,rcmw->rcnw", spread, matched, precision=lax.Precision.HIGHEST)
        state = (state + summed) / denom[None, None, :, None]
    columns = jnp.einsum("qn,rcnw->rcqw", quarter, state, precision=lax.Precision.HIGHEST).reshape(
        -1, NFLD, LEV
    )[:, :, :CLEV].reshape(-1, NFLD * CLEV)
    per_dev = columns.shape[0]
    count = per_dev // ndev
    keys_local = phys_slot.reshape(-1)
    order = jnp.argsort(keys_local, stable=True)
    out_keys = keys_local[order]
    outgoing = jnp.concatenate(
        [columns[order], out_keys.astype(jnp.float32)[:, None]], axis=1
    )
    arrived = exchange(outgoing.reshape(ndev, count, NFLD * CLEV + 1)).reshape(per_dev, -1)
    slots = arrived[:, NFLD * CLEV].astype(jnp.int32) % per_dev
    physics = jnp.zeros((per_dev, NFLD * CLEV), jnp.float32).at[slots].set(arrived[:, : NFLD * CLEV])
    forcing = physics.reshape(per_dev, NFLD, CLEV).transpose(1, 2, 0)
    crm_new, tend = crm_second(part, start_mean, forcing, crm_active)
    tend_rows = tend.reshape(NFLD * CLEV, per_dev).T[slots]
    returned = exchange(tend_rows.reshape(ndev, count, NFLD * CLEV))
    placed = (
        jnp.zeros((per_dev, NFLD * CLEV), jnp.float32)
        .at[order]
        .set(returned.reshape(per_dev, NFLD * CLEV))
    )
    column_tend = placed.reshape(rows_dev, cols_dev, 4, NFLD * CLEV)
    return (state, column_tend, crm_new)


def solution(mesh):
    return jax.shard_map(
        per_device,
        mesh=mesh,
        in_specs=(
            P("face", "col", None, None),
            P("face", "col", None),
            P("face", "col", None),
            P(("face", "col")),
            P(None, None, None, ("face", "col")),
        ),
        out_specs=(
            P("face", "col", None, None),
            P("face", "col", None, None),
            P(None, None, None, ("face", "col")),
        ),
        check_vma=False,
    )
```

```python
import jax
import jax.numpy as jnp
import numpy as np
from jax import lax
from jax.experimental import pallas as pl
from jax.experimental.pallas import tpu as pltpu
from jax.sharding import PartitionSpec as P

NFLD = 10
LEV = 72
CLEV = 32
DSTEPS = 2
CSTEPS = 2


KAPPA = 0.1
ADVECT = 0.1
DIFF_X = 0.2
DIFF_Z = 0.1
RELAX = 0.2
CONVERT = 0.5
KEEP = 1.0 - 2.0 * DIFF_X - 2.0 * DIFF_Z


def extended_2(cells, sides, width):
    for axis, dim in sides:
        count = lax.axis_size(axis)
        head = lax.slice_in_dim(cells, 0, width, axis=dim)
        tail = lax.slice_in_dim(cells, cells.shape[dim] - width, cells.shape[dim], axis=dim)
        cells = jnp.concatenate(
            [
                lax.ppermute(tail, axis, [(i, (i + 1) % count) for i in range(count)]),
                cells,
                lax.ppermute(head, axis, [((i + 1) % count, i) for i in range(count)]),
            ],
            axis=dim,
        )
    return cells


def node_tables():
    laplace = np.zeros((16, 16), np.float32)
    for row_a in range(4):
        for row_b in range(4):
            here = row_a * 4 + row_b
            for step_a, step_b in ((1, 0), (-1, 0), (0, 1), (0, -1)):
                near_a, near_b = (row_a + step_a, row_b + step_b)
                if 0 <= near_a < 4 and 0 <= near_b < 4:
                    laplace[here, near_a * 4 + near_b] += 1.0
                    laplace[here, here] -= 1.0
    edge_nodes = np.array([[0, 1, 2, 3], [3, 7, 11, 15], [12, 13, 14, 15], [0, 4, 8, 12]])
    spread = np.zeros((16, 16), np.float32)
    for edge in range(4):
        for point in range(4):
            spread[edge_nodes[edge, point], edge * 4 + point] = 1.0
    denom = 1.0 + spread.sum(axis=1)
    quarter = np.zeros((4, 16), np.float32)
    for row_a in range(4):
        for row_b in range(4):
            quarter[row_a // 2 * 2 + row_b // 2, row_a * 4 + row_b] = 0.25
    return (laplace, spread, denom, quarter)


def matched_points(links):
    other_edge = links // 2 % 4
    reversal = links % 2
    points = jnp.arange(4, dtype=jnp.int32)
    along = jnp.where(reversal[..., None] == 1, 3 - points, points)
    base = jnp.where(other_edge == 1, 3, jnp.where(other_edge == 2, 12, 0))
    stride = jnp.where((other_edge == 1) | (other_edge == 3), 4, 1)
    return base[..., None] + stride[..., None] * along


ZCHUNK = 2
BCHUNK = 2


def chunk_copies(src, dst, sems, count, size=ZCHUNK):
    def one(c):
        part = pl.ds(c * size, size)
        return pltpu.make_async_copy(src.at[:, part], dst.at[:, part], sems.at[c])

    return [one(c) for c in range(count)]


def neighbours(z, nlev):
    return jnp.minimum(z + 1, nlev - 1), jnp.maximum(z - 1, 0)


def crm_first_kernel(live_ref, state_hbm, part_hbm, mean_ref, held, wide, part, in_sem, out_sem):
    nfld, nlev, nx, _ = held.shape
    chunks = nlev // ZCHUNK
    loads = chunk_copies(state_hbm, held, in_sem, chunks)
    stores = chunk_copies(part, part_hbm, out_sem, chunks)
    for copy in loads:
        copy.start()
    live = live_ref[...] == 1

    def level(z, carry):
        upper_z, lower_z = neighbours(z, nlev)
        lead = ADVECT * wide[0, z]
        for f in range(nfld):
            state = wide[f, z]
            lower = wide[f, lower_z]
            upper = held[f, upper_z].astype(jnp.float32)
            wide[f, upper_z] = upper
            east = pltpu.roll(state, nx - 1, 0)
            west = pltpu.roll(state, 1, 0)
            mean_ref[f, pl.ds(z, 1)] = jnp.mean(state, axis=0, keepdims=True)
            fresh = KEEP * state + DIFF_X * (east + west) + DIFF_Z * (upper + lower) - lead * (east - west)
            part[f, z] = jnp.where(live, fresh, state)
        return carry

    for c in range(chunks):
        if c == 0:
            loads[0].wait()
            for f in range(nfld):
                wide[f, 0] = held[f, 0].astype(jnp.float32)
        if c + 1 < chunks:
            loads[c + 1].wait()
        lax.fori_loop(c * ZCHUNK, (c + 1) * ZCHUNK, level, 0)
        stores[c].start()
    for copy in stores:
        copy.wait()


def crm_second_kernel(force_ref, live_ref, mean_ref, part_hbm, new_hbm, tend_ref, mid, out, in_sem, out_sem):
    nfld, nlev, nx, _ = mid.shape
    chunks = nlev // BCHUNK
    loads = chunk_copies(part_hbm, mid, in_sem, chunks, BCHUNK)
    stores = chunk_copies(out, new_hbm, out_sem, chunks, BCHUNK)
    for copy in loads:
        copy.start()
    live = live_ref[...] == 1

    def finish_first(z, carry):
        fresh = [
            mid[f, z]
            + jnp.where(live, RELAX * (force_ref[f, pl.ds(z, 1)] - mean_ref[f, pl.ds(z, 1)]), 0.0)
            for f in range(nfld)
        ]
        cond = CONVERT * jnp.maximum(fresh[3] - fresh[2], 0.0)
        fresh[3] = jnp.where(live, fresh[3] - cond, fresh[3])
        fresh[4] = jnp.where(live, fresh[4] + cond, fresh[4])
        for f in range(nfld):
            mid[f, z] = fresh[f]
        return carry

    def level(z, carry):
        upper_z, lower_z = neighbours(z, nlev)
        lead = ADVECT * mid[0, z]
        kept = {}

        def finish(f, fresh, state):
            new = jnp.where(live, fresh, state)
            out[f, z] = new.astype(out.dtype)
            tend_ref[f, pl.ds(z, 1)] = (jnp.mean(new, axis=0, keepdims=True) - mean_ref[f, pl.ds(z, 1)]) / CSTEPS

        for f in range(nfld):
            state = mid[f, z]
            upper = mid[f, upper_z]
            lower = mid[f, lower_z]
            east = pltpu.roll(state, nx - 1, 0)
            west = pltpu.roll(state, 1, 0)
            mean_x = jnp.mean(state, axis=0, keepdims=True)
            fresh = (
                KEEP * state
                + DIFF_X * (east + west)
                + DIFF_Z * (upper + lower)
                - lead * (east - west)
                + RELAX * (force_ref[f, pl.ds(z, 1)] - mean_x)
            )
            if f in (2, 3):
                kept[f] = (fresh, state)
                if f == 3:
                    cond = CONVERT * jnp.maximum(kept[3][0] - kept[2][0], 0.0)
                    finish(2, *kept[2])
                    finish(3, kept[3][0] - cond, kept[3][1])
                continue
            if f == 4:
                fresh = fresh + cond
            finish(f, fresh, state)
        return carry

    def ahead(z, carry):
        @pl.when(z + 1 < nlev)
        def _():
            finish_first(z + 1, 0)

        return level(z, carry)

    loads[0].wait()
    finish_first(0, 0)
    for c in range(chunks):
        if c + 1 < chunks:
            loads[c + 1].wait()
        lax.fori_loop(c * BCHUNK, (c + 1) * BCHUNK, ahead, 0, unroll=2)
        stores[c].start()
    for copy in stores:
        copy.wait()


def crm_first(state, active):
    nfld, nlev, nx, ncol = state.shape
    chunks = nlev // ZCHUNK
    return pl.pallas_call(
        crm_first_kernel,
        out_shape=(
            jax.ShapeDtypeStruct(state.shape, jnp.float32),
            jax.ShapeDtypeStruct((nfld, nlev, ncol), jnp.float32),
        ),
        in_specs=[pl.BlockSpec(memory_space=pltpu.VMEM), pl.BlockSpec(memory_space=pl.ANY)],
        out_specs=(pl.BlockSpec(memory_space=pl.ANY), pl.BlockSpec(memory_space=pltpu.VMEM)),
        scratch_shapes=[
            pltpu.VMEM(state.shape, jnp.bfloat16),
            pltpu.VMEM(state.shape, jnp.float32),
            pltpu.VMEM(state.shape, jnp.float32),
            pltpu.SemaphoreType.DMA((chunks,)),
            pltpu.SemaphoreType.DMA((chunks,)),
        ],
        compiler_params=pltpu.CompilerParams(vmem_limit_bytes=48 * 1024 * 1024),
    )(active.reshape(1, ncol), state)


def crm_second(part, start_mean, forcing, active):
    nfld, nlev, nx, ncol = part.shape
    chunks = nlev // BCHUNK
    return pl.pallas_call(
        crm_second_kernel,
        out_shape=(
            jax.ShapeDtypeStruct(part.shape, jnp.bfloat16),
            jax.ShapeDtypeStruct((nfld, nlev, ncol), jnp.float32),
        ),
        in_specs=[
            pl.BlockSpec(memory_space=pltpu.VMEM),
            pl.BlockSpec(memory_space=pltpu.VMEM),
            pl.BlockSpec(memory_space=pltpu.VMEM),
            pl.BlockSpec(memory_space=pl.ANY),
        ],
        out_specs=(pl.BlockSpec(memory_space=pl.ANY), pl.BlockSpec(memory_space=pltpu.VMEM)),
        scratch_shapes=[
            pltpu.VMEM(part.shape, jnp.float32),
            pltpu.VMEM(part.shape, jnp.bfloat16),
            pltpu.SemaphoreType.DMA((chunks,)),
            pltpu.SemaphoreType.DMA((chunks,)),
        ],
        compiler_params=pltpu.CompilerParams(vmem_limit_bytes=48 * 1024 * 1024),
    )(forcing, active.reshape(1, ncol), start_mean, part)


def crm_run(state, forcing, active):
    part, start_mean = crm_first(state, active)
    return crm_second(part, start_mean, forcing, active)


TWO_STAGE = False


def exchange(chunks):
    if not TWO_STAGE:
        return lax.all_to_all(chunks, ("face", "col"), split_axis=0, concat_axis=0, tiled=True)
    nface = lax.axis_size("face")
    ncol = lax.axis_size("col")
    grid = chunks.reshape((nface, ncol) + chunks.shape[1:])
    grid = lax.all_to_all(grid, "col", split_axis=1, concat_axis=1, tiled=True)
    grid = lax.all_to_all(grid, "face", split_axis=0, concat_axis=0, tiled=True)
    return grid.reshape(chunks.shape)


def per_device(dyn_state, edge_links, phys_slot, crm_active, crm_state):
    laplace, spread, denom, quarter = [jnp.asarray(table) for table in node_tables()]
    rows_dev, cols_dev, nodes, width = dyn_state.shape
    nface = lax.axis_size("face")
    ncol = lax.axis_size("col")
    ndev = nface * ncol
    total_rows = rows_dev * nface
    total_cols = cols_dev * ncol
    neighbour = edge_links // 8
    pick = matched_points(edge_links)
    near_row = neighbour // total_cols
    near_col = neighbour % total_cols
    local_row = lax.broadcasted_iota(jnp.int32, (rows_dev, cols_dev, 4), 0)
    local_col = lax.broadcasted_iota(jnp.int32, (rows_dev, cols_dev, 4), 1)
    drow = (near_row - (lax.axis_index("face") * rows_dev + local_row) + 1) % total_rows - 1
    dcol = (near_col - (lax.axis_index("col") * cols_dev + local_col) + 1) % total_cols - 1
    place = (local_row + drow + 1) * (cols_dev + 2) + (local_col + dcol + 1)
    index_flat = place[..., None] * 16 + pick
    index_flat = index_flat.reshape(-1)
    part, start_mean = crm_first(crm_state, crm_active)
    state = dyn_state
    for step in range(DSTEPS):
        state = state + KAPPA * jnp.einsum(
            "nm,rcmw->rcnw", laplace, state, precision=lax.Precision.HIGHEST
        )
        if step == 0:
            faced = extended_2(state, (("face", 0),), 1)
            faced, part, start_mean = lax.optimization_barrier((faced, part, start_mean))
            extended = extended_2(faced, (("col", 1),), 1)
        else:
            extended = extended_2(state, (("col", 1), ("face", 0)), 1)
        matched = jnp.take(extended.reshape(-1, width), index_flat, axis=0).reshape(
            rows_dev, cols_dev, 16, width
        )
        summed = jnp.einsum("nm,rcmw->rcnw", spread, matched, precision=lax.Precision.HIGHEST)
        state = (state + summed) / denom[None, None, :, None]
    columns = jnp.einsum("qn,rcnw->rcqw", quarter, state, precision=lax.Precision.HIGHEST).reshape(
        -1, NFLD, LEV
    )[:, :, :CLEV].reshape(-1, NFLD * CLEV)
    per_dev = columns.shape[0]
    count = per_dev // ndev
    keys_local = phys_slot.reshape(-1)
    order = jnp.argsort(keys_local, stable=True)
    out_keys = keys_local[order]
    outgoing = jnp.concatenate(
        [columns[order], out_keys.astype(jnp.float32)[:, None]], axis=1
    )
    arrived = exchange(outgoing.reshape(ndev, count, NFLD * CLEV + 1)).reshape(per_dev, -1)
    slots = arrived[:, NFLD * CLEV].astype(jnp.int32) % per_dev
    physics = jnp.zeros((per_dev, NFLD * CLEV), jnp.float32).at[slots].set(arrived[:, : NFLD * CLEV])
    forcing = physics.reshape(per_dev, NFLD, CLEV).transpose(1, 2, 0)
    crm_new, tend = crm_second(part, start_mean, forcing, crm_active)
    tend_rows = tend.reshape(NFLD * CLEV, per_dev).T[slots]
    returned = exchange(tend_rows.reshape(ndev, count, NFLD * CLEV))
    placed = (
        jnp.zeros((per_dev, NFLD * CLEV), jnp.float32)
        .at[order]
        .set(returned.reshape(per_dev, NFLD * CLEV))
    )
    column_tend = placed.reshape(rows_dev, cols_dev, 4, NFLD * CLEV)
    return (state, column_tend, crm_new)


def solution(mesh):
    return jax.shard_map(
        per_device,
        mesh=mesh,
        in_specs=(
            P("face", "col", None, None),
            P("face", "col", None),
            P("face", "col", None),
            P(("face", "col")),
            P(None, None, None, ("face", "col")),
        ),
        out_specs=(
            P("face", "col", None, None),
            P("face", "col", None, None),
            P(None, None, None, ("face", "col")),
        ),
        check_vma=False,
    )
```
